32 devices in a mesh: groups: 2 (over x), ctx: 16 (over z, y, core).
Axes of the slice: x: 2, y: 2, z: 4, core: 2. Of those that a mesh axis runs over, the one named last changes fastest.
Arguments:
- queries: bfloat16 [4096, 2048], P(('groups', 'ctx')), parts along dimension 0, may hold values from -60 to 60, as said below
- key_vectors: bfloat16 [4096, 2048], P(('groups', 'ctx')), parts along dimension 0, may hold values from -60 to 60, as said below
- values: bfloat16 [4096, 2048], P(('groups', 'ctx')), parts along dimension 0, may hold values from -6 to 6
- grad_out: bfloat16 [4096, 2048], P(('groups', 'ctx')), parts along dimension 0, may hold values from -6 to 6
- file_lengths: int32 [128], P('groups'), parts along dimension 0, may hold values from 1 to 512, 2048 in all
- reach_table: int32 [32], P(('groups', 'ctx')), parts along dimension 0, may hold values from 1 to 11
Outputs:
- attended: bfloat16 [4096, 2048], P(('groups', 'ctx')), parts along dimension 0
- grad_queries: bfloat16 [4096, 2048], P(('groups', 'ctx')), parts along dimension 0
- grad_keys: bfloat16 [4096, 2048], P(('groups', 'ctx')), parts along dimension 0
- grad_values: bfloat16 [4096, 2048], P(('groups', 'ctx')), parts along dimension 0
The draws below stay inside these ranges and needn't reach their ends.
There are 2 independent parts, one for each index of `groups`. The reference program is written for one: setup_inputs(seed, part) draws one part's arguments, and reference() takes and returns one part's arrays. A program takes and returns all parts, laid end to end along the dimension named above; each array names one. Nothing has to cross between parts.
Inputs may be any that keep to these rules, and one draw needn't show every extreme that they name: `queries`: entries are finite. `key_vectors`: entries are finite.
All inputs are finite; a program needn't handle non-finite values.
Results may differ from the reference program's by a relative error of at most 0.0045.
The reference program's roundings to bfloat16 on the way count: a program that leaves them out, or rounds other values in their place, can miss the bound.
Values may be sent and summed in bfloat16 or wider, within the bound.
No kernel may reach another device: no remote copies, remote signals or barrier semaphores. Data moves between devices by JAX's collectives and lax.ppermute only.
A program may use at most 128 MiB of HBM per device.

```python
import math
import jax
import jax.numpy as jnp
import numpy as np
from jax import lax

HEADS = 16
HEAD_DIM = 128
BLOCK = 128
TOK_DEV = 128
FILES = 64
REACH = 11
TOKENS = 2048
BLOCKS = 16
N_CTX = 16


def scaled_noise(key):
    shape_two = (TOKENS, HEADS * HEAD_DIM)
    noise = jax.random.truncated_normal(jax.random.fold_in(key, 3), -6.0, 6.0, shape_two, jnp.float32)
    spread = jnp.exp(jax.random.uniform(jax.random.fold_in(key, 4), (TOKENS, 1), jnp.float32, math.log(0.3), math.log(3.0)))
    return noise * spread


def draw_queries(key, part):
    drawn = scaled_noise(jax.random.fold_in(key, 11))
    return drawn.astype(jnp.bfloat16)


def draw_key_vectors(key, part):
    drawn = scaled_noise(jax.random.fold_in(key, 13))
    return drawn.astype(jnp.bfloat16)


def set_ends(values, key, low, top_value):
    shape = values.shape
    spot = [jax.random.randint(jax.random.fold_in(key, axis), (), 0, shape[axis]) for axis in range(len(shape))]
    values = values.at[tuple(spot)].set(low)
    longest = shape.index(max(shape))
    spot[longest] = (spot[longest] + 1) % shape[longest]
    return values.at[tuple(spot)].set(top_value)


def block_levels(key, shape, pieces, low, largest):
    factor_of, own = 1.0, jax.random.fold_in(key, 6)
    for dim, blocks in pieces:
        steps = jnp.exp(jax.random.uniform(jax.random.fold_in(own, dim), (blocks,), jnp.float32, low / len(pieces), largest / len(pieces)))
        factor_of = factor_of * jnp.repeat(steps, shape[dim] // blocks).reshape([-1 if axis == dim else 1 for axis in range(len(shape))])
    return factor_of


def split_up(count, total, limit, skew):
    loads = [(1 << 20) // math.isqrt(rank ** skew) + 1 for rank in range(2, count + 1)]
    spare, given = total - limit - (count - 1), [1] * (count - 1)
    while spare > 0:
        candidates = [i for i in range(count - 1) if given[i] < limit]
        whole, remaining = sum([loads[i] for i in candidates]), spare
        for i in candidates:
            extra = min(limit - given[i], max(1, remaining * loads[i] // whole), spare)
            given[i] = given[i] + extra
            spare = spare - extra
    return np.array([limit] + given)


def ragged(key, amount, total, bound, skew):
    if amount == 2:
        one = jax.random.randint(key, (), max(1, total - bound), min(bound, total - 1) + 1)
        return jnp.stack([one, total - one])
    lengths = jnp.asarray(split_up(amount, total, bound, skew), jnp.int32)
    couples = (amount - 1) // 2
    giver, receiver = lengths[1:1 + 2 * couples:2], lengths[2:2 + 2 * couples:2]
    margin = jnp.minimum(giver - 1, bound - receiver)
    shifted = jax.random.randint(jax.random.fold_in(key, 1), (couples,), 0, 1 << 20) % (margin + 1)
    lengths = lengths.at[1:1 + 2 * couples:2].set(giver - shifted).at[2:2 + 2 * couples:2].set(receiver + shifted)
    return lengths[jax.random.permutation(jax.random.fold_in(key, 2), amount)]


def normal_values(rng, dims, scale, most, pieces=(), held_as=jnp.bfloat16):
    gain = block_levels(rng, dims, pieces, -0.22, 0.18) if pieces else 1.0
    values = jax.random.normal(rng, dims, jnp.float32) * scale * gain
    return jnp.minimum(jnp.maximum(values, -most), most).astype(held_as)


def setup_inputs(seed: int = 0, part: int = 0) -> dict:
    key_of = jax.random.split(jax.random.key(seed), 7)
    part_keys = jax.random.split(jax.random.fold_in(key_of[6], part), 7)
    queries = draw_queries(jax.random.fold_in(jax.random.fold_in(key_of[6], part), 71), part)
    key_vectors = draw_key_vectors(jax.random.fold_in(jax.random.fold_in(key_of[6], part), 71), part)
    values = normal_values(part_keys[2], (TOKENS, HEADS * HEAD_DIM), 1.0, 6.0, ((0, 16),))
    grad_out = normal_values(part_keys[3], (TOKENS, HEADS * HEAD_DIM), 1.0, 6.0, ((0, 16),))
    file_lengths = ragged(part_keys[4], FILES, TOKENS, TOKENS // 4, 2).astype(jnp.int32)
    reach_table = set_ends(jax.random.randint(part_keys[5], (BLOCKS,), 1, REACH + 1), jax.random.fold_in(part_keys[5], 1), 1, REACH).astype(jnp.int32)
    return {"queries": queries, "key_vectors": key_vectors, "values": values, "grad_out": grad_out, "file_lengths": file_lengths, "reach_table": reach_table}


def rounded(matrix):
    return lax.optimization_barrier(matrix.astype(jnp.bfloat16))

def file_positions(file_lengths, global_rows):
    file_ends = jnp.cumsum(file_lengths).astype(jnp.int32)
    starts = (file_ends - file_lengths).astype(jnp.int32)
    owned_mask = starts[None, :] <= global_rows[:, None]
    latest = lax.optimization_barrier(jnp.max(jnp.where(owned_mask, starts[None, :], 0), axis=1))
    return (global_rows - latest).astype(jnp.int32)

def rotary(matrix, positions, head_count, head_width, inverse):
    half_width = head_width // 2
    exponent = jnp.arange(half_width, dtype=jnp.float32) * (2.0 / head_width)
    frequency = jnp.exp(exponent * -math.log(10000.0))
    angles = positions.astype(jnp.float32)[:, None] * frequency[None, :]
    cosine = jnp.cos(angles)[:, None, :]
    sine_table = jnp.sin(angles)[:, None, :]
    shaped = matrix.astype(jnp.float32).reshape(matrix.shape[0], head_count, head_width)
    former = shaped[..., :half_width]
    latter = shaped[..., half_width:]
    if inverse:
        turned = jnp.concatenate([former * cosine + latter * sine_table, latter * cosine - former * sine_table], axis=-1)
    else:
        turned = jnp.concatenate([former * cosine - latter * sine_table, latter * cosine + former * sine_table], axis=-1)
    return turned.reshape(matrix.shape[0], head_count * head_width)

def block_sources(per_shard, levels):
    layout = []
    for query_block in range(per_shard):
        entries = [(0, query_block)]
        for level_index in range(levels):
            target = query_block - 2 ** level_index
            entries.append((-(target // per_shard), target % per_shard))
        layout.append(entries)
    return layout

def reach_mask(reach_rows, first_block, per_shard, levels):
    block_ids = first_block + jnp.arange(per_shard, dtype=jnp.int32)
    level_ids = jnp.arange(levels, dtype=jnp.int32)
    distances = jnp.array([2 ** level_index for level_index in range(levels)], dtype=jnp.int32)
    reached = (level_ids[None, :] < reach_rows[:, None]) & (block_ids[:, None] - distances[None, :] >= 0)
    return jnp.concatenate([jnp.ones((per_shard, 1), dtype=bool), reached], axis=1)

def score_mask(valid_slots, block_rows):
    row_ids = jnp.arange(block_rows)
    causal = row_ids[None, :] <= row_ids[:, None]
    first_slot = jnp.arange(valid_slots.shape[1]) == 0
    inside = jnp.where(first_slot[:, None, None], causal[None], True)
    allowed = inside[None] & valid_slots[:, :, None, None]
    return jnp.transpose(allowed, (0, 2, 1, 3))[:, None]

def product(form, left, right):
    return jnp.einsum(form, left.astype(jnp.float32), right.astype(jnp.float32), precision=lax.Precision.HIGHEST)

def reference(queries, key_vectors, values, grad_out, file_lengths, reach_table):
    per_shard = TOK_DEV // BLOCK
    levels = (BLOCKS - 1).bit_length()
    layout = block_sources(per_shard, levels)
    slot_count = N_CTX.bit_length()
    scale_factor = 1.0 / math.sqrt(HEAD_DIM)
    positions = file_positions(file_lengths, jnp.arange(TOKENS, dtype=jnp.int32))
    query_rot = rounded(rotary(queries, positions, HEADS, HEAD_DIM, False))
    key_rot = rounded(rotary(key_vectors, positions, HEADS, HEAD_DIM, False))
    shape_five = (N_CTX, per_shard, BLOCK, HEADS, HEAD_DIM)
    key_blocks = key_rot.reshape(shape_five)
    value_blocks = values.reshape(shape_five)
    query_blocks = query_rot.reshape(shape_five)
    grad_blocks = grad_out.reshape(shape_five)
    reach_blocks = reach_table.reshape(N_CTX, per_shard)

    def pick(source, shard_index, offset, block_index):
        chosen = lax.dynamic_index_in_dim(source, jnp.maximum(shard_index - offset, 0).astype(jnp.int32), 0, keepdims=False)
        return chosen[block_index]

    def shard_step(carried, inputs):
        key_accum, value_accum = carried
        query_stack, grad_stack, reach_rows, shard_index = inputs
        key_stack = jnp.stack([jnp.stack([pick(key_blocks, shard_index, offset, block_index) for offset, block_index in entries]) for entries in layout])
        value_stack = jnp.stack([jnp.stack([pick(value_blocks, shard_index, offset, block_index) for offset, block_index in entries]) for entries in layout])
        valid_slots = reach_mask(reach_rows, shard_index * per_shard, per_shard, levels)
        allowed = score_mask(valid_slots, BLOCK)
        scores = jnp.where(allowed, product('bthd,bnuhd->bhtnu', query_stack, key_stack) * scale_factor, -1e+30)
        row_peak = lax.optimization_barrier(jnp.max(scores, axis=(3, 4), keepdims=True))
        summed = lax.optimization_barrier(jnp.sum(jnp.exp(scores - row_peak), axis=(3, 4), keepdims=True))
        log_total = row_peak + jnp.log(summed)
        weights32 = jnp.exp(scores - log_total)
        weights = rounded(weights32)
        output = rounded(product('bhtnu,bnuhd->bthd', weights, value_stack))
        grad_probs = product('bthd,bnuhd->bhtnu', grad_stack, value_stack)
        delta_rows = lax.optimization_barrier(jnp.sum(grad_stack.astype(jnp.float32) * output.astype(jnp.float32), axis=-1))
        delta_rows = jnp.transpose(delta_rows, (0, 2, 1))[:, :, :, None, None]
        grad_scores = rounded(weights32 * (grad_probs - delta_rows) * scale_factor)
        query_grad = product('bhtnu,bnuhd->bthd', grad_scores, key_stack)
        key_terms = product('bhtnu,bthd->bnuhd', grad_scores, query_stack)
        value_terms = product('bhtnu,bthd->bnuhd', weights, grad_stack)
        key_parts = [jnp.zeros((per_shard, BLOCK, HEADS, HEAD_DIM), jnp.float32) for slot_index in range(slot_count)]
        value_parts = [jnp.zeros((per_shard, BLOCK, HEADS, HEAD_DIM), jnp.float32) for slot_index in range(slot_count)]
        for query_block, entries in enumerate(layout):
            for slot_position, (offset, block_index) in enumerate(entries):
                slot_number = offset.bit_length()
                key_parts[slot_number] = key_parts[slot_number].at[block_index].add(key_terms[query_block, slot_position])
                value_parts[slot_number] = value_parts[slot_number].at[block_index].add(value_terms[query_block, slot_position])
        for slot_index in range(slot_count):
            offset = 0 if slot_index == 0 else 2 ** (slot_index - 1)
            target = jnp.maximum(shard_index - offset, 0).astype(jnp.int32)
            key_accum = key_accum.at[target].add(rounded(key_parts[slot_index]).astype(jnp.float32))
            value_accum = value_accum.at[target].add(rounded(value_parts[slot_index]).astype(jnp.float32))
        return ((key_accum, value_accum), (output, query_grad))
    zero_accum = jnp.zeros(shape_five, jnp.float32)
    shard_ids = jnp.arange(N_CTX, dtype=jnp.int32)
    (key_accum, value_accum), (outputs, query_grads) = lax.scan(shard_step, (zero_accum, zero_accum), (query_blocks, grad_blocks, reach_blocks, shard_ids))
    width_all = HEADS * HEAD_DIM
    attended = outputs.reshape(TOKENS, width_all)
    grad_queries = rotary(query_grads.reshape(TOKENS, width_all), positions, HEADS, HEAD_DIM, True).astype(jnp.bfloat16)
    grad_keys = rotary(key_accum.reshape(TOKENS, width_all), positions, HEADS, HEAD_DIM, True).astype(jnp.bfloat16)
    grad_values = value_accum.reshape(TOKENS, width_all).astype(jnp.bfloat16)
    return (attended, grad_queries, grad_keys, grad_values)
```

```python
import math

import jax
import jax.numpy as jnp
from jax import lax
from jax.sharding import PartitionSpec as P

HEADS = 16
HEAD_DIM = 128
BLOCK = 128
CHUNKS = 4


def from_behind(value, axis, steps):
    count = lax.axis_size(axis)
    leading, last = (max(0, -steps), min(count, count - steps))
    return lax.ppermute(value, axis, [(source, source + steps) for source in range(leading, last)])


def rounded(matrix):
    return lax.optimization_barrier(matrix.astype(jnp.bfloat16))


def file_positions(file_lengths, global_rows):
    file_ends = jnp.cumsum(file_lengths)
    starts = file_ends - file_lengths
    owned_mask = starts[None, :] <= global_rows[:, None]
    latest = jnp.max(jnp.where(owned_mask, starts[None, :], 0), axis=1)
    return global_rows - latest


def rotary(matrix, positions, head_count, head_width, inverse):
    half_width = head_width // 2
    exponent = jnp.arange(half_width, dtype=jnp.float32) * (2.0 / head_width)
    frequency = jnp.exp(exponent * -math.log(10000.0))
    angles = positions.astype(jnp.float32)[:, None] * frequency[None, :]
    cosine = jnp.cos(angles)[:, None, :]
    sine_table = jnp.sin(angles)[:, None, :]
    shaped = matrix.astype(jnp.float32).reshape(matrix.shape[0], head_count, head_width)
    former = shaped[..., :half_width]
    latter = shaped[..., half_width:]
    if inverse:
        turned = jnp.concatenate(
            [former * cosine + latter * sine_table, latter * cosine - former * sine_table], axis=-1
        )
    else:
        turned = jnp.concatenate(
            [former * cosine - latter * sine_table, latter * cosine + former * sine_table], axis=-1
        )
    return turned.reshape(matrix.shape[0], head_count * head_width)


def reach_mask(reach_rows, first_block, per_shard, levels):
    block_ids = first_block + jnp.arange(per_shard, dtype=jnp.int32)
    level_ids = jnp.arange(levels, dtype=jnp.int32)
    distances = jnp.array([2**level_index for level_index in range(levels)], dtype=jnp.int32)
    reached = (level_ids[None, :] < reach_rows[:, None]) & (
        block_ids[:, None] - distances[None, :] >= 0
    )
    return jnp.concatenate([jnp.ones((per_shard, 1), dtype=bool), reached], axis=1)


def score_mask(valid_slots, block_rows):
    row_ids = jnp.arange(block_rows)
    causal = row_ids[None, :] <= row_ids[:, None]
    first_slot = jnp.arange(valid_slots.shape[1]) == 0
    inside = jnp.where(first_slot[:, None, None], causal[None], True)
    allowed = inside[None] & valid_slots[:, :, None, None]
    return jnp.transpose(allowed, (0, 2, 1, 3))[:, None]


def attend_chunk(query_c, key_c, value_c, grad_c, allowed, offsets, heads):
    scale_factor = 1.0 / math.sqrt(HEAD_DIM)
    rows = query_c.shape[0]
    head_shape = (rows, heads, HEAD_DIM)
    pair = jnp.stack([key_c, value_c])
    received = [pair] + [from_behind(pair, "ctx", offset) for offset in offsets]
    key_stack = jnp.stack([moved[0].reshape(head_shape) for moved in received])[None]
    value_stack = jnp.stack([moved[1].reshape(head_shape) for moved in received])[None]
    query_stack = query_c.reshape((1,) + head_shape)
    grad_stack = grad_c.reshape((1,) + head_shape)
    raw_scores = (
        jnp.einsum("bthd,bnuhd->bhtnu", query_stack, key_stack, preferred_element_type=jnp.float32)
        * scale_factor
    )
    scores = jnp.where(allowed, raw_scores, -1e30)
    row_peak = jnp.max(scores, axis=(3, 4), keepdims=True)
    summed = jnp.sum(jnp.exp(scores - row_peak), axis=(3, 4), keepdims=True)
    log_total = row_peak + jnp.log(summed)
    weights32 = jnp.exp(scores - log_total)
    weights = rounded(weights32)
    output = rounded(
        jnp.einsum("bhtnu,bnuhd->bthd", weights, value_stack, preferred_element_type=jnp.float32)
    )
    grad_probs = jnp.einsum(
        "bthd,bnuhd->bhtnu", grad_stack, value_stack, preferred_element_type=jnp.float32
    )
    delta_rows = jnp.sum(grad_stack.astype(jnp.float32) * output.astype(jnp.float32), axis=-1)
    delta_rows = jnp.transpose(delta_rows, (0, 2, 1))[:, :, :, None, None]
    grad_scores = rounded(weights32 * (grad_probs - delta_rows) * scale_factor)
    query_grad = jnp.einsum(
        "bhtnu,bnuhd->bthd", grad_scores, key_stack, preferred_element_type=jnp.float32
    )
    key_terms = jnp.einsum(
        "bhtnu,bthd->bnuhd", grad_scores, query_stack, preferred_element_type=jnp.float32
    )
    value_terms = jnp.einsum(
        "bhtnu,bthd->bnuhd", weights, grad_stack, preferred_element_type=jnp.float32
    )
    key_accum = rounded(key_terms[0, 0]).astype(jnp.float32)
    value_accum = rounded(value_terms[0, 0]).astype(jnp.float32)
    for slot_index, offset in enumerate(offsets, start=1):
        outgoing = jnp.stack([key_terms[0, slot_index], value_terms[0, slot_index]]).astype(
            jnp.bfloat16
        )
        returned = from_behind(outgoing, "ctx", -offset)
        key_accum = key_accum + returned[0].astype(jnp.float32)
        value_accum = value_accum + returned[1].astype(jnp.float32)
    width = heads * HEAD_DIM
    return (
        output.reshape(rows, width),
        query_grad.reshape(rows, width),
        key_accum.reshape(rows, width),
        value_accum.reshape(rows, width),
    )


def on_device(queries, key_vectors, values, grad_out, file_lengths, reach_table):
    local_rows = queries.shape[0]
    width_all = queries.shape[1]
    per_shard = local_rows // BLOCK
    ctx_size = lax.axis_size("ctx")
    levels = (per_shard * ctx_size - 1).bit_length()
    offsets = [2**level_index for level_index in range(levels)]
    shard_index = lax.axis_index("ctx")
    global_rows = shard_index * local_rows + jnp.arange(local_rows, dtype=jnp.int32)
    positions = file_positions(file_lengths, global_rows)
    query_rot = rounded(rotary(queries, positions, HEADS, HEAD_DIM, False))
    key_rot = rounded(rotary(key_vectors, positions, HEADS, HEAD_DIM, False))
    valid_slots = reach_mask(reach_table, shard_index * per_shard, per_shard, levels)
    allowed = score_mask(valid_slots, BLOCK)
    chunk_heads = HEADS // CHUNKS
    chunk_width = chunk_heads * HEAD_DIM
    pieces = []
    for chunk in range(CHUNKS):
        cols = slice(chunk * chunk_width, (chunk + 1) * chunk_width)
        pieces.append(
            attend_chunk(
                query_rot[:, cols],
                key_rot[:, cols],
                values[:, cols],
                grad_out[:, cols],
                allowed,
                offsets,
                chunk_heads,
            )
        )
    attended, query_grad, key_accum, value_accum = [
        jnp.concatenate(parts, axis=1) for parts in zip(*pieces)
    ]
    grad_queries = rotary(query_grad, positions, HEADS, HEAD_DIM, True).astype(jnp.bfloat16)
    grad_keys = rotary(key_accum, positions, HEADS, HEAD_DIM, True).astype(jnp.bfloat16)
    grad_values = value_accum.astype(jnp.bfloat16)
    return (attended, grad_queries, grad_keys, grad_values)


def solution(mesh):
    placed = (
        P(("groups", "ctx"), None),
        P(("groups", "ctx"), None),
        P(("groups", "ctx"), None),
        P(("groups", "ctx"), None),
        P("groups"),
        P(("groups", "ctx")),
    )
    return jax.shard_map(
        on_device,
        mesh=mesh,
        in_specs=placed,
        out_specs=(
            P(("groups", "ctx"), None),
            P(("groups", "ctx"), None),
            P(("groups", "ctx"), None),
            P(("groups", "ctx"), None),
        ),
        check_vma=False,
    )
```

```python
import math

import jax
import jax.numpy as jnp
from jax import lax
from jax.sharding import PartitionSpec as P

HEADS = 16
HEAD_DIM = 128
BLOCK = 128
CHUNKS = 4


def from_behind(value, axis, steps):
    count = lax.axis_size(axis)
    leading, last = (max(0, -steps), min(count, count - steps))
    return lax.ppermute(value, axis, [(source, source + steps) for source in range(leading, last)])


def rounded(matrix):
    return lax.optimization_barrier(matrix.astype(jnp.bfloat16))


def file_positions(file_lengths, global_rows):
    file_ends = jnp.cumsum(file_lengths)
    starts = file_ends - file_lengths
    owned_mask = starts[None, :] <= global_rows[:, None]
    latest = jnp.max(jnp.where(owned_mask, starts[None, :], 0), axis=1)
    return global_rows - latest


def rotary(matrix, positions, head_count, head_width, inverse):
    half_width = head_width // 2
    exponent = jnp.arange(half_width, dtype=jnp.float32) * (2.0 / head_width)
    frequency = jnp.exp(exponent * -math.log(10000.0))
    angles = positions.astype(jnp.float32)[:, None] * frequency[None, :]
    cosine = jnp.cos(angles)[:, None, :]
    sine_table = jnp.sin(angles)[:, None, :]
    shaped = matrix.astype(jnp.float32).reshape(matrix.shape[0], head_count, head_width)
    former = shaped[..., :half_width]
    latter = shaped[..., half_width:]
    if inverse:
        turned = jnp.concatenate(
            [former * cosine + latter * sine_table, latter * cosine - former * sine_table], axis=-1
        )
    else:
        turned = jnp.concatenate(
            [former * cosine - latter * sine_table, latter * cosine + former * sine_table], axis=-1
        )
    return turned.reshape(matrix.shape[0], head_count * head_width)


def reach_mask(reach_rows, first_block, per_shard, levels):
    block_ids = first_block + jnp.arange(per_shard, dtype=jnp.int32)
    level_ids = jnp.arange(levels, dtype=jnp.int32)
    distances = jnp.array([2**level_index for level_index in range(levels)], dtype=jnp.int32)
    reached = (level_ids[None, :] < reach_rows[:, None]) & (
        block_ids[:, None] - distances[None, :] >= 0
    )
    return jnp.concatenate([jnp.ones((per_shard, 1), dtype=bool), reached], axis=1)


def score_mask(valid_slots, block_rows):
    row_ids = jnp.arange(block_rows)
    causal = row_ids[None, :] <= row_ids[:, None]
    first_slot = jnp.arange(valid_slots.shape[1]) == 0
    inside = jnp.where(first_slot[:, None, None], causal[None], True)
    allowed = inside[None] & valid_slots[:, :, None, None]
    return jnp.transpose(allowed, (0, 2, 1, 3))[:, None]


def send_chunk(key_c, value_c, offsets):
    pair = jnp.stack([key_c, value_c])
    return [pair] + [from_behind(pair, "ctx", offset) for offset in offsets]


def attend_chunk(query_c, received, grad_c, allowed, offsets, heads):
    scale_factor = 1.0 / math.sqrt(HEAD_DIM)
    rows = query_c.shape[0]
    head_shape = (rows, heads, HEAD_DIM)
    key_stack = jnp.stack([moved[0].reshape(head_shape) for moved in received])[None]
    value_stack = jnp.stack([moved[1].reshape(head_shape) for moved in received])[None]
    query_stack = query_c.reshape((1,) + head_shape)
    grad_stack = grad_c.reshape((1,) + head_shape)
    raw_scores = (
        jnp.einsum("bthd,bnuhd->bhtnu", query_stack, key_stack, preferred_element_type=jnp.float32)
        * scale_factor
    )
    scores = jnp.where(allowed, raw_scores, -1e30)
    row_peak = jnp.max(scores, axis=(3, 4), keepdims=True)
    summed = jnp.sum(jnp.exp(scores - row_peak), axis=(3, 4), keepdims=True)
    log_total = row_peak + jnp.log(summed)
    weights32 = jnp.exp(scores - log_total)
    weights = rounded(weights32)
    output = rounded(
        jnp.einsum("bhtnu,bnuhd->bthd", weights, value_stack, preferred_element_type=jnp.float32)
    )
    grad_probs = jnp.einsum(
        "bthd,bnuhd->bhtnu", grad_stack, value_stack, preferred_element_type=jnp.float32
    )
    delta_rows = jnp.sum(grad_stack.astype(jnp.float32) * output.astype(jnp.float32), axis=-1)
    delta_rows = jnp.transpose(delta_rows, (0, 2, 1))[:, :, :, None, None]
    grad_scores = rounded(weights32 * (grad_probs - delta_rows) * scale_factor)
    query_grad = jnp.einsum(
        "bhtnu,bnuhd->bthd", grad_scores, key_stack, preferred_element_type=jnp.float32
    )
    key_terms = jnp.einsum(
        "bhtnu,bthd->bnuhd", grad_scores, query_stack, preferred_element_type=jnp.float32
    )
    value_terms = jnp.einsum(
        "bhtnu,bthd->bnuhd", weights, grad_stack, preferred_element_type=jnp.float32
    )
    own = (rounded(key_terms[0, 0]), rounded(value_terms[0, 0]))
    outgoing = [
        jnp.stack([key_terms[0, slot_index], value_terms[0, slot_index]]).astype(jnp.bfloat16)
        for slot_index in range(1, len(offsets) + 1)
    ]
    return output, query_grad, own, outgoing


def gather_back(own, outgoing, offsets):
    key_accum = own[0].astype(jnp.float32)
    value_accum = own[1].astype(jnp.float32)
    for parts, offset in zip(outgoing, offsets):
        returned = from_behind(parts, "ctx", -offset)
        key_accum = key_accum + returned[0].astype(jnp.float32)
        value_accum = value_accum + returned[1].astype(jnp.float32)
    return key_accum, value_accum


def on_device(queries, key_vectors, values, grad_out, file_lengths, reach_table):
    local_rows = queries.shape[0]
    width_all = queries.shape[1]
    per_shard = local_rows // BLOCK
    ctx_size = lax.axis_size("ctx")
    levels = (per_shard * ctx_size - 1).bit_length()
    offsets = [2**level_index for level_index in range(levels)]
    shard_index = lax.axis_index("ctx")
    global_rows = shard_index * local_rows + jnp.arange(local_rows, dtype=jnp.int32)
    positions = file_positions(file_lengths, global_rows)
    query_rot = rounded(rotary(queries, positions, HEADS, HEAD_DIM, False))
    key_rot = rounded(rotary(key_vectors, positions, HEADS, HEAD_DIM, False))
    valid_slots = reach_mask(reach_table, shard_index * per_shard, per_shard, levels)
    allowed = score_mask(valid_slots, BLOCK)
    chunk_heads = HEADS // CHUNKS
    chunk_width = chunk_heads * HEAD_DIM
    columns = [slice(chunk * chunk_width, (chunk + 1) * chunk_width) for chunk in range(CHUNKS)]
    pieces = []
    pending = []
    previous = None
    for chunk, cols in enumerate(columns):
        key_c, value_c = key_rot[:, cols], values[:, cols]
        if previous is not None:
            key_c, value_c, _ = lax.optimization_barrier((key_c, value_c, previous))
        if len(pending) >= 2:
            key_c, value_c, _ = lax.optimization_barrier((key_c, value_c, pending[-2]))
        received = send_chunk(key_c, value_c, offsets)
        previous = received[1:]
        output, query_grad, own, outgoing = attend_chunk(
            query_rot[:, cols], received, grad_out[:, cols], allowed, offsets, chunk_heads
        )
        pending.append(outgoing)
        key_accum_c, value_accum_c = gather_back(own, outgoing, offsets)
        rows = query_rot.shape[0]
        pieces.append(
            (
                output.reshape(rows, chunk_width),
                query_grad.reshape(rows, chunk_width),
                key_accum_c.reshape(rows, chunk_width),
                value_accum_c.reshape(rows, chunk_width),
            )
        )
    attended, query_grad, key_accum, value_accum = [
        jnp.concatenate(parts, axis=1) for parts in zip(*pieces)
    ]
    grad_queries = rotary(query_grad, positions, HEADS, HEAD_DIM, True).astype(jnp.bfloat16)
    grad_keys = rotary(key_accum, positions, HEADS, HEAD_DIM, True).astype(jnp.bfloat16)
    grad_values = value_accum.astype(jnp.bfloat16)
    return (attended, grad_queries, grad_keys, grad_values)


def solution(mesh):
    placed = (
        P(("groups", "ctx"), None),
        P(("groups", "ctx"), None),
        P(("groups", "ctx"), None),
        P(("groups", "ctx"), None),
        P("groups"),
        P(("groups", "ctx")),
    )
    return jax.shard_map(
        on_device,
        mesh=mesh,
        in_specs=placed,
        out_specs=(
            P(("groups", "ctx"), None),
            P(("groups", "ctx"), None),
            P(("groups", "ctx"), None),
            P(("groups", "ctx"), None),
        ),
        check_vma=False,
    )
```

```python
import math

import jax
import jax.numpy as jnp
from jax import lax
from jax.sharding import PartitionSpec as P

HEADS = 16
HEAD_DIM = 128
BLOCK = 128
CHUNKS = 1


def from_behind(value, axis, steps):
    count = lax.axis_size(axis)
    leading, last = (max(0, -steps), min(count, count - steps))
    return lax.ppermute(value, axis, [(source, source + steps) for source in range(leading, last)])


def rounded(matrix):
    return lax.optimization_barrier(matrix.astype(jnp.bfloat16))


def file_positions(file_lengths, global_rows):
    file_ends = jnp.cumsum(file_lengths)
    starts = file_ends - file_lengths
    owned_mask = starts[None, :] <= global_rows[:, None]
    latest = jnp.max(jnp.where(owned_mask, starts[None, :], 0), axis=1)
    return global_rows - latest


def rotary(matrix, positions, head_count, head_width, inverse):
    half_width = head_width // 2
    exponent = jnp.arange(half_width, dtype=jnp.float32) * (2.0 / head_width)
    frequency = jnp.exp(exponent * -math.log(10000.0))
    angles = positions.astype(jnp.float32)[:, None] * frequency[None, :]
    cosine = jnp.cos(angles)[:, None, :]
    sine_table = jnp.sin(angles)[:, None, :]
    shaped = matrix.astype(jnp.float32).reshape(matrix.shape[0], head_count, head_width)
    former = shaped[..., :half_width]
    latter = shaped[..., half_width:]
    if inverse:
        turned = jnp.concatenate(
            [former * cosine + latter * sine_table, latter * cosine - former * sine_table], axis=-1
        )
    else:
        turned = jnp.concatenate(
            [former * cosine - latter * sine_table, latter * cosine + former * sine_table], axis=-1
        )
    return turned.reshape(matrix.shape[0], head_count * head_width)


def reach_mask(reach_rows, first_block, per_shard, levels):
    block_ids = first_block + jnp.arange(per_shard, dtype=jnp.int32)
    level_ids = jnp.arange(levels, dtype=jnp.int32)
    distances = jnp.array([2**level_index for level_index in range(levels)], dtype=jnp.int32)
    reached = (level_ids[None, :] < reach_rows[:, None]) & (
        block_ids[:, None] - distances[None, :] >= 0
    )
    return jnp.concatenate([jnp.ones((per_shard, 1), dtype=bool), reached], axis=1)


def score_mask(valid_slots, block_rows):
    row_ids = jnp.arange(block_rows)
    causal = row_ids[None, :] <= row_ids[:, None]
    first_slot = jnp.arange(valid_slots.shape[1]) == 0
    inside = jnp.where(first_slot[:, None, None], causal[None], True)
    allowed = inside[None] & valid_slots[:, :, None, None]
    return jnp.transpose(allowed, (0, 2, 1, 3))[:, None]


def send_chunk(key_c, value_c, offsets):
    pair = jnp.stack([key_c, value_c])
    return [pair] + [from_behind(pair, "ctx", offset) for offset in offsets]


def attend_chunk(query_c, received, grad_c, allowed, offsets, heads):
    scale_factor = 1.0 / math.sqrt(HEAD_DIM)
    rows = query_c.shape[0]
    head_shape = (rows, heads, HEAD_DIM)
    key_stack = jnp.stack([moved[0].reshape(head_shape) for moved in received])[None]
    value_stack = jnp.stack([moved[1].reshape(head_shape) for moved in received])[None]
    query_stack = query_c.reshape((1,) + head_shape)
    grad_stack = grad_c.reshape((1,) + head_shape)
    raw_scores = (
        jnp.einsum("bthd,bnuhd->bhtnu", query_stack, key_stack, preferred_element_type=jnp.float32)
        * scale_factor
    )
    scores = jnp.where(allowed, raw_scores, -1e30)
    row_peak = jnp.max(scores, axis=(3, 4), keepdims=True)
    summed = jnp.sum(jnp.exp(scores - row_peak), axis=(3, 4), keepdims=True)
    log_total = row_peak + jnp.log(summed)
    weights32 = jnp.exp(scores - log_total)
    weights = rounded(weights32)
    output = rounded(
        jnp.einsum("bhtnu,bnuhd->bthd", weights, value_stack, preferred_element_type=jnp.float32)
    )
    grad_probs = jnp.einsum(
        "bthd,bnuhd->bhtnu", grad_stack, value_stack, preferred_element_type=jnp.float32
    )
    delta_rows = jnp.sum(grad_stack.astype(jnp.float32) * output.astype(jnp.float32), axis=-1)
    delta_rows = jnp.transpose(delta_rows, (0, 2, 1))[:, :, :, None, None]
    grad_scores = rounded(weights32 * (grad_probs - delta_rows) * scale_factor)
    query_grad = jnp.einsum(
        "bhtnu,bnuhd->bthd", grad_scores, key_stack, preferred_element_type=jnp.float32
    )
    key_terms = jnp.einsum(
        "bhtnu,bthd->bnuhd", grad_scores, query_stack, preferred_element_type=jnp.float32
    )
    value_terms = jnp.einsum(
        "bhtnu,bthd->bnuhd", weights, grad_stack, preferred_element_type=jnp.float32
    )
    own = (rounded(key_terms[0, 0]), rounded(value_terms[0, 0]))
    outgoing = [
        jnp.stack([key_terms[0, slot_index], value_terms[0, slot_index]]).astype(jnp.bfloat16)
        for slot_index in range(1, len(offsets) + 1)
    ]
    return output, query_grad, own, outgoing


def gather_back(own, outgoing, offsets):
    key_accum = own[0].astype(jnp.float32)
    value_accum = own[1].astype(jnp.float32)
    for parts, offset in zip(outgoing, offsets):
        returned = from_behind(parts, "ctx", -offset)
        key_accum = key_accum + returned[0].astype(jnp.float32)
        value_accum = value_accum + returned[1].astype(jnp.float32)
    return key_accum, value_accum


def on_device(queries, key_vectors, values, grad_out, file_lengths, reach_table):
    local_rows = queries.shape[0]
    width_all = queries.shape[1]
    per_shard = local_rows // BLOCK
    ctx_size = lax.axis_size("ctx")
    levels = (per_shard * ctx_size - 1).bit_length()
    offsets = [2**level_index for level_index in range(levels)]
    shard_index = lax.axis_index("ctx")
    global_rows = shard_index * local_rows + jnp.arange(local_rows, dtype=jnp.int32)
    positions = file_positions(file_lengths, global_rows)
    query_rot = rounded(rotary(queries, positions, HEADS, HEAD_DIM, False))
    key_rot = rounded(rotary(key_vectors, positions, HEADS, HEAD_DIM, False))
    valid_slots = reach_mask(reach_table, shard_index * per_shard, per_shard, levels)
    allowed = score_mask(valid_slots, BLOCK)
    chunk_heads = HEADS // CHUNKS
    chunk_width = chunk_heads * HEAD_DIM
    columns = [slice(chunk * chunk_width, (chunk + 1) * chunk_width) for chunk in range(CHUNKS)]
    pieces = []
    pending = []
    previous = None
    for chunk, cols in enumerate(columns):
        key_c, value_c = key_rot[:, cols], values[:, cols]
        if previous is not None:
            key_c, value_c, _ = lax.optimization_barrier((key_c, value_c, previous))
        if len(pending) >= 2:
            key_c, value_c, _ = lax.optimization_barrier((key_c, value_c, pending[-2]))
        received = send_chunk(key_c, value_c, offsets)
        previous = received[1:]
        output, query_grad, own, outgoing = attend_chunk(
            query_rot[:, cols], received, grad_out[:, cols], allowed, offsets, chunk_heads
        )
        pending.append(outgoing)
        key_accum_c, value_accum_c = gather_back(own, outgoing, offsets)
        rows = query_rot.shape[0]
        pieces.append(
            (
                output.reshape(rows, chunk_width),
                query_grad.reshape(rows, chunk_width),
                key_accum_c.reshape(rows, chunk_width),
                value_accum_c.reshape(rows, chunk_width),
            )
        )
    attended, query_grad, key_accum, value_accum = [
        jnp.concatenate(parts, axis=1) for parts in zip(*pieces)
    ]
    grad_queries = rotary(query_grad, positions, HEADS, HEAD_DIM, True).astype(jnp.bfloat16)
    grad_keys = rotary(key_accum, positions, HEADS, HEAD_DIM, True).astype(jnp.bfloat16)
    grad_values = value_accum.astype(jnp.bfloat16)
    return (attended, grad_queries, grad_keys, grad_values)


def solution(mesh):
    placed = (
        P(("groups", "ctx"), None),
        P(("groups", "ctx"), None),
        P(("groups", "ctx"), None),
        P(("groups", "ctx"), None),
        P("groups"),
        P(("groups", "ctx")),
    )
    return jax.shard_map(
        on_device,
        mesh=mesh,
        in_specs=placed,
        out_specs=(
            P(("groups", "ctx"), None),
            P(("groups", "ctx"), None),
            P(("groups", "ctx"), None),
            P(("groups", "ctx"), None),
        ),
        check_vma=False,
    )
```

```python
import math

import jax
import jax.numpy as jnp
from jax import lax
from jax.sharding import PartitionSpec as P

HEADS = 16
HEAD_DIM = 128
BLOCK = 128
CHUNKS = 1


def from_behind(value, axis, steps):
    count = lax.axis_size(axis)
    leading, last = (max(0, -steps), min(count, count - steps))
    return lax.ppermute(value, axis, [(source, source + steps) for source in range(leading, last)])


def rounded(matrix):
    return lax.optimization_barrier(matrix.astype(jnp.bfloat16))


def file_positions(file_lengths, global_rows):
    file_ends = jnp.cumsum(file_lengths)
    starts = file_ends - file_lengths
    owned_mask = starts[None, :] <= global_rows[:, None]
    latest = jnp.max(jnp.where(owned_mask, starts[None, :], 0), axis=1)
    return global_rows - latest


def rotary(matrix, positions, head_count, head_width, inverse):
    half_width = head_width // 2
    exponent = jnp.arange(half_width, dtype=jnp.float32) * (2.0 / head_width)
    frequency = jnp.exp(exponent * -math.log(10000.0))
    angles = positions.astype(jnp.float32)[:, None] * frequency[None, :]
    cosine = jnp.cos(angles)[:, None, :]
    sine_table = jnp.sin(angles)[:, None, :]
    shaped = matrix.astype(jnp.float32).reshape(matrix.shape[0], head_count, head_width)
    former = shaped[..., :half_width]
    latter = shaped[..., half_width:]
    if inverse:
        turned = jnp.concatenate(
            [former * cosine + latter * sine_table, latter * cosine - former * sine_table], axis=-1
        )
    else:
        turned = jnp.concatenate(
            [former * cosine - latter * sine_table, latter * cosine + former * sine_table], axis=-1
        )
    return turned.reshape(matrix.shape[0], head_count * head_width)


def reach_mask(reach_rows, first_block, per_shard, levels):
    block_ids = first_block + jnp.arange(per_shard, dtype=jnp.int32)
    level_ids = jnp.arange(levels, dtype=jnp.int32)
    distances = jnp.array([2**level_index for level_index in range(levels)], dtype=jnp.int32)
    reached = (level_ids[None, :] < reach_rows[:, None]) & (
        block_ids[:, None] - distances[None, :] >= 0
    )
    return jnp.concatenate([jnp.ones((per_shard, 1), dtype=bool), reached], axis=1)


def score_mask(valid_slots, block_rows):
    row_ids = jnp.arange(block_rows)
    causal = row_ids[None, :] <= row_ids[:, None]
    first_slot = jnp.arange(valid_slots.shape[1]) == 0
    inside = jnp.where(first_slot[:, None, None], causal[None], True)
    allowed = inside[None] & valid_slots[:, :, None, None]
    return jnp.transpose(allowed, (0, 2, 1, 3))[:, None]


def send_chunk(key_c, value_c, offsets):
    pair = jnp.stack([key_c, value_c])
    received = {0: pair}
    for offset in offsets:
        if (offset.bit_length() - 1) % 2 == 1:
            half = offset // 2
            received[offset] = from_behind(received[half], "ctx", half)
        else:
            received[offset] = from_behind(pair, "ctx", offset)
    return [received[0]] + [received[offset] for offset in offsets]


def attend_chunk(query_c, received, grad_c, allowed, offsets, heads):
    scale_factor = 1.0 / math.sqrt(HEAD_DIM)
    rows = query_c.shape[0]
    head_shape = (rows, heads, HEAD_DIM)
    key_stack = jnp.stack([moved[0].reshape(head_shape) for moved in received])[None]
    value_stack = jnp.stack([moved[1].reshape(head_shape) for moved in received])[None]
    query_stack = query_c.reshape((1,) + head_shape)
    grad_stack = grad_c.reshape((1,) + head_shape)
    raw_scores = (
        jnp.einsum("bthd,bnuhd->bhtnu", query_stack, key_stack, preferred_element_type=jnp.float32)
        * scale_factor
    )
    scores = jnp.where(allowed, raw_scores, -1e30)
    row_peak = jnp.max(scores, axis=(3, 4), keepdims=True)
    summed = jnp.sum(jnp.exp(scores - row_peak), axis=(3, 4), keepdims=True)
    log_total = row_peak + jnp.log(summed)
    weights32 = jnp.exp(scores - log_total)
    weights = rounded(weights32)
    output = rounded(
        jnp.einsum("bhtnu,bnuhd->bthd", weights, value_stack, preferred_element_type=jnp.float32)
    )
    grad_probs = jnp.einsum(
        "bthd,bnuhd->bhtnu", grad_stack, value_stack, preferred_element_type=jnp.float32
    )
    delta_rows = jnp.sum(grad_stack.astype(jnp.float32) * output.astype(jnp.float32), axis=-1)
    delta_rows = jnp.transpose(delta_rows, (0, 2, 1))[:, :, :, None, None]
    grad_scores = rounded(weights32 * (grad_probs - delta_rows) * scale_factor)
    query_grad = jnp.einsum(
        "bhtnu,bnuhd->bthd", grad_scores, key_stack, preferred_element_type=jnp.float32
    )
    key_terms = jnp.einsum(
        "bhtnu,bthd->bnuhd", grad_scores, query_stack, preferred_element_type=jnp.float32
    )
    value_terms = jnp.einsum(
        "bhtnu,bthd->bnuhd", weights, grad_stack, preferred_element_type=jnp.float32
    )
    own = (rounded(key_terms[0, 0]), rounded(value_terms[0, 0]))
    outgoing = [
        jnp.stack([key_terms[0, slot_index], value_terms[0, slot_index]]).astype(jnp.bfloat16)
        for slot_index in range(1, len(offsets) + 1)
    ]
    return output, query_grad, own, outgoing


def gather_back(own, outgoing, offsets):
    key_accum = own[0].astype(jnp.float32)
    value_accum = own[1].astype(jnp.float32)
    for parts, offset in zip(outgoing, offsets):
        returned = from_behind(parts, "ctx", -offset)
        key_accum = key_accum + returned[0].astype(jnp.float32)
        value_accum = value_accum + returned[1].astype(jnp.float32)
    return key_accum, value_accum


def on_device(queries, key_vectors, values, grad_out, file_lengths, reach_table):
    local_rows = queries.shape[0]
    width_all = queries.shape[1]
    per_shard = local_rows // BLOCK
    ctx_size = lax.axis_size("ctx")
    levels = (per_shard * ctx_size - 1).bit_length()
    offsets = [2**level_index for level_index in range(levels)]
    shard_index = lax.axis_index("ctx")
    global_rows = shard_index * local_rows + jnp.arange(local_rows, dtype=jnp.int32)
    positions = file_positions(file_lengths, global_rows)
    query_rot = rounded(rotary(queries, positions, HEADS, HEAD_DIM, False))
    key_rot = rounded(rotary(key_vectors, positions, HEADS, HEAD_DIM, False))
    valid_slots = reach_mask(reach_table, shard_index * per_shard, per_shard, levels)
    allowed = score_mask(valid_slots, BLOCK)
    chunk_heads = HEADS // CHUNKS
    chunk_width = chunk_heads * HEAD_DIM
    columns = [slice(chunk * chunk_width, (chunk + 1) * chunk_width) for chunk in range(CHUNKS)]
    pieces = []
    pending = []
    previous = None
    for chunk, cols in enumerate(columns):
        key_c, value_c = key_rot[:, cols], values[:, cols]
        if previous is not None:
            key_c, value_c, _ = lax.optimization_barrier((key_c, value_c, previous))
        if len(pending) >= 2:
            key_c, value_c, _ = lax.optimization_barrier((key_c, value_c, pending[-2]))
        received = send_chunk(key_c, value_c, offsets)
        previous = received[1:]
        output, query_grad, own, outgoing = attend_chunk(
            query_rot[:, cols], received, grad_out[:, cols], allowed, offsets, chunk_heads
        )
        pending.append(outgoing)
        key_accum_c, value_accum_c = gather_back(own, outgoing, offsets)
        rows = query_rot.shape[0]
        pieces.append(
            (
                output.reshape(rows, chunk_width),
                query_grad.reshape(rows, chunk_width),
                key_accum_c.reshape(rows, chunk_width),
                value_accum_c.reshape(rows, chunk_width),
            )
        )
    attended, query_grad, key_accum, value_accum = [
        jnp.concatenate(parts, axis=1) for parts in zip(*pieces)
    ]
    grad_queries = rotary(query_grad, positions, HEADS, HEAD_DIM, True).astype(jnp.bfloat16)
    grad_keys = rotary(key_accum, positions, HEADS, HEAD_DIM, True).astype(jnp.bfloat16)
    grad_values = value_accum.astype(jnp.bfloat16)
    return (attended, grad_queries, grad_keys, grad_values)


def solution(mesh):
    placed = (
        P(("groups", "ctx"), None),
        P(("groups", "ctx"), None),
        P(("groups", "ctx"), None),
        P(("groups", "ctx"), None),
        P("groups"),
        P(("groups", "ctx")),
    )
    return jax.shard_map(
        on_device,
        mesh=mesh,
        in_specs=placed,
        out_specs=(
            P(("groups", "ctx"), None),
            P(("groups", "ctx"), None),
            P(("groups", "ctx"), None),
            P(("groups", "ctx"), None),
        ),
        check_vma=False,
    )
```

```python
import math

import jax
import jax.numpy as jnp
from jax import lax
from jax.sharding import PartitionSpec as P

HEADS = 16
HEAD_DIM = 128
BLOCK = 128
CHUNKS = 2


def from_behind(value, axis, steps):
    count = lax.axis_size(axis)
    leading, last = (max(0, -steps), min(count, count - steps))
    return lax.ppermute(value, axis, [(source, source + steps) for source in range(leading, last)])


def rounded(matrix):
    return lax.optimization_barrier(matrix.astype(jnp.bfloat16))


def file_positions(file_lengths, global_rows):
    file_ends = jnp.cumsum(file_lengths)
    starts = file_ends - file_lengths
    owned_mask = starts[None, :] <= global_rows[:, None]
    latest = jnp.max(jnp.where(owned_mask, starts[None, :], 0), axis=1)
    return global_rows - latest


def rotary(matrix, positions, head_count, head_width, inverse):
    half_width = head_width // 2
    exponent = jnp.arange(half_width, dtype=jnp.float32) * (2.0 / head_width)
    frequency = jnp.exp(exponent * -math.log(10000.0))
    angles = positions.astype(jnp.float32)[:, None] * frequency[None, :]
    cosine = jnp.cos(angles)[:, None, :]
    sine_table = jnp.sin(angles)[:, None, :]
    shaped = matrix.astype(jnp.float32).reshape(matrix.shape[0], head_count, head_width)
    former = shaped[..., :half_width]
    latter = shaped[..., half_width:]
    if inverse:
        turned = jnp.concatenate(
            [former * cosine + latter * sine_table, latter * cosine - former * sine_table], axis=-1
        )
    else:
        turned = jnp.concatenate(
            [former * cosine - latter * sine_table, latter * cosine + former * sine_table], axis=-1
        )
    return turned.reshape(matrix.shape[0], head_count * head_width)


def reach_mask(reach_rows, first_block, per_shard, levels):
    block_ids = first_block + jnp.arange(per_shard, dtype=jnp.int32)
    level_ids = jnp.arange(levels, dtype=jnp.int32)
    distances = jnp.array([2**level_index for level_index in range(levels)], dtype=jnp.int32)
    reached = (level_ids[None, :] < reach_rows[:, None]) & (
        block_ids[:, None] - distances[None, :] >= 0
    )
    return jnp.concatenate([jnp.ones((per_shard, 1), dtype=bool), reached], axis=1)


def score_mask(valid_slots, block_rows):
    row_ids = jnp.arange(block_rows)
    causal = row_ids[None, :] <= row_ids[:, None]
    first_slot = jnp.arange(valid_slots.shape[1]) == 0
    inside = jnp.where(first_slot[:, None, None], causal[None], True)
    allowed = inside[None] & valid_slots[:, :, None, None]
    return jnp.transpose(allowed, (0, 2, 1, 3))[:, None]


def send_chunk(key_c, value_c, offsets):
    pair = jnp.stack([key_c, value_c])
    received = {0: pair}
    for offset in offsets:
        if (offset.bit_length() - 1) % 2 == 1:
            half = offset // 2
            received[offset] = from_behind(received[half], "ctx", half)
        else:
            received[offset] = from_behind(pair, "ctx", offset)
    return [received[0]] + [received[offset] for offset in offsets]


def attend_chunk(query_c, received, grad_c, allowed, offsets, heads):
    scale_factor = 1.0 / math.sqrt(HEAD_DIM)
    rows = query_c.shape[0]
    head_shape = (rows, heads, HEAD_DIM)
    key_stack = jnp.stack([moved[0].reshape(head_shape) for moved in received])[None]
    value_stack = jnp.stack([moved[1].reshape(head_shape) for moved in received])[None]
    query_stack = query_c.reshape((1,) + head_shape)
    grad_stack = grad_c.reshape((1,) + head_shape)
    raw_scores = (
        jnp.einsum("bthd,bnuhd->bhtnu", query_stack, key_stack, preferred_element_type=jnp.float32)
        * scale_factor
    )
    scores = jnp.where(allowed, raw_scores, -1e30)
    row_peak = jnp.max(scores, axis=(3, 4), keepdims=True)
    summed = jnp.sum(jnp.exp(scores - row_peak), axis=(3, 4), keepdims=True)
    log_total = row_peak + jnp.log(summed)
    weights32 = jnp.exp(scores - log_total)
    weights = rounded(weights32)
    output = rounded(
        jnp.einsum("bhtnu,bnuhd->bthd", weights, value_stack, preferred_element_type=jnp.float32)
    )
    grad_probs = jnp.einsum(
        "bthd,bnuhd->bhtnu", grad_stack, value_stack, preferred_element_type=jnp.float32
    )
    delta_rows = jnp.sum(grad_stack.astype(jnp.float32) * output.astype(jnp.float32), axis=-1)
    delta_rows = jnp.transpose(delta_rows, (0, 2, 1))[:, :, :, None, None]
    grad_scores = rounded(weights32 * (grad_probs - delta_rows) * scale_factor)
    query_grad = jnp.einsum(
        "bhtnu,bnuhd->bthd", grad_scores, key_stack, preferred_element_type=jnp.float32
    )
    key_terms = jnp.einsum(
        "bhtnu,bthd->bnuhd", grad_scores, query_stack, preferred_element_type=jnp.float32
    )
    value_terms = jnp.einsum(
        "bhtnu,bthd->bnuhd", weights, grad_stack, preferred_element_type=jnp.float32
    )
    own = (rounded(key_terms[0, 0]), rounded(value_terms[0, 0]))
    outgoing = [
        jnp.stack([key_terms[0, slot_index], value_terms[0, slot_index]]).astype(jnp.bfloat16)
        for slot_index in range(1, len(offsets) + 1)
    ]
    return output, query_grad, own, outgoing


def gather_back(own, outgoing, offsets):
    key_accum = own[0].astype(jnp.float32)
    value_accum = own[1].astype(jnp.float32)
    for parts, offset in zip(outgoing, offsets):
        returned = from_behind(parts, "ctx", -offset)
        key_accum = key_accum + returned[0].astype(jnp.float32)
        value_accum = value_accum + returned[1].astype(jnp.float32)
    return key_accum, value_accum


def on_device(queries, key_vectors, values, grad_out, file_lengths, reach_table):
    local_rows = queries.shape[0]
    width_all = queries.shape[1]
    per_shard = local_rows // BLOCK
    ctx_size = lax.axis_size("ctx")
    levels = (per_shard * ctx_size - 1).bit_length()
    offsets = [2**level_index for level_index in range(levels)]
    shard_index = lax.axis_index("ctx")
    global_rows = shard_index * local_rows + jnp.arange(local_rows, dtype=jnp.int32)
    positions = file_positions(file_lengths, global_rows)
    query_rot = rounded(rotary(queries, positions, HEADS, HEAD_DIM, False))
    key_rot = rounded(rotary(key_vectors, positions, HEADS, HEAD_DIM, False))
    valid_slots = reach_mask(reach_table, shard_index * per_shard, per_shard, levels)
    allowed = score_mask(valid_slots, BLOCK)
    chunk_heads = HEADS // CHUNKS
    chunk_width = chunk_heads * HEAD_DIM
    columns = [slice(chunk * chunk_width, (chunk + 1) * chunk_width) for chunk in range(CHUNKS)]
    pieces = []
    pending = []
    for chunk, cols in enumerate(columns):
        key_c, value_c = key_rot[:, cols], values[:, cols]
        if pending:
            key_c, value_c, _ = lax.optimization_barrier((key_c, value_c, pending[-1]))
        received = send_chunk(key_c, value_c, offsets)
        output, query_grad, own, outgoing = attend_chunk(
            query_rot[:, cols], received, grad_out[:, cols], allowed, offsets, chunk_heads
        )
        pending.append(outgoing)
        key_accum_c, value_accum_c = gather_back(own, outgoing, offsets)
        rows = query_rot.shape[0]
        pieces.append(
            (
                output.reshape(rows, chunk_width),
                query_grad.reshape(rows, chunk_width),
                key_accum_c.reshape(rows, chunk_width),
                value_accum_c.reshape(rows, chunk_width),
            )
        )
    attended, query_grad, key_accum, value_accum = [
        jnp.concatenate(parts, axis=1) for parts in zip(*pieces)
    ]
    grad_queries = rotary(query_grad, positions, HEADS, HEAD_DIM, True).astype(jnp.bfloat16)
    grad_keys = rotary(key_accum, positions, HEADS, HEAD_DIM, True).astype(jnp.bfloat16)
    grad_values = value_accum.astype(jnp.bfloat16)
    return (attended, grad_queries, grad_keys, grad_values)


def solution(mesh):
    placed = (
        P(("groups", "ctx"), None),
        P(("groups", "ctx"), None),
        P(("groups", "ctx"), None),
        P(("groups", "ctx"), None),
        P("groups"),
        P(("groups", "ctx")),
    )
    return jax.shard_map(
        on_device,
        mesh=mesh,
        in_specs=placed,
        out_specs=(
            P(("groups", "ctx"), None),
            P(("groups", "ctx"), None),
            P(("groups", "ctx"), None),
            P(("groups", "ctx"), None),
        ),
        check_vma=False,
    )
```

```python
import math

import jax
import jax.numpy as jnp
from jax import lax
from jax.sharding import PartitionSpec as P

HEADS = 16
HEAD_DIM = 128
BLOCK = 128
CHUNKS = 2


def from_behind(value, axis, steps):
    count = lax.axis_size(axis)
    leading, last = (max(0, -steps), min(count, count - steps))
    return lax.ppermute(value, axis, [(source, source + steps) for source in range(leading, last)])


def rounded(matrix):
    return lax.optimization_barrier(matrix.astype(jnp.bfloat16))


def file_positions(file_lengths, global_rows):
    file_ends = jnp.cumsum(file_lengths)
    starts = file_ends - file_lengths
    owned_mask = starts[None, :] <= global_rows[:, None]
    latest = jnp.max(jnp.where(owned_mask, starts[None, :], 0), axis=1)
    return global_rows - latest


def rotary(matrix, positions, head_count, head_width, inverse):
    half_width = head_width // 2
    exponent = jnp.arange(half_width, dtype=jnp.float32) * (2.0 / head_width)
    frequency = jnp.exp(exponent * -math.log(10000.0))
    angles = positions.astype(jnp.float32)[:, None] * frequency[None, :]
    cosine = jnp.cos(angles)[:, None, :]
    sine_table = jnp.sin(angles)[:, None, :]
    shaped = matrix.astype(jnp.float32).reshape(matrix.shape[0], head_count, head_width)
    former = shaped[..., :half_width]
    latter = shaped[..., half_width:]
    if inverse:
        turned = jnp.concatenate(
            [former * cosine + latter * sine_table, latter * cosine - former * sine_table], axis=-1
        )
    else:
        turned = jnp.concatenate(
            [former * cosine - latter * sine_table, latter * cosine + former * sine_table], axis=-1
        )
    return turned.reshape(matrix.shape[0], head_count * head_width)


def reach_mask(reach_rows, first_block, per_shard, levels):
    block_ids = first_block + jnp.arange(per_shard, dtype=jnp.int32)
    level_ids = jnp.arange(levels, dtype=jnp.int32)
    distances = jnp.array([2**level_index for level_index in range(levels)], dtype=jnp.int32)
    reached = (level_ids[None, :] < reach_rows[:, None]) & (
        block_ids[:, None] - distances[None, :] >= 0
    )
    return jnp.concatenate([jnp.ones((per_shard, 1), dtype=bool), reached], axis=1)


def score_mask(valid_slots, block_rows):
    row_ids = jnp.arange(block_rows)
    causal = row_ids[None, :] <= row_ids[:, None]
    first_slot = jnp.arange(valid_slots.shape[1]) == 0
    inside = jnp.where(first_slot[:, None, None], causal[None], True)
    allowed = inside[None] & valid_slots[:, :, None, None]
    return jnp.transpose(allowed, (0, 2, 1, 3))[:, None]


def send_chunk(key_c, value_c, offsets):
    pair = jnp.stack([key_c, value_c])
    received = {0: pair}
    for offset in offsets:
        if (offset.bit_length() - 1) % 2 == 1:
            half = offset // 2
            received[offset] = from_behind(received[half], "ctx", half)
        else:
            received[offset] = from_behind(pair, "ctx", offset)
    return [received[0]] + [received[offset] for offset in offsets]


def attend_chunk(query_c, received, grad_c, allowed, offsets, heads):
    scale_factor = 1.0 / math.sqrt(HEAD_DIM)
    rows = query_c.shape[0]
    head_shape = (rows, heads, HEAD_DIM)
    key_stack = jnp.stack([moved[0].reshape(head_shape) for moved in received])[None]
    value_stack = jnp.stack([moved[1].reshape(head_shape) for moved in received])[None]
    query_stack = query_c.reshape((1,) + head_shape)
    grad_stack = grad_c.reshape((1,) + head_shape)
    raw_scores = (
        jnp.einsum("bthd,bnuhd->bhtnu", query_stack, key_stack, preferred_element_type=jnp.float32)
        * scale_factor
    )
    scores = jnp.where(allowed, raw_scores, -1e30)
    row_peak = jnp.max(scores, axis=(3, 4), keepdims=True)
    summed = jnp.sum(jnp.exp(scores - row_peak), axis=(3, 4), keepdims=True)
    log_total = row_peak + jnp.log(summed)
    weights32 = jnp.exp(scores - log_total)
    weights = rounded(weights32)
    output = rounded(
        jnp.einsum("bhtnu,bnuhd->bthd", weights, value_stack, preferred_element_type=jnp.float32)
    )
    grad_probs = jnp.einsum(
        "bthd,bnuhd->bhtnu", grad_stack, value_stack, preferred_element_type=jnp.float32
    )
    delta_rows = jnp.sum(grad_stack.astype(jnp.float32) * output.astype(jnp.float32), axis=-1)
    delta_rows = jnp.transpose(delta_rows, (0, 2, 1))[:, :, :, None, None]
    grad_scores = rounded(weights32 * (grad_probs - delta_rows) * scale_factor)
    query_grad = jnp.einsum(
        "bhtnu,bnuhd->bthd", grad_scores, key_stack, preferred_element_type=jnp.float32
    )
    key_terms = jnp.einsum(
        "bhtnu,bthd->bnuhd", grad_scores, query_stack, preferred_element_type=jnp.float32
    )
    value_terms = jnp.einsum(
        "bhtnu,bthd->bnuhd", weights, grad_stack, preferred_element_type=jnp.float32
    )
    own = (rounded(key_terms[0, 0]), rounded(value_terms[0, 0]))
    outgoing = [
        jnp.stack([key_terms[0, slot_index], value_terms[0, slot_index]]).astype(jnp.bfloat16)
        for slot_index in range(1, len(offsets) + 1)
    ]
    return output, query_grad, own, outgoing


def gather_back(own, outgoing, offsets):
    key_accum = own[0].astype(jnp.float32)
    value_accum = own[1].astype(jnp.float32)
    for parts, offset in zip(outgoing, offsets):
        returned = from_behind(parts, "ctx", -offset)
        key_accum = key_accum + returned[0].astype(jnp.float32)
        value_accum = value_accum + returned[1].astype(jnp.float32)
    return key_accum, value_accum


def on_device(queries, key_vectors, values, grad_out, file_lengths, reach_table):
    local_rows = queries.shape[0]
    width_all = queries.shape[1]
    per_shard = local_rows // BLOCK
    ctx_size = lax.axis_size("ctx")
    levels = (per_shard * ctx_size - 1).bit_length()
    offsets = [2**level_index for level_index in range(levels)]
    shard_index = lax.axis_index("ctx")
    global_rows = shard_index * local_rows + jnp.arange(local_rows, dtype=jnp.int32)
    positions = file_positions(file_lengths, global_rows)
    query_rot = rounded(rotary(queries, positions, HEADS, HEAD_DIM, False))
    key_rot = rounded(rotary(key_vectors, positions, HEADS, HEAD_DIM, False))
    valid_slots = reach_mask(reach_table, shard_index * per_shard, per_shard, levels)
    allowed = score_mask(valid_slots, BLOCK)
    chunk_heads = HEADS // CHUNKS
    chunk_width = chunk_heads * HEAD_DIM
    columns = [slice(chunk * chunk_width, (chunk + 1) * chunk_width) for chunk in range(CHUNKS)]
    pieces = []
    pending = []
    for chunk, cols in enumerate(columns):
        key_c, value_c = key_rot[:, cols], values[:, cols]
        if pending:
            key_c, value_c, _ = lax.optimization_barrier((key_c, value_c, pieces[-1][0]))
        received = send_chunk(key_c, value_c, offsets)
        output, query_grad, own, outgoing = attend_chunk(
            query_rot[:, cols], received, grad_out[:, cols], allowed, offsets, chunk_heads
        )
        pending.append(outgoing)
        key_accum_c, value_accum_c = gather_back(own, outgoing, offsets)
        rows = query_rot.shape[0]
        pieces.append(
            (
                output.reshape(rows, chunk_width),
                query_grad.reshape(rows, chunk_width),
                key_accum_c.reshape(rows, chunk_width),
                value_accum_c.reshape(rows, chunk_width),
            )
        )
    attended, query_grad, key_accum, value_accum = [
        jnp.concatenate(parts, axis=1) for parts in zip(*pieces)
    ]
    grad_queries = rotary(query_grad, positions, HEADS, HEAD_DIM, True).astype(jnp.bfloat16)
    grad_keys = rotary(key_accum, positions, HEADS, HEAD_DIM, True).astype(jnp.bfloat16)
    grad_values = value_accum.astype(jnp.bfloat16)
    return (attended, grad_queries, grad_keys, grad_values)


def solution(mesh):
    placed = (
        P(("groups", "ctx"), None),
        P(("groups", "ctx"), None),
        P(("groups", "ctx"), None),
        P(("groups", "ctx"), None),
        P("groups"),
        P(("groups", "ctx")),
    )
    return jax.shard_map(
        on_device,
        mesh=mesh,
        in_specs=placed,
        out_specs=(
            P(("groups", "ctx"), None),
            P(("groups", "ctx"), None),
            P(("groups", "ctx"), None),
            P(("groups", "ctx"), None),
        ),
        check_vma=False,
    )
```

```python
import math

import jax
import jax.numpy as jnp
from jax import lax
from jax.sharding import PartitionSpec as P

HEADS = 16
HEAD_DIM = 128
BLOCK = 128
CHUNKS = 4


def from_behind(value, axis, steps):
    count = lax.axis_size(axis)
    leading, last = (max(0, -steps), min(count, count - steps))
    return lax.ppermute(value, axis, [(source, source + steps) for source in range(leading, last)])


def rounded(matrix):
    return lax.optimization_barrier(matrix.astype(jnp.bfloat16))


def file_positions(file_lengths, global_rows):
    file_ends = jnp.cumsum(file_lengths)
    starts = file_ends - file_lengths
    owned_mask = starts[None, :] <= global_rows[:, None]
    latest = jnp.max(jnp.where(owned_mask, starts[None, :], 0), axis=1)
    return global_rows - latest


def rotary(matrix, positions, head_count, head_width, inverse):
    half_width = head_width // 2
    exponent = jnp.arange(half_width, dtype=jnp.float32) * (2.0 / head_width)
    frequency = jnp.exp(exponent * -math.log(10000.0))
    angles = positions.astype(jnp.float32)[:, None] * frequency[None, :]
    cosine = jnp.cos(angles)[:, None, :]
    sine_table = jnp.sin(angles)[:, None, :]
    shaped = matrix.astype(jnp.float32).reshape(matrix.shape[0], head_count, head_width)
    former = shaped[..., :half_width]
    latter = shaped[..., half_width:]
    if inverse:
        turned = jnp.concatenate(
            [former * cosine + latter * sine_table, latter * cosine - former * sine_table], axis=-1
        )
    else:
        turned = jnp.concatenate(
            [former * cosine - latter * sine_table, latter * cosine + former * sine_table], axis=-1
        )
    return turned.reshape(matrix.shape[0], head_count * head_width)


def reach_mask(reach_rows, first_block, per_shard, levels):
    block_ids = first_block + jnp.arange(per_shard, dtype=jnp.int32)
    level_ids = jnp.arange(levels, dtype=jnp.int32)
    distances = jnp.array([2**level_index for level_index in range(levels)], dtype=jnp.int32)
    reached = (level_ids[None, :] < reach_rows[:, None]) & (
        block_ids[:, None] - distances[None, :] >= 0
    )
    return jnp.concatenate([jnp.ones((per_shard, 1), dtype=bool), reached], axis=1)


def score_mask(valid_slots, block_rows):
    row_ids = jnp.arange(block_rows)
    causal = row_ids[None, :] <= row_ids[:, None]
    first_slot = jnp.arange(valid_slots.shape[1]) == 0
    inside = jnp.where(first_slot[:, None, None], causal[None], True)
    allowed = inside[None] & valid_slots[:, :, None, None]
    return jnp.transpose(allowed, (0, 2, 1, 3))[:, None]


def send_chunk(key_c, value_c, offsets):
    pair = jnp.stack([key_c, value_c])
    received = {0: pair}
    for offset in offsets:
        if (offset.bit_length() - 1) % 2 == 1:
            half = offset // 2
            received[offset] = from_behind(received[half], "ctx", half)
        else:
            received[offset] = from_behind(pair, "ctx", offset)
    return [received[0]] + [received[offset] for offset in offsets]


def attend_chunk(query_c, received, grad_c, allowed, offsets, heads):
    scale_factor = 1.0 / math.sqrt(HEAD_DIM)
    rows = query_c.shape[0]
    head_shape = (rows, heads, HEAD_DIM)
    key_stack = jnp.stack([moved[0].reshape(head_shape) for moved in received])[None]
    value_stack = jnp.stack([moved[1].reshape(head_shape) for moved in received])[None]
    query_stack = query_c.reshape((1,) + head_shape)
    grad_stack = grad_c.reshape((1,) + head_shape)
    raw_scores = (
        jnp.einsum("bthd,bnuhd->bhtnu", query_stack, key_stack, preferred_element_type=jnp.float32)
        * scale_factor
    )
    scores = jnp.where(allowed, raw_scores, -1e30)
    row_peak = jnp.max(scores, axis=(3, 4), keepdims=True)
    summed = jnp.sum(jnp.exp(scores - row_peak), axis=(3, 4), keepdims=True)
    log_total = row_peak + jnp.log(summed)
    weights32 = jnp.exp(scores - log_total)
    weights = rounded(weights32)
    output = rounded(
        jnp.einsum("bhtnu,bnuhd->bthd", weights, value_stack, preferred_element_type=jnp.float32)
    )
    grad_probs = jnp.einsum(
        "bthd,bnuhd->bhtnu", grad_stack, value_stack, preferred_element_type=jnp.float32
    )
    delta_rows = jnp.sum(grad_stack.astype(jnp.float32) * output.astype(jnp.float32), axis=-1)
    delta_rows = jnp.transpose(delta_rows, (0, 2, 1))[:, :, :, None, None]
    grad_scores = rounded(weights32 * (grad_probs - delta_rows) * scale_factor)
    query_grad = jnp.einsum(
        "bhtnu,bnuhd->bthd", grad_scores, key_stack, preferred_element_type=jnp.float32
    )
    key_terms = jnp.einsum(
        "bhtnu,bthd->bnuhd", grad_scores, query_stack, preferred_element_type=jnp.float32
    )
    value_terms = jnp.einsum(
        "bhtnu,bthd->bnuhd", weights, grad_stack, preferred_element_type=jnp.float32
    )
    own = (rounded(key_terms[0, 0]), rounded(value_terms[0, 0]))
    outgoing = [
        jnp.stack([key_terms[0, slot_index], value_terms[0, slot_index]]).astype(jnp.bfloat16)
        for slot_index in range(1, len(offsets) + 1)
    ]
    return output, query_grad, own, outgoing


def gather_back(own, outgoing, offsets):
    key_accum = own[0].astype(jnp.float32)
    value_accum = own[1].astype(jnp.float32)
    for parts, offset in zip(outgoing, offsets):
        returned = from_behind(parts, "ctx", -offset)
        key_accum = key_accum + returned[0].astype(jnp.float32)
        value_accum = value_accum + returned[1].astype(jnp.float32)
    return key_accum, value_accum


def on_device(queries, key_vectors, values, grad_out, file_lengths, reach_table):
    local_rows = queries.shape[0]
    width_all = queries.shape[1]
    per_shard = local_rows // BLOCK
    ctx_size = lax.axis_size("ctx")
    levels = (per_shard * ctx_size - 1).bit_length()
    offsets = [2**level_index for level_index in range(levels)]
    shard_index = lax.axis_index("ctx")
    global_rows = shard_index * local_rows + jnp.arange(local_rows, dtype=jnp.int32)
    positions = file_positions(file_lengths, global_rows)
    query_rot = rounded(rotary(queries, positions, HEADS, HEAD_DIM, False))
    key_rot = rounded(rotary(key_vectors, positions, HEADS, HEAD_DIM, False))
    valid_slots = reach_mask(reach_table, shard_index * per_shard, per_shard, levels)
    allowed = score_mask(valid_slots, BLOCK)
    chunk_heads = HEADS // CHUNKS
    chunk_width = chunk_heads * HEAD_DIM
    columns = [slice(chunk * chunk_width, (chunk + 1) * chunk_width) for chunk in range(CHUNKS)]
    pieces = []
    pending = []
    for chunk, cols in enumerate(columns):
        key_c, value_c = key_rot[:, cols], values[:, cols]
        if pending:
            key_c, value_c, _ = lax.optimization_barrier((key_c, value_c, pieces[-1][0]))
        received = send_chunk(key_c, value_c, offsets)
        output, query_grad, own, outgoing = attend_chunk(
            query_rot[:, cols], received, grad_out[:, cols], allowed, offsets, chunk_heads
        )
        pending.append(outgoing)
        key_accum_c, value_accum_c = gather_back(own, outgoing, offsets)
        rows = query_rot.shape[0]
        pieces.append(
            (
                output.reshape(rows, chunk_width),
                query_grad.reshape(rows, chunk_width),
                key_accum_c.reshape(rows, chunk_width),
                value_accum_c.reshape(rows, chunk_width),
            )
        )
    attended, query_grad, key_accum, value_accum = [
        jnp.concatenate(parts, axis=1) for parts in zip(*pieces)
    ]
    grad_queries = rotary(query_grad, positions, HEADS, HEAD_DIM, True).astype(jnp.bfloat16)
    grad_keys = rotary(key_accum, positions, HEADS, HEAD_DIM, True).astype(jnp.bfloat16)
    grad_values = value_accum.astype(jnp.bfloat16)
    return (attended, grad_queries, grad_keys, grad_values)


def solution(mesh):
    placed = (
        P(("groups", "ctx"), None),
        P(("groups", "ctx"), None),
        P(("groups", "ctx"), None),
        P(("groups", "ctx"), None),
        P("groups"),
        P(("groups", "ctx")),
    )
    return jax.shard_map(
        on_device,
        mesh=mesh,
        in_specs=placed,
        out_specs=(
            P(("groups", "ctx"), None),
            P(("groups", "ctx"), None),
            P(("groups", "ctx"), None),
            P(("groups", "ctx"), None),
        ),
        check_vma=False,
    )
```

```python
import math

import jax
import jax.numpy as jnp
from jax import lax
from jax.experimental import pallas as pl
from jax.sharding import PartitionSpec as P

HEADS = 16
HEAD_DIM = 128
BLOCK = 128
CHUNKS = 2


def from_behind(value, axis, steps):
    count = lax.axis_size(axis)
    leading, last = (max(0, -steps), min(count, count - steps))
    return lax.ppermute(value, axis, [(source, source + steps) for source in range(leading, last)])


def rounded(matrix):
    return lax.optimization_barrier(matrix.astype(jnp.bfloat16))


def file_positions(file_lengths, global_rows):
    file_ends = jnp.cumsum(file_lengths)
    starts = file_ends - file_lengths
    owned_mask = starts[None, :] <= global_rows[:, None]
    latest = jnp.max(jnp.where(owned_mask, starts[None, :], 0), axis=1)
    return global_rows - latest


def rotary(matrix, positions, head_count, head_width, inverse):
    half_width = head_width // 2
    exponent = jnp.arange(half_width, dtype=jnp.float32) * (2.0 / head_width)
    frequency = jnp.exp(exponent * -math.log(10000.0))
    angles = positions.astype(jnp.float32)[:, None] * frequency[None, :]
    cosine = jnp.cos(angles)[:, None, :]
    sine_table = jnp.sin(angles)[:, None, :]
    shaped = matrix.astype(jnp.float32).reshape(matrix.shape[0], head_count, head_width)
    former = shaped[..., :half_width]
    latter = shaped[..., half_width:]
    if inverse:
        turned = jnp.concatenate(
            [former * cosine + latter * sine_table, latter * cosine - former * sine_table], axis=-1
        )
    else:
        turned = jnp.concatenate(
            [former * cosine - latter * sine_table, latter * cosine + former * sine_table], axis=-1
        )
    return turned.reshape(matrix.shape[0], head_count * head_width)


def reach_mask(reach_rows, first_block, per_shard, levels):
    block_ids = first_block + jnp.arange(per_shard, dtype=jnp.int32)
    level_ids = jnp.arange(levels, dtype=jnp.int32)
    distances = jnp.array([2**level_index for level_index in range(levels)], dtype=jnp.int32)
    reached = (level_ids[None, :] < reach_rows[:, None]) & (
        block_ids[:, None] - distances[None, :] >= 0
    )
    return jnp.concatenate([jnp.ones((per_shard, 1), dtype=bool), reached], axis=1)


def score_mask(valid_slots, block_rows):
    row_ids = jnp.arange(block_rows)
    causal = row_ids[None, :] <= row_ids[:, None]
    first_slot = jnp.arange(valid_slots.shape[1]) == 0
    inside = jnp.where(first_slot[:, None, None], causal[None], True)
    allowed = inside[None] & valid_slots[:, :, None, None]
    return jnp.transpose(allowed, (0, 2, 1, 3))[:, None]


def send_chunk(key_c, value_c, offsets):
    pair = jnp.stack([key_c, value_c])
    received = {0: pair}
    for offset in offsets:
        if (offset.bit_length() - 1) % 2 == 1:
            half = offset // 2
            received[offset] = from_behind(received[half], "ctx", half)
        else:
            received[offset] = from_behind(pair, "ctx", offset)
    return [received[0]] + [received[offset] for offset in offsets]


def attention_kernel(*refs):
    slots = (len(refs) - 5) // 2
    query_ref, grad_ref, mask_ref = refs[0], refs[1], refs[2]
    pair_refs = refs[3 : 3 + slots]
    out_ref, qgrad_ref = refs[3 + slots], refs[4 + slots]
    part_refs = refs[5 + slots :]
    scale_factor = 1.0 / math.sqrt(HEAD_DIM)
    query = query_ref[...]
    grad = grad_ref[...]
    keys = jnp.concatenate([ref[0] for ref in pair_refs], axis=0)
    vals = jnp.concatenate([ref[1] for ref in pair_refs], axis=0)
    last = (((1,), (1,)), ((), ()))
    first = (((0,), (0,)), ((), ()))
    raw = lax.dot_general(query, keys, last, preferred_element_type=jnp.float32)
    scores = jnp.where(mask_ref[...] > 0, raw * scale_factor, -1e30)
    row_peak = jnp.max(scores, axis=1, keepdims=True)
    summed = jnp.sum(jnp.exp(scores - row_peak), axis=1, keepdims=True)
    log_total = row_peak + jnp.log(summed)
    weights32 = jnp.exp(scores - log_total)
    weights = weights32.astype(jnp.bfloat16)
    output = jnp.dot(weights, vals, preferred_element_type=jnp.float32).astype(jnp.bfloat16)
    out_ref[...] = output
    grad_probs = lax.dot_general(grad, vals, last, preferred_element_type=jnp.float32)
    delta = jnp.sum(grad.astype(jnp.float32) * output.astype(jnp.float32), axis=1, keepdims=True)
    grad_scores = (weights32 * (grad_probs - delta) * scale_factor).astype(jnp.bfloat16)
    qgrad_ref[...] = jnp.dot(grad_scores, keys, preferred_element_type=jnp.float32)
    key_terms = lax.dot_general(grad_scores, query, first, preferred_element_type=jnp.float32)
    value_terms = lax.dot_general(weights, grad, first, preferred_element_type=jnp.float32)
    rows = query.shape[0]
    for slot, ref in enumerate(part_refs):
        ref[0] = key_terms[slot * rows : (slot + 1) * rows].astype(jnp.bfloat16)
        ref[1] = value_terms[slot * rows : (slot + 1) * rows].astype(jnp.bfloat16)


def attend_chunk(query_c, received, grad_c, allowed, offsets, heads):
    rows, width = query_c.shape
    slots = len(received)
    mask = jnp.where(allowed, 1.0, 0.0).astype(jnp.float32).reshape(rows, slots * rows)
    flat_spec = pl.BlockSpec((rows, HEAD_DIM), lambda h: (0, h))
    pair_spec = pl.BlockSpec((2, rows, HEAD_DIM), lambda h: (0, 0, h))
    mask_spec = pl.BlockSpec((rows, slots * rows), lambda h: (0, 0))
    pair_shape = jax.ShapeDtypeStruct((2, rows, width), jnp.bfloat16)
    results = pl.pallas_call(
        attention_kernel,
        grid=(heads,),
        in_specs=[flat_spec, flat_spec, mask_spec] + [pair_spec] * slots,
        out_specs=[flat_spec, flat_spec] + [pair_spec] * slots,
        out_shape=[
            jax.ShapeDtypeStruct((rows, width), jnp.bfloat16),
            jax.ShapeDtypeStruct((rows, width), jnp.float32),
        ]
        + [pair_shape] * slots,
    )(query_c, grad_c, mask, *received)
    output, query_grad = results[0], results[1]
    own = (results[2][0], results[2][1])
    outgoing = list(results[3:])
    return output, query_grad, own, outgoing


def gather_back(own, outgoing, offsets):
    key_accum = own[0].astype(jnp.float32)
    value_accum = own[1].astype(jnp.float32)
    for parts, offset in zip(outgoing, offsets):
        returned = from_behind(parts, "ctx", -offset)
        key_accum = key_accum + returned[0].astype(jnp.float32)
        value_accum = value_accum + returned[1].astype(jnp.float32)
    return key_accum, value_accum


def on_device(queries, key_vectors, values, grad_out, file_lengths, reach_table):
    local_rows = queries.shape[0]
    width_all = queries.shape[1]
    per_shard = local_rows // BLOCK
    ctx_size = lax.axis_size("ctx")
    levels = (per_shard * ctx_size - 1).bit_length()
    offsets = [2**level_index for level_index in range(levels)]
    shard_index = lax.axis_index("ctx")
    global_rows = shard_index * local_rows + jnp.arange(local_rows, dtype=jnp.int32)
    positions = file_positions(file_lengths, global_rows)
    query_rot = rounded(rotary(queries, positions, HEADS, HEAD_DIM, False))
    key_rot = rounded(rotary(key_vectors, positions, HEADS, HEAD_DIM, False))
    valid_slots = reach_mask(reach_table, shard_index * per_shard, per_shard, levels)
    allowed = score_mask(valid_slots, BLOCK)
    chunk_heads = HEADS // CHUNKS
    chunk_width = chunk_heads * HEAD_DIM
    columns = [slice(chunk * chunk_width, (chunk + 1) * chunk_width) for chunk in range(CHUNKS)]
    pieces = []
    pending = []
    for chunk, cols in enumerate(columns):
        key_c, value_c = key_rot[:, cols], values[:, cols]
        if pending:
            key_c, value_c, _ = lax.optimization_barrier((key_c, value_c, pieces[-1][0]))
        received = send_chunk(key_c, value_c, offsets)
        output, query_grad, own, outgoing = attend_chunk(
            query_rot[:, cols], received, grad_out[:, cols], allowed, offsets, chunk_heads
        )
        pending.append(outgoing)
        key_accum_c, value_accum_c = gather_back(own, outgoing, offsets)
        rows = query_rot.shape[0]
        pieces.append(
            (
                output.reshape(rows, chunk_width),
                query_grad.reshape(rows, chunk_width),
                key_accum_c.reshape(rows, chunk_width),
                value_accum_c.reshape(rows, chunk_width),
            )
        )
    attended, query_grad, key_accum, value_accum = [
        jnp.concatenate(parts, axis=1) for parts in zip(*pieces)
    ]
    grad_queries = rotary(query_grad, positions, HEADS, HEAD_DIM, True).astype(jnp.bfloat16)
    grad_keys = rotary(key_accum, positions, HEADS, HEAD_DIM, True).astype(jnp.bfloat16)
    grad_values = value_accum.astype(jnp.bfloat16)
    return (attended, grad_queries, grad_keys, grad_values)


def solution(mesh):
    placed = (
        P(("groups", "ctx"), None),
        P(("groups", "ctx"), None),
        P(("groups", "ctx"), None),
        P(("groups", "ctx"), None),
        P("groups"),
        P(("groups", "ctx")),
    )
    return jax.shard_map(
        on_device,
        mesh=mesh,
        in_specs=placed,
        out_specs=(
            P(("groups", "ctx"), None),
            P(("groups", "ctx"), None),
            P(("groups", "ctx"), None),
            P(("groups", "ctx"), None),
        ),
        check_vma=False,
    )
```

```python
import math

import jax
import jax.numpy as jnp
from jax import lax
from jax.experimental import pallas as pl
from jax.sharding import PartitionSpec as P

HEADS = 16
HEAD_DIM = 128
BLOCK = 128
CHUNK_HEADS = (4, 6, 6)


def from_behind(value, axis, steps):
    count = lax.axis_size(axis)
    leading, last = (max(0, -steps), min(count, count - steps))
    return lax.ppermute(value, axis, [(source, source + steps) for source in range(leading, last)])


def rounded(matrix):
    return lax.optimization_barrier(matrix.astype(jnp.bfloat16))


def file_positions(file_lengths, global_rows):
    file_ends = jnp.cumsum(file_lengths)
    starts = file_ends - file_lengths
    owned_mask = starts[None, :] <= global_rows[:, None]
    latest = jnp.max(jnp.where(owned_mask, starts[None, :], 0), axis=1)
    return global_rows - latest


def rotary(matrix, positions, head_count, head_width, inverse):
    half_width = head_width // 2
    exponent = jnp.arange(half_width, dtype=jnp.float32) * (2.0 / head_width)
    frequency = jnp.exp(exponent * -math.log(10000.0))
    angles = positions.astype(jnp.float32)[:, None] * frequency[None, :]
    cosine = jnp.cos(angles)[:, None, :]
    sine_table = jnp.sin(angles)[:, None, :]
    shaped = matrix.astype(jnp.float32).reshape(matrix.shape[0], head_count, head_width)
    former = shaped[..., :half_width]
    latter = shaped[..., half_width:]
    if inverse:
        turned = jnp.concatenate(
            [former * cosine + latter * sine_table, latter * cosine - former * sine_table], axis=-1
        )
    else:
        turned = jnp.concatenate(
            [former * cosine - latter * sine_table, latter * cosine + former * sine_table], axis=-1
        )
    return turned.reshape(matrix.shape[0], head_count * head_width)


def reach_mask(reach_rows, first_block, per_shard, levels):
    block_ids = first_block + jnp.arange(per_shard, dtype=jnp.int32)
    level_ids = jnp.arange(levels, dtype=jnp.int32)
    distances = jnp.array([2**level_index for level_index in range(levels)], dtype=jnp.int32)
    reached = (level_ids[None, :] < reach_rows[:, None]) & (
        block_ids[:, None] - distances[None, :] >= 0
    )
    return jnp.concatenate([jnp.ones((per_shard, 1), dtype=bool), reached], axis=1)


def score_mask(valid_slots, block_rows):
    row_ids = jnp.arange(block_rows)
    causal = row_ids[None, :] <= row_ids[:, None]
    first_slot = jnp.arange(valid_slots.shape[1]) == 0
    inside = jnp.where(first_slot[:, None, None], causal[None], True)
    allowed = inside[None] & valid_slots[:, :, None, None]
    return jnp.transpose(allowed, (0, 2, 1, 3))[:, None]


def send_chunk(key_c, value_c, offsets):
    pair = jnp.stack([key_c, value_c])
    received = {0: pair}
    for offset in offsets:
        if (offset.bit_length() - 1) % 2 == 1:
            half = offset // 2
            received[offset] = from_behind(received[half], "ctx", half)
        else:
            received[offset] = from_behind(pair, "ctx", offset)
    return [received[0]] + [received[offset] for offset in offsets]


def attention_kernel(*refs):
    slots = (len(refs) - 5) // 2
    query_ref, grad_ref, mask_ref = refs[0], refs[1], refs[2]
    pair_refs = refs[3 : 3 + slots]
    out_ref, qgrad_ref = refs[3 + slots], refs[4 + slots]
    part_refs = refs[5 + slots :]
    scale_factor = 1.0 / math.sqrt(HEAD_DIM)
    query = query_ref[...]
    grad = grad_ref[...]
    keys = jnp.concatenate([ref[0] for ref in pair_refs], axis=0)
    vals = jnp.concatenate([ref[1] for ref in pair_refs], axis=0)
    last = (((1,), (1,)), ((), ()))
    first = (((0,), (0,)), ((), ()))
    raw = lax.dot_general(query, keys, last, preferred_element_type=jnp.float32)
    scores = jnp.where(mask_ref[...] > 0, raw * scale_factor, -1e30)
    row_peak = jnp.max(scores, axis=1, keepdims=True)
    summed = jnp.sum(jnp.exp(scores - row_peak), axis=1, keepdims=True)
    log_total = row_peak + jnp.log(summed)
    weights32 = jnp.exp(scores - log_total)
    weights = weights32.astype(jnp.bfloat16)
    output = jnp.dot(weights, vals, preferred_element_type=jnp.float32).astype(jnp.bfloat16)
    out_ref[...] = output
    grad_probs = lax.dot_general(grad, vals, last, preferred_element_type=jnp.float32)
    delta = jnp.sum(grad.astype(jnp.float32) * output.astype(jnp.float32), axis=1, keepdims=True)
    grad_scores = (weights32 * (grad_probs - delta) * scale_factor).astype(jnp.bfloat16)
    qgrad_ref[...] = jnp.dot(grad_scores, keys, preferred_element_type=jnp.float32)
    key_terms = lax.dot_general(grad_scores, query, first, preferred_element_type=jnp.float32)
    value_terms = lax.dot_general(weights, grad, first, preferred_element_type=jnp.float32)
    rows = query.shape[0]
    for slot, ref in enumerate(part_refs):
        ref[0] = key_terms[slot * rows : (slot + 1) * rows].astype(jnp.bfloat16)
        ref[1] = value_terms[slot * rows : (slot + 1) * rows].astype(jnp.bfloat16)


def attend_chunk(query_c, received, grad_c, allowed, offsets, heads):
    rows, width = query_c.shape
    slots = len(received)
    mask = jnp.where(allowed, 1.0, 0.0).astype(jnp.float32).reshape(rows, slots * rows)
    flat_spec = pl.BlockSpec((rows, HEAD_DIM), lambda h: (0, h))
    pair_spec = pl.BlockSpec((2, rows, HEAD_DIM), lambda h: (0, 0, h))
    mask_spec = pl.BlockSpec((rows, slots * rows), lambda h: (0, 0))
    pair_shape = jax.ShapeDtypeStruct((2, rows, width), jnp.bfloat16)
    results = pl.pallas_call(
        attention_kernel,
        grid=(heads,),
        in_specs=[flat_spec, flat_spec, mask_spec] + [pair_spec] * slots,
        out_specs=[flat_spec, flat_spec] + [pair_spec] * slots,
        out_shape=[
            jax.ShapeDtypeStruct((rows, width), jnp.bfloat16),
            jax.ShapeDtypeStruct((rows, width), jnp.float32),
        ]
        + [pair_shape] * slots,
    )(query_c, grad_c, mask, *received)
    output, query_grad = results[0], results[1]
    own = (results[2][0], results[2][1])
    outgoing = list(results[3:])
    return output, query_grad, own, outgoing


def gather_back(own, outgoing, offsets):
    key_accum = own[0].astype(jnp.float32)
    value_accum = own[1].astype(jnp.float32)
    for parts, offset in zip(outgoing, offsets):
        returned = from_behind(parts, "ctx", -offset)
        key_accum = key_accum + returned[0].astype(jnp.float32)
        value_accum = value_accum + returned[1].astype(jnp.float32)
    return key_accum, value_accum


def on_device(queries, key_vectors, values, grad_out, file_lengths, reach_table):
    local_rows = queries.shape[0]
    width_all = queries.shape[1]
    per_shard = local_rows // BLOCK
    ctx_size = lax.axis_size("ctx")
    levels = (per_shard * ctx_size - 1).bit_length()
    offsets = [2**level_index for level_index in range(levels)]
    shard_index = lax.axis_index("ctx")
    global_rows = shard_index * local_rows + jnp.arange(local_rows, dtype=jnp.int32)
    positions = file_positions(file_lengths, global_rows)
    query_rot = rounded(rotary(queries, positions, HEADS, HEAD_DIM, False))
    key_rot = rounded(rotary(key_vectors, positions, HEADS, HEAD_DIM, False))
    valid_slots = reach_mask(reach_table, shard_index * per_shard, per_shard, levels)
    allowed = score_mask(valid_slots, BLOCK)
    bounds = [sum(CHUNK_HEADS[:chunk]) * HEAD_DIM for chunk in range(len(CHUNK_HEADS) + 1)]
    pieces = []
    pending = []
    for chunk, chunk_heads in enumerate(CHUNK_HEADS):
        chunk_width = chunk_heads * HEAD_DIM
        cols = slice(bounds[chunk], bounds[chunk + 1])
        key_c, value_c = key_rot[:, cols], values[:, cols]
        if pending:
            key_c, value_c, _ = lax.optimization_barrier((key_c, value_c, pieces[-1][0]))
        received = send_chunk(key_c, value_c, offsets)
        output, query_grad, own, outgoing = attend_chunk(
            query_rot[:, cols], received, grad_out[:, cols], allowed, offsets, chunk_heads
        )
        pending.append(outgoing)
        key_accum_c, value_accum_c = gather_back(own, outgoing, offsets)
        rows = query_rot.shape[0]
        pieces.append(
            (
                output.reshape(rows, chunk_width),
                query_grad.reshape(rows, chunk_width),
                key_accum_c.reshape(rows, chunk_width),
                value_accum_c.reshape(rows, chunk_width),
            )
        )
    attended, query_grad, key_accum, value_accum = [
        jnp.concatenate(parts, axis=1) for parts in zip(*pieces)
    ]
    grad_queries = rotary(query_grad, positions, HEADS, HEAD_DIM, True).astype(jnp.bfloat16)
    grad_keys = rotary(key_accum, positions, HEADS, HEAD_DIM, True).astype(jnp.bfloat16)
    grad_values = value_accum.astype(jnp.bfloat16)
    return (attended, grad_queries, grad_keys, grad_values)


def solution(mesh):
    placed = (
        P(("groups", "ctx"), None),
        P(("groups", "ctx"), None),
        P(("groups", "ctx"), None),
        P(("groups", "ctx"), None),
        P("groups"),
        P(("groups", "ctx")),
    )
    return jax.shard_map(
        on_device,
        mesh=mesh,
        in_specs=placed,
        out_specs=(
            P(("groups", "ctx"), None),
            P(("groups", "ctx"), None),
            P(("groups", "ctx"), None),
            P(("groups", "ctx"), None),
        ),
        check_vma=False,
    )
```

```python
import math

import jax
import jax.numpy as jnp
from jax import lax
from jax.experimental import pallas as pl
from jax.sharding import PartitionSpec as P

HEADS = 16
HEAD_DIM = 128
BLOCK = 128
CHUNKS = 2


def from_behind(value, axis, steps):
    count = lax.axis_size(axis)
    leading, last = (max(0, -steps), min(count, count - steps))
    return lax.ppermute(value, axis, [(source, source + steps) for source in range(leading, last)])


def rounded(matrix):
    return lax.optimization_barrier(matrix.astype(jnp.bfloat16))


def file_positions(file_lengths, global_rows):
    file_ends = jnp.cumsum(file_lengths)
    starts = file_ends - file_lengths
    owned_mask = starts[None, :] <= global_rows[:, None]
    latest = jnp.max(jnp.where(owned_mask, starts[None, :], 0), axis=1)
    return global_rows - latest


def rotary(matrix, positions, head_count, head_width, inverse):
    half_width = head_width // 2
    exponent = jnp.arange(half_width, dtype=jnp.float32) * (2.0 / head_width)
    frequency = jnp.exp(exponent * -math.log(10000.0))
    angles = positions.astype(jnp.float32)[:, None] * frequency[None, :]
    cosine = jnp.cos(angles)[:, None, :]
    sine_table = jnp.sin(angles)[:, None, :]
    shaped = matrix.astype(jnp.float32).reshape(matrix.shape[0], head_count, head_width)
    former = shaped[..., :half_width]
    latter = shaped[..., half_width:]
    if inverse:
        turned = jnp.concatenate(
            [former * cosine + latter * sine_table, latter * cosine - former * sine_table], axis=-1
        )
    else:
        turned = jnp.concatenate(
            [former * cosine - latter * sine_table, latter * cosine + former * sine_table], axis=-1
        )
    return turned.reshape(matrix.shape[0], head_count * head_width)


def reach_mask(reach_rows, first_block, per_shard, levels):
    block_ids = first_block + jnp.arange(per_shard, dtype=jnp.int32)
    level_ids = jnp.arange(levels, dtype=jnp.int32)
    distances = jnp.array([2**level_index for level_index in range(levels)], dtype=jnp.int32)
    reached = (level_ids[None, :] < reach_rows[:, None]) & (
        block_ids[:, None] - distances[None, :] >= 0
    )
    return jnp.concatenate([jnp.ones((per_shard, 1), dtype=bool), reached], axis=1)


def score_mask(valid_slots, block_rows):
    row_ids = jnp.arange(block_rows)
    causal = row_ids[None, :] <= row_ids[:, None]
    first_slot = jnp.arange(valid_slots.shape[1]) == 0
    inside = jnp.where(first_slot[:, None, None], causal[None], True)
    allowed = inside[None] & valid_slots[:, :, None, None]
    return jnp.transpose(allowed, (0, 2, 1, 3))[:, None]


def send_chunk(key_c, value_c, offsets):
    pair = jnp.stack([key_c, value_c])
    received = {0: pair}
    for offset in offsets:
        if (offset.bit_length() - 1) % 2 == 1:
            half = offset // 2
            received[offset] = from_behind(received[half], "ctx", half)
        else:
            received[offset] = from_behind(pair, "ctx", offset)
    return [received[0]] + [received[offset] for offset in offsets]


def attention_kernel(*refs):
    slots = (len(refs) - 5) // 2
    query_ref, grad_ref, mask_ref = refs[0], refs[1], refs[2]
    pair_refs = refs[3 : 3 + slots]
    out_ref, qgrad_ref = refs[3 + slots], refs[4 + slots]
    part_refs = refs[5 + slots :]
    scale_factor = 1.0 / math.sqrt(HEAD_DIM)
    query = query_ref[...]
    grad = grad_ref[...]
    keys = jnp.concatenate([ref[0] for ref in pair_refs], axis=0)
    vals = jnp.concatenate([ref[1] for ref in pair_refs], axis=0)
    last = (((1,), (1,)), ((), ()))
    first = (((0,), (0,)), ((), ()))
    raw = lax.dot_general(query, keys, last, preferred_element_type=jnp.float32)
    scores = jnp.where(mask_ref[...] > 0, raw * scale_factor, -1e30)
    row_peak = jnp.max(scores, axis=1, keepdims=True)
    summed = jnp.sum(jnp.exp(scores - row_peak), axis=1, keepdims=True)
    log_total = row_peak + jnp.log(summed)
    weights32 = jnp.exp(scores - log_total)
    weights = weights32.astype(jnp.bfloat16)
    output = jnp.dot(weights, vals, preferred_element_type=jnp.float32).astype(jnp.bfloat16)
    out_ref[...] = output
    grad_probs = lax.dot_general(grad, vals, last, preferred_element_type=jnp.float32)
    delta = jnp.sum(grad.astype(jnp.float32) * output.astype(jnp.float32), axis=1, keepdims=True)
    grad_scores = (weights32 * (grad_probs - delta) * scale_factor).astype(jnp.bfloat16)
    qgrad_ref[...] = jnp.dot(grad_scores, keys, preferred_element_type=jnp.float32)
    key_terms = lax.dot_general(grad_scores, query, first, preferred_element_type=jnp.float32)
    value_terms = lax.dot_general(weights, grad, first, preferred_element_type=jnp.float32)
    rows = query.shape[0]
    for slot, ref in enumerate(part_refs):
        ref[0] = key_terms[slot * rows : (slot + 1) * rows].astype(jnp.bfloat16)
        ref[1] = value_terms[slot * rows : (slot + 1) * rows].astype(jnp.bfloat16)


def attend_chunk(query_c, received, grad_c, allowed, offsets, heads):
    rows, width = query_c.shape
    slots = len(received)
    mask = jnp.where(allowed, 1.0, 0.0).astype(jnp.float32).reshape(rows, slots * rows)
    flat_spec = pl.BlockSpec((rows, HEAD_DIM), lambda h: (0, h))
    pair_spec = pl.BlockSpec((2, rows, HEAD_DIM), lambda h: (0, 0, h))
    mask_spec = pl.BlockSpec((rows, slots * rows), lambda h: (0, 0))
    pair_shape = jax.ShapeDtypeStruct((2, rows, width), jnp.bfloat16)
    results = pl.pallas_call(
        attention_kernel,
        grid=(heads,),
        in_specs=[flat_spec, flat_spec, mask_spec] + [pair_spec] * slots,
        out_specs=[flat_spec, flat_spec] + [pair_spec] * slots,
        out_shape=[
            jax.ShapeDtypeStruct((rows, width), jnp.bfloat16),
            jax.ShapeDtypeStruct((rows, width), jnp.float32),
        ]
        + [pair_shape] * slots,
    )(query_c, grad_c, mask, *received)
    output, query_grad = results[0], results[1]
    own = (results[2][0], results[2][1])
    outgoing = list(results[3:])
    return output, query_grad, own, outgoing


def gather_back(own, outgoing, offsets):
    key_accum = own[0].astype(jnp.float32)
    value_accum = own[1].astype(jnp.float32)
    for parts, offset in zip(outgoing, offsets):
        returned = from_behind(parts, "ctx", -offset)
        key_accum = key_accum + returned[0].astype(jnp.float32)
        value_accum = value_accum + returned[1].astype(jnp.float32)
    return key_accum, value_accum


def on_device(queries, key_vectors, values, grad_out, file_lengths, reach_table):
    local_rows = queries.shape[0]
    width_all = queries.shape[1]
    per_shard = local_rows // BLOCK
    ctx_size = lax.axis_size("ctx")
    levels = (per_shard * ctx_size - 1).bit_length()
    offsets = [2**level_index for level_index in range(levels)]
    shard_index = lax.axis_index("ctx")
    global_rows = shard_index * local_rows + jnp.arange(local_rows, dtype=jnp.int32)
    positions = file_positions(file_lengths, global_rows)
    query_rot = rounded(rotary(queries, positions, HEADS, HEAD_DIM, False))
    key_rot = rounded(rotary(key_vectors, positions, HEADS, HEAD_DIM, False))
    valid_slots = reach_mask(reach_table, shard_index * per_shard, per_shard, levels)
    allowed = score_mask(valid_slots, BLOCK)
    chunk_heads = HEADS // CHUNKS
    chunk_width = chunk_heads * HEAD_DIM
    columns = [slice(chunk * chunk_width, (chunk + 1) * chunk_width) for chunk in range(CHUNKS)]
    pieces = []
    pending = []
    for chunk, cols in enumerate(columns):
        key_c, value_c = key_rot[:, cols], values[:, cols]
        if pending:
            key_c, value_c, _ = lax.optimization_barrier((key_c, value_c, arrived))
        received = send_chunk(key_c, value_c, offsets)
        arrived = received[1:]
        output, query_grad, own, outgoing = attend_chunk(
            query_rot[:, cols], received, grad_out[:, cols], allowed, offsets, chunk_heads
        )
        pending.append(outgoing)
        key_accum_c, value_accum_c = gather_back(own, outgoing, offsets)
        rows = query_rot.shape[0]
        pieces.append(
            (
                output.reshape(rows, chunk_width),
                query_grad.reshape(rows, chunk_width),
                key_accum_c.reshape(rows, chunk_width),
                value_accum_c.reshape(rows, chunk_width),
            )
        )
    attended, query_grad, key_accum, value_accum = [
        jnp.concatenate(parts, axis=1) for parts in zip(*pieces)
    ]
    grad_queries = rotary(query_grad, positions, HEADS, HEAD_DIM, True).astype(jnp.bfloat16)
    grad_keys = rotary(key_accum, positions, HEADS, HEAD_DIM, True).astype(jnp.bfloat16)
    grad_values = value_accum.astype(jnp.bfloat16)
    return (attended, grad_queries, grad_keys, grad_values)


def solution(mesh):
    placed = (
        P(("groups", "ctx"), None),
        P(("groups", "ctx"), None),
        P(("groups", "ctx"), None),
        P(("groups", "ctx"), None),
        P("groups"),
        P(("groups", "ctx")),
    )
    return jax.shard_map(
        on_device,
        mesh=mesh,
        in_specs=placed,
        out_specs=(
            P(("groups", "ctx"), None),
            P(("groups", "ctx"), None),
            P(("groups", "ctx"), None),
            P(("groups", "ctx"), None),
        ),
        check_vma=False,
    )
```

```python
import math

import jax
import jax.numpy as jnp
from jax import lax
from jax.sharding import PartitionSpec as P

HEADS = 16
HEAD_DIM = 128
BLOCK = 128
CHUNK_HEADS = (6, 10)


def from_behind(value, axis, steps):
    count = lax.axis_size(axis)
    leading, last = (max(0, -steps), min(count, count - steps))
    return lax.ppermute(value, axis, [(source, source + steps) for source in range(leading, last)])


def rounded(matrix):
    return lax.optimization_barrier(matrix.astype(jnp.bfloat16))


def file_positions(file_lengths, global_rows):
    file_ends = jnp.cumsum(file_lengths)
    starts = file_ends - file_lengths
    owned_mask = starts[None, :] <= global_rows[:, None]
    latest = jnp.max(jnp.where(owned_mask, starts[None, :], 0), axis=1)
    return global_rows - latest


def rotary(matrix, positions, head_count, head_width, inverse):
    half_width = head_width // 2
    exponent = jnp.arange(half_width, dtype=jnp.float32) * (2.0 / head_width)
    frequency = jnp.exp(exponent * -math.log(10000.0))
    angles = positions.astype(jnp.float32)[:, None] * frequency[None, :]
    cosine = jnp.cos(angles)[:, None, :]
    sine_table = jnp.sin(angles)[:, None, :]
    shaped = matrix.astype(jnp.float32).reshape(matrix.shape[0], head_count, head_width)
    former = shaped[..., :half_width]
    latter = shaped[..., half_width:]
    if inverse:
        turned = jnp.concatenate(
            [former * cosine + latter * sine_table, latter * cosine - former * sine_table], axis=-1
        )
    else:
        turned = jnp.concatenate(
            [former * cosine - latter * sine_table, latter * cosine + former * sine_table], axis=-1
        )
    return turned.reshape(matrix.shape[0], head_count * head_width)


def reach_mask(reach_rows, first_block, per_shard, levels):
    block_ids = first_block + jnp.arange(per_shard, dtype=jnp.int32)
    level_ids = jnp.arange(levels, dtype=jnp.int32)
    distances = jnp.array([2**level_index for level_index in range(levels)], dtype=jnp.int32)
    reached = (level_ids[None, :] < reach_rows[:, None]) & (
        block_ids[:, None] - distances[None, :] >= 0
    )
    return jnp.concatenate([jnp.ones((per_shard, 1), dtype=bool), reached], axis=1)


def score_mask(valid_slots, block_rows):
    row_ids = jnp.arange(block_rows)
    causal = row_ids[None, :] <= row_ids[:, None]
    first_slot = jnp.arange(valid_slots.shape[1]) == 0
    inside = jnp.where(first_slot[:, None, None], causal[None], True)
    allowed = inside[None] & valid_slots[:, :, None, None]
    return jnp.transpose(allowed, (0, 2, 1, 3))[:, None]


def send_chunk(key_c, value_c, offsets):
    pair = jnp.stack([key_c, value_c])
    received = {0: pair}
    for offset in offsets:
        if (offset.bit_length() - 1) % 2 == 1:
            half = offset // 2
            received[offset] = from_behind(received[half], "ctx", half)
        else:
            received[offset] = from_behind(pair, "ctx", offset)
    return [received[0]] + [received[offset] for offset in offsets]


def attend_chunk(query_c, received, grad_c, allowed, offsets, heads):
    scale_factor = 1.0 / math.sqrt(HEAD_DIM)
    rows = query_c.shape[0]
    head_shape = (rows, heads, HEAD_DIM)
    key_stack = jnp.stack([moved[0].reshape(head_shape) for moved in received])[None]
    value_stack = jnp.stack([moved[1].reshape(head_shape) for moved in received])[None]
    query_stack = query_c.reshape((1,) + head_shape)
    grad_stack = grad_c.reshape((1,) + head_shape)
    raw_scores = (
        jnp.einsum("bthd,bnuhd->bhtnu", query_stack, key_stack, preferred_element_type=jnp.float32)
        * scale_factor
    )
    scores = jnp.where(allowed, raw_scores, -1e30)
    row_peak = jnp.max(scores, axis=(3, 4), keepdims=True)
    summed = jnp.sum(jnp.exp(scores - row_peak), axis=(3, 4), keepdims=True)
    log_total = row_peak + jnp.log(summed)
    weights32 = jnp.exp(scores - log_total)
    weights = rounded(weights32)
    output = rounded(
        jnp.einsum("bhtnu,bnuhd->bthd", weights, value_stack, preferred_element_type=jnp.float32)
    )
    grad_probs = jnp.einsum(
        "bthd,bnuhd->bhtnu", grad_stack, value_stack, preferred_element_type=jnp.float32
    )
    delta_rows = jnp.sum(grad_stack.astype(jnp.float32) * output.astype(jnp.float32), axis=-1)
    delta_rows = jnp.transpose(delta_rows, (0, 2, 1))[:, :, :, None, None]
    grad_scores = rounded(weights32 * (grad_probs - delta_rows) * scale_factor)
    query_grad = jnp.einsum(
        "bhtnu,bnuhd->bthd", grad_scores, key_stack, preferred_element_type=jnp.float32
    )
    key_terms = jnp.einsum(
        "bhtnu,bthd->bnuhd", grad_scores, query_stack, preferred_element_type=jnp.float32
    )
    value_terms = jnp.einsum(
        "bhtnu,bthd->bnuhd", weights, grad_stack, preferred_element_type=jnp.float32
    )
    own = (rounded(key_terms[0, 0]), rounded(value_terms[0, 0]))
    outgoing = [
        jnp.stack([key_terms[0, slot_index], value_terms[0, slot_index]]).astype(jnp.bfloat16)
        for slot_index in range(1, len(offsets) + 1)
    ]
    return output, query_grad, own, outgoing


def gather_back(own, outgoing, offsets):
    key_accum = own[0].astype(jnp.float32)
    value_accum = own[1].astype(jnp.float32)
    for parts, offset in zip(outgoing, offsets):
        returned = from_behind(parts, "ctx", -offset)
        key_accum = key_accum + returned[0].astype(jnp.float32)
        value_accum = value_accum + returned[1].astype(jnp.float32)
    return key_accum, value_accum


def on_device(queries, key_vectors, values, grad_out, file_lengths, reach_table):
    local_rows = queries.shape[0]
    width_all = queries.shape[1]
    per_shard = local_rows // BLOCK
    ctx_size = lax.axis_size("ctx")
    levels = (per_shard * ctx_size - 1).bit_length()
    offsets = [2**level_index for level_index in range(levels)]
    shard_index = lax.axis_index("ctx")
    global_rows = shard_index * local_rows + jnp.arange(local_rows, dtype=jnp.int32)
    positions = file_positions(file_lengths, global_rows)
    query_rot = rounded(rotary(queries, positions, HEADS, HEAD_DIM, False))
    key_rot = rounded(rotary(key_vectors, positions, HEADS, HEAD_DIM, False))
    valid_slots = reach_mask(reach_table, shard_index * per_shard, per_shard, levels)
    allowed = score_mask(valid_slots, BLOCK)
    bounds = [sum(CHUNK_HEADS[:chunk]) * HEAD_DIM for chunk in range(len(CHUNK_HEADS) + 1)]
    pieces = []
    pending = []
    for chunk, chunk_heads in enumerate(CHUNK_HEADS):
        chunk_width = chunk_heads * HEAD_DIM
        cols = slice(bounds[chunk], bounds[chunk + 1])
        key_c, value_c = key_rot[:, cols], values[:, cols]
        if pending:
            key_c, value_c, _ = lax.optimization_barrier((key_c, value_c, pieces[-1][0]))
        received = send_chunk(key_c, value_c, offsets)
        output, query_grad, own, outgoing = attend_chunk(
            query_rot[:, cols], received, grad_out[:, cols], allowed, offsets, chunk_heads
        )
        pending.append(outgoing)
        key_accum_c, value_accum_c = gather_back(own, outgoing, offsets)
        rows = query_rot.shape[0]
        pieces.append(
            (
                output.reshape(rows, chunk_width),
                query_grad.reshape(rows, chunk_width),
                key_accum_c.reshape(rows, chunk_width),
                value_accum_c.reshape(rows, chunk_width),
            )
        )
    attended, query_grad, key_accum, value_accum = [
        jnp.concatenate(parts, axis=1) for parts in zip(*pieces)
    ]
    grad_queries = rotary(query_grad, positions, HEADS, HEAD_DIM, True).astype(jnp.bfloat16)
    grad_keys = rotary(key_accum, positions, HEADS, HEAD_DIM, True).astype(jnp.bfloat16)
    grad_values = value_accum.astype(jnp.bfloat16)
    return (attended, grad_queries, grad_keys, grad_values)


def solution(mesh):
    placed = (
        P(("groups", "ctx"), None),
        P(("groups", "ctx"), None),
        P(("groups", "ctx"), None),
        P(("groups", "ctx"), None),
        P("groups"),
        P(("groups", "ctx")),
    )
    return jax.shard_map(
        on_device,
        mesh=mesh,
        in_specs=placed,
        out_specs=(
            P(("groups", "ctx"), None),
            P(("groups", "ctx"), None),
            P(("groups", "ctx"), None),
            P(("groups", "ctx"), None),
        ),
        check_vma=False,
    )
```

```python
import math

import jax
import jax.numpy as jnp
from jax import lax
from jax.sharding import PartitionSpec as P

HEADS = 16
HEAD_DIM = 128
BLOCK = 128
CHUNKS = 2


def from_behind(value, axis, steps):
    count = lax.axis_size(axis)
    leading, last = (max(0, -steps), min(count, count - steps))
    return lax.ppermute(value, axis, [(source, source + steps) for source in range(leading, last)])


def rounded(matrix):
    return lax.optimization_barrier(matrix.astype(jnp.bfloat16))


def file_positions(file_lengths, global_rows):
    file_ends = jnp.cumsum(file_lengths)
    starts = file_ends - file_lengths
    owned_mask = starts[None, :] <= global_rows[:, None]
    latest = jnp.max(jnp.where(owned_mask, starts[None, :], 0), axis=1)
    return global_rows - latest


def rotary(matrix, positions, head_count, head_width, inverse):
    half_width = head_width // 2
    exponent = jnp.arange(half_width, dtype=jnp.float32) * (2.0 / head_width)
    frequency = jnp.exp(exponent * -math.log(10000.0))
    angles = positions.astype(jnp.float32)[:, None] * frequency[None, :]
    cosine = jnp.cos(angles)[:, None, :]
    sine_table = jnp.sin(angles)[:, None, :]
    shaped = matrix.astype(jnp.float32).reshape(matrix.shape[0], head_count, head_width)
    former = shaped[..., :half_width]
    latter = shaped[..., half_width:]
    if inverse:
        turned = jnp.concatenate(
            [former * cosine + latter * sine_table, latter * cosine - former * sine_table], axis=-1
        )
    else:
        turned = jnp.concatenate(
            [former * cosine - latter * sine_table, latter * cosine + former * sine_table], axis=-1
        )
    return turned.reshape(matrix.shape[0], head_count * head_width)


def reach_mask(reach_rows, first_block, per_shard, levels):
    block_ids = first_block + jnp.arange(per_shard, dtype=jnp.int32)
    level_ids = jnp.arange(levels, dtype=jnp.int32)
    distances = jnp.array([2**level_index for level_index in range(levels)], dtype=jnp.int32)
    reached = (level_ids[None, :] < reach_rows[:, None]) & (
        block_ids[:, None] - distances[None, :] >= 0
    )
    return jnp.concatenate([jnp.ones((per_shard, 1), dtype=bool), reached], axis=1)


def score_mask(valid_slots, block_rows):
    row_ids = jnp.arange(block_rows)
    causal = row_ids[None, :] <= row_ids[:, None]
    first_slot = jnp.arange(valid_slots.shape[1]) == 0
    inside = jnp.where(first_slot[:, None, None], causal[None], True)
    allowed = inside[None] & valid_slots[:, :, None, None]
    return jnp.transpose(allowed, (0, 2, 1, 3))[:, None]


def gather_chunk(key_c, value_c, offsets):
    pair = jnp.stack([key_c, value_c])
    gathered = lax.all_gather(pair, "ctx")
    shard_index = lax.axis_index("ctx")
    picked = [
        lax.dynamic_index_in_dim(gathered, jnp.maximum(shard_index - offset, 0), 0, keepdims=False)
        for offset in offsets
    ]
    return [pair] + picked


def send_chunk(key_c, value_c, offsets):
    pair = jnp.stack([key_c, value_c])
    received = {0: pair}
    for offset in offsets:
        if (offset.bit_length() - 1) % 2 == 1:
            half = offset // 2
            received[offset] = from_behind(received[half], "ctx", half)
        else:
            received[offset] = from_behind(pair, "ctx", offset)
    return [received[0]] + [received[offset] for offset in offsets]


def attend_chunk(query_c, received, grad_c, allowed, offsets, heads):
    scale_factor = 1.0 / math.sqrt(HEAD_DIM)
    rows = query_c.shape[0]
    head_shape = (rows, heads, HEAD_DIM)
    key_stack = jnp.stack([moved[0].reshape(head_shape) for moved in received])[None]
    value_stack = jnp.stack([moved[1].reshape(head_shape) for moved in received])[None]
    query_stack = query_c.reshape((1,) + head_shape)
    grad_stack = grad_c.reshape((1,) + head_shape)
    raw_scores = (
        jnp.einsum("bthd,bnuhd->bhtnu", query_stack, key_stack, preferred_element_type=jnp.float32)
        * scale_factor
    )
    scores = jnp.where(allowed, raw_scores, -1e30)
    row_peak = jnp.max(scores, axis=(3, 4), keepdims=True)
    summed = jnp.sum(jnp.exp(scores - row_peak), axis=(3, 4), keepdims=True)
    log_total = row_peak + jnp.log(summed)
    weights32 = jnp.exp(scores - log_total)
    weights = rounded(weights32)
    output = rounded(
        jnp.einsum("bhtnu,bnuhd->bthd", weights, value_stack, preferred_element_type=jnp.float32)
    )
    grad_probs = jnp.einsum(
        "bthd,bnuhd->bhtnu", grad_stack, value_stack, preferred_element_type=jnp.float32
    )
    delta_rows = jnp.sum(grad_stack.astype(jnp.float32) * output.astype(jnp.float32), axis=-1)
    delta_rows = jnp.transpose(delta_rows, (0, 2, 1))[:, :, :, None, None]
    grad_scores = rounded(weights32 * (grad_probs - delta_rows) * scale_factor)
    query_grad = jnp.einsum(
        "bhtnu,bnuhd->bthd", grad_scores, key_stack, preferred_element_type=jnp.float32
    )
    key_terms = jnp.einsum(
        "bhtnu,bthd->bnuhd", grad_scores, query_stack, preferred_element_type=jnp.float32
    )
    value_terms = jnp.einsum(
        "bhtnu,bthd->bnuhd", weights, grad_stack, preferred_element_type=jnp.float32
    )
    own = (rounded(key_terms[0, 0]), rounded(value_terms[0, 0]))
    outgoing = [
        jnp.stack([key_terms[0, slot_index], value_terms[0, slot_index]]).astype(jnp.bfloat16)
        for slot_index in range(1, len(offsets) + 1)
    ]
    return output, query_grad, own, outgoing


def gather_back(own, outgoing, offsets):
    key_accum = own[0].astype(jnp.float32)
    value_accum = own[1].astype(jnp.float32)
    for parts, offset in zip(outgoing, offsets):
        returned = from_behind(parts, "ctx", -offset)
        key_accum = key_accum + returned[0].astype(jnp.float32)
        value_accum = value_accum + returned[1].astype(jnp.float32)
    return key_accum, value_accum


def on_device(queries, key_vectors, values, grad_out, file_lengths, reach_table):
    local_rows = queries.shape[0]
    width_all = queries.shape[1]
    per_shard = local_rows // BLOCK
    ctx_size = lax.axis_size("ctx")
    levels = (per_shard * ctx_size - 1).bit_length()
    offsets = [2**level_index for level_index in range(levels)]
    shard_index = lax.axis_index("ctx")
    global_rows = shard_index * local_rows + jnp.arange(local_rows, dtype=jnp.int32)
    positions = file_positions(file_lengths, global_rows)
    query_rot = rounded(rotary(queries, positions, HEADS, HEAD_DIM, False))
    key_rot = rounded(rotary(key_vectors, positions, HEADS, HEAD_DIM, False))
    valid_slots = reach_mask(reach_table, shard_index * per_shard, per_shard, levels)
    allowed = score_mask(valid_slots, BLOCK)
    chunk_heads = HEADS // CHUNKS
    chunk_width = chunk_heads * HEAD_DIM
    columns = [slice(chunk * chunk_width, (chunk + 1) * chunk_width) for chunk in range(CHUNKS)]
    pieces = []
    pending = []
    for chunk, cols in enumerate(columns):
        key_c, value_c = key_rot[:, cols], values[:, cols]
        if pending:
            key_c, value_c, _ = lax.optimization_barrier((key_c, value_c, pieces[-1][0]))
        fetch = gather_chunk if chunk == 0 else send_chunk
        received = fetch(key_c, value_c, offsets)
        output, query_grad, own, outgoing = attend_chunk(
            query_rot[:, cols], received, grad_out[:, cols], allowed, offsets, chunk_heads
        )
        pending.append(outgoing)
        key_accum_c, value_accum_c = gather_back(own, outgoing, offsets)
        rows = query_rot.shape[0]
        pieces.append(
            (
                output.reshape(rows, chunk_width),
                query_grad.reshape(rows, chunk_width),
                key_accum_c.reshape(rows, chunk_width),
                value_accum_c.reshape(rows, chunk_width),
            )
        )
    attended, query_grad, key_accum, value_accum = [
        jnp.concatenate(parts, axis=1) for parts in zip(*pieces)
    ]
    grad_queries = rotary(query_grad, positions, HEADS, HEAD_DIM, True).astype(jnp.bfloat16)
    grad_keys = rotary(key_accum, positions, HEADS, HEAD_DIM, True).astype(jnp.bfloat16)
    grad_values = value_accum.astype(jnp.bfloat16)
    return (attended, grad_queries, grad_keys, grad_values)


def solution(mesh):
    placed = (
        P(("groups", "ctx"), None),
        P(("groups", "ctx"), None),
        P(("groups", "ctx"), None),
        P(("groups", "ctx"), None),
        P("groups"),
        P(("groups", "ctx")),
    )
    return jax.shard_map(
        on_device,
        mesh=mesh,
        in_specs=placed,
        out_specs=(
            P(("groups", "ctx"), None),
            P(("groups", "ctx"), None),
            P(("groups", "ctx"), None),
            P(("groups", "ctx"), None),
        ),
        check_vma=False,
    )
```

```python
import math

import jax
import jax.numpy as jnp
from jax import lax
from jax.sharding import PartitionSpec as P

HEADS = 16
HEAD_DIM = 128
BLOCK = 128
CHUNK_HEADS = (10, 6)


def from_behind(value, axis, steps):
    count = lax.axis_size(axis)
    leading, last = (max(0, -steps), min(count, count - steps))
    return lax.ppermute(value, axis, [(source, source + steps) for source in range(leading, last)])


def rounded(matrix):
    return lax.optimization_barrier(matrix.astype(jnp.bfloat16))


def file_positions(file_lengths, global_rows):
    file_ends = jnp.cumsum(file_lengths)
    starts = file_ends - file_lengths
    owned_mask = starts[None, :] <= global_rows[:, None]
    latest = jnp.max(jnp.where(owned_mask, starts[None, :], 0), axis=1)
    return global_rows - latest


def rotary(matrix, positions, head_count, head_width, inverse):
    half_width = head_width // 2
    exponent = jnp.arange(half_width, dtype=jnp.float32) * (2.0 / head_width)
    frequency = jnp.exp(exponent * -math.log(10000.0))
    angles = positions.astype(jnp.float32)[:, None] * frequency[None, :]
    cosine = jnp.cos(angles)[:, None, :]
    sine_table = jnp.sin(angles)[:, None, :]
    shaped = matrix.astype(jnp.float32).reshape(matrix.shape[0], head_count, head_width)
    former = shaped[..., :half_width]
    latter = shaped[..., half_width:]
    if inverse:
        turned = jnp.concatenate(
            [former * cosine + latter * sine_table, latter * cosine - former * sine_table], axis=-1
        )
    else:
        turned = jnp.concatenate(
            [former * cosine - latter * sine_table, latter * cosine + former * sine_table], axis=-1
        )
    return turned.reshape(matrix.shape[0], head_count * head_width)


def reach_mask(reach_rows, first_block, per_shard, levels):
    block_ids = first_block + jnp.arange(per_shard, dtype=jnp.int32)
    level_ids = jnp.arange(levels, dtype=jnp.int32)
    distances = jnp.array([2**level_index for level_index in range(levels)], dtype=jnp.int32)
    reached = (level_ids[None, :] < reach_rows[:, None]) & (
        block_ids[:, None] - distances[None, :] >= 0
    )
    return jnp.concatenate([jnp.ones((per_shard, 1), dtype=bool), reached], axis=1)


def score_mask(valid_slots, block_rows):
    row_ids = jnp.arange(block_rows)
    causal = row_ids[None, :] <= row_ids[:, None]
    first_slot = jnp.arange(valid_slots.shape[1]) == 0
    inside = jnp.where(first_slot[:, None, None], causal[None], True)
    allowed = inside[None] & valid_slots[:, :, None, None]
    return jnp.transpose(allowed, (0, 2, 1, 3))[:, None]


def send_chunk(key_c, value_c, offsets):
    pair = jnp.stack([key_c, value_c])
    received = {0: pair}
    for offset in offsets:
        if (offset.bit_length() - 1) % 2 == 1:
            half = offset // 2
            received[offset] = from_behind(received[half], "ctx", half)
        else:
            received[offset] = from_behind(pair, "ctx", offset)
    return [received[0]] + [received[offset] for offset in offsets]


def attend_chunk(query_c, received, grad_c, allowed, offsets, heads):
    scale_factor = 1.0 / math.sqrt(HEAD_DIM)
    rows = query_c.shape[0]
    head_shape = (rows, heads, HEAD_DIM)
    key_stack = jnp.stack([moved[0].reshape(head_shape) for moved in received])[None]
    value_stack = jnp.stack([moved[1].reshape(head_shape) for moved in received])[None]
    query_stack = query_c.reshape((1,) + head_shape)
    grad_stack = grad_c.reshape((1,) + head_shape)
    raw_scores = (
        jnp.einsum("bthd,bnuhd->bhtnu", query_stack, key_stack, preferred_element_type=jnp.float32)
        * scale_factor
    )
    scores = jnp.where(allowed, raw_scores, -1e30)
    row_peak = jnp.max(scores, axis=(3, 4), keepdims=True)
    summed = jnp.sum(jnp.exp(scores - row_peak), axis=(3, 4), keepdims=True)
    log_total = row_peak + jnp.log(summed)
    weights32 = jnp.exp(scores - log_total)
    weights = rounded(weights32)
    output = rounded(
        jnp.einsum("bhtnu,bnuhd->bthd", weights, value_stack, preferred_element_type=jnp.float32)
    )
    grad_probs = jnp.einsum(
        "bthd,bnuhd->bhtnu", grad_stack, value_stack, preferred_element_type=jnp.float32
    )
    delta_rows = jnp.sum(grad_stack.astype(jnp.float32) * output.astype(jnp.float32), axis=-1)
    delta_rows = jnp.transpose(delta_rows, (0, 2, 1))[:, :, :, None, None]
    grad_scores = rounded(weights32 * (grad_probs - delta_rows) * scale_factor)
    query_grad = jnp.einsum(
        "bhtnu,bnuhd->bthd", grad_scores, key_stack, preferred_element_type=jnp.float32
    )
    key_terms = jnp.einsum(
        "bhtnu,bthd->bnuhd", grad_scores, query_stack, preferred_element_type=jnp.float32
    )
    value_terms = jnp.einsum(
        "bhtnu,bthd->bnuhd", weights, grad_stack, preferred_element_type=jnp.float32
    )
    own = (rounded(key_terms[0, 0]), rounded(value_terms[0, 0]))
    outgoing = [
        jnp.stack([key_terms[0, slot_index], value_terms[0, slot_index]]).astype(jnp.bfloat16)
        for slot_index in range(1, len(offsets) + 1)
    ]
    return output, query_grad, own, outgoing


def gather_back(own, outgoing, offsets):
    key_accum = own[0].astype(jnp.float32)
    value_accum = own[1].astype(jnp.float32)
    for parts, offset in zip(outgoing, offsets):
        returned = from_behind(parts, "ctx", -offset)
        key_accum = key_accum + returned[0].astype(jnp.float32)
        value_accum = value_accum + returned[1].astype(jnp.float32)
    return key_accum, value_accum


def on_device(queries, key_vectors, values, grad_out, file_lengths, reach_table):
    local_rows = queries.shape[0]
    width_all = queries.shape[1]
    per_shard = local_rows // BLOCK
    ctx_size = lax.axis_size("ctx")
    levels = (per_shard * ctx_size - 1).bit_length()
    offsets = [2**level_index for level_index in range(levels)]
    shard_index = lax.axis_index("ctx")
    global_rows = shard_index * local_rows + jnp.arange(local_rows, dtype=jnp.int32)
    positions = file_positions(file_lengths, global_rows)
    query_rot = rounded(rotary(queries, positions, HEADS, HEAD_DIM, False))
    key_rot = rounded(rotary(key_vectors, positions, HEADS, HEAD_DIM, False))
    valid_slots = reach_mask(reach_table, shard_index * per_shard, per_shard, levels)
    allowed = score_mask(valid_slots, BLOCK)
    bounds = [sum(CHUNK_HEADS[:chunk]) * HEAD_DIM for chunk in range(len(CHUNK_HEADS) + 1)]
    pieces = []
    pending = []
    for chunk, chunk_heads in enumerate(CHUNK_HEADS):
        chunk_width = chunk_heads * HEAD_DIM
        cols = slice(bounds[chunk], bounds[chunk + 1])
        key_c, value_c = key_rot[:, cols], values[:, cols]
        if pending:
            key_c, value_c, _ = lax.optimization_barrier((key_c, value_c, pieces[-1][0]))
        received = send_chunk(key_c, value_c, offsets)
        output, query_grad, own, outgoing = attend_chunk(
            query_rot[:, cols], received, grad_out[:, cols], allowed, offsets, chunk_heads
        )
        pending.append(outgoing)
        key_accum_c, value_accum_c = gather_back(own, outgoing, offsets)
        rows = query_rot.shape[0]
        pieces.append(
            (
                output.reshape(rows, chunk_width),
                query_grad.reshape(rows, chunk_width),
                key_accum_c.reshape(rows, chunk_width),
                value_accum_c.reshape(rows, chunk_width),
            )
        )
    attended, query_grad, key_accum, value_accum = [
        jnp.concatenate(parts, axis=1) for parts in zip(*pieces)
    ]
    grad_queries = rotary(query_grad, positions, HEADS, HEAD_DIM, True).astype(jnp.bfloat16)
    grad_keys = rotary(key_accum, positions, HEADS, HEAD_DIM, True).astype(jnp.bfloat16)
    grad_values = value_accum.astype(jnp.bfloat16)
    return (attended, grad_queries, grad_keys, grad_values)


def solution(mesh):
    placed = (
        P(("groups", "ctx"), None),
        P(("groups", "ctx"), None),
        P(("groups", "ctx"), None),
        P(("groups", "ctx"), None),
        P("groups"),
        P(("groups", "ctx")),
    )
    return jax.shard_map(
        on_device,
        mesh=mesh,
        in_specs=placed,
        out_specs=(
            P(("groups", "ctx"), None),
            P(("groups", "ctx"), None),
            P(("groups", "ctx"), None),
            P(("groups", "ctx"), None),
        ),
        check_vma=False,
    )
```

```python
import math

import jax
import jax.numpy as jnp
from jax import lax
from jax.experimental import pallas as pl
from jax.sharding import PartitionSpec as P

HEADS = 16
HEAD_DIM = 128
BLOCK = 128
CHUNKS = 2


def from_behind(value, axis, steps):
    count = lax.axis_size(axis)
    leading, last = (max(0, -steps), min(count, count - steps))
    return lax.ppermute(value, axis, [(source, source + steps) for source in range(leading, last)])


def rounded(matrix):
    return lax.optimization_barrier(matrix.astype(jnp.bfloat16))


def file_positions(file_lengths, global_rows):
    file_ends = jnp.cumsum(file_lengths)
    starts = file_ends - file_lengths
    owned_mask = starts[None, :] <= global_rows[:, None]
    latest = jnp.max(jnp.where(owned_mask, starts[None, :], 0), axis=1)
    return global_rows - latest


def rotary(matrix, positions, head_count, head_width, inverse):
    half_width = head_width // 2
    exponent = jnp.arange(half_width, dtype=jnp.float32) * (2.0 / head_width)
    frequency = jnp.exp(exponent * -math.log(10000.0))
    angles = positions.astype(jnp.float32)[:, None] * frequency[None, :]
    cosine = jnp.cos(angles)[:, None, :]
    sine_table = jnp.sin(angles)[:, None, :]
    shaped = matrix.astype(jnp.float32).reshape(matrix.shape[0], head_count, head_width)
    former = shaped[..., :half_width]
    latter = shaped[..., half_width:]
    if inverse:
        turned = jnp.concatenate(
            [former * cosine + latter * sine_table, latter * cosine - former * sine_table], axis=-1
        )
    else:
        turned = jnp.concatenate(
            [former * cosine - latter * sine_table, latter * cosine + former * sine_table], axis=-1
        )
    return turned.reshape(matrix.shape[0], head_count * head_width)


def reach_mask(reach_rows, first_block, per_shard, levels):
    block_ids = first_block + jnp.arange(per_shard, dtype=jnp.int32)
    level_ids = jnp.arange(levels, dtype=jnp.int32)
    distances = jnp.array([2**level_index for level_index in range(levels)], dtype=jnp.int32)
    reached = (level_ids[None, :] < reach_rows[:, None]) & (
        block_ids[:, None] - distances[None, :] >= 0
    )
    return jnp.concatenate([jnp.ones((per_shard, 1), dtype=bool), reached], axis=1)


def score_mask(valid_slots, block_rows):
    row_ids = jnp.arange(block_rows)
    causal = row_ids[None, :] <= row_ids[:, None]
    first_slot = jnp.arange(valid_slots.shape[1]) == 0
    inside = jnp.where(first_slot[:, None, None], causal[None], True)
    allowed = inside[None] & valid_slots[:, :, None, None]
    return jnp.transpose(allowed, (0, 2, 1, 3))[:, None]


def send_chunk(key_c, value_c, offsets):
    pair = jnp.stack([key_c, value_c])
    received = {0: pair}
    for offset in offsets:
        if (offset.bit_length() - 1) % 2 == 1:
            half = offset // 2
            received[offset] = from_behind(received[half], "ctx", half)
        else:
            received[offset] = from_behind(pair, "ctx", offset)
    return [received[0]] + [received[offset] for offset in offsets]


def forward_kernel(*refs):
    query_ref, mask_ref = refs[0], refs[1]
    pair_refs = refs[2:-2]
    out_ref, weights_ref = refs[-2], refs[-1]
    scale_factor = 1.0 / math.sqrt(HEAD_DIM)
    query = query_ref[...]
    keys = jnp.concatenate([ref[0] for ref in pair_refs], axis=0)
    vals = jnp.concatenate([ref[1] for ref in pair_refs], axis=0)
    last = (((1,), (1,)), ((), ()))
    raw = lax.dot_general(query, keys, last, preferred_element_type=jnp.float32)
    scores = jnp.where(mask_ref[...] > 0, raw * scale_factor, -1e30)
    row_peak = jnp.max(scores, axis=1, keepdims=True)
    summed = jnp.sum(jnp.exp(scores - row_peak), axis=1, keepdims=True)
    log_total = row_peak + jnp.log(summed)
    weights32 = jnp.exp(scores - log_total)
    weights_ref[0] = weights32
    weights = weights32.astype(jnp.bfloat16)
    out_ref[...] = jnp.dot(weights, vals, preferred_element_type=jnp.float32).astype(jnp.bfloat16)


def backward_kernel(*refs):
    slots = (len(refs) - 5) // 2
    query_ref, grad_ref, out_ref, weights_ref = refs[0], refs[1], refs[2], refs[3]
    pair_refs = refs[4 : 4 + slots]
    qgrad_ref = refs[4 + slots]
    part_refs = refs[5 + slots :]
    scale_factor = 1.0 / math.sqrt(HEAD_DIM)
    query = query_ref[...]
    grad = grad_ref[...]
    output = out_ref[...]
    weights32 = weights_ref[0]
    weights = weights32.astype(jnp.bfloat16)
    keys = jnp.concatenate([ref[0] for ref in pair_refs], axis=0)
    vals = jnp.concatenate([ref[1] for ref in pair_refs], axis=0)
    last = (((1,), (1,)), ((), ()))
    first = (((0,), (0,)), ((), ()))
    grad_probs = lax.dot_general(grad, vals, last, preferred_element_type=jnp.float32)
    delta = jnp.sum(grad.astype(jnp.float32) * output.astype(jnp.float32), axis=1, keepdims=True)
    grad_scores = (weights32 * (grad_probs - delta) * scale_factor).astype(jnp.bfloat16)
    qgrad_ref[...] = jnp.dot(grad_scores, keys, preferred_element_type=jnp.float32)
    key_terms = lax.dot_general(grad_scores, query, first, preferred_element_type=jnp.float32)
    value_terms = lax.dot_general(weights, grad, first, preferred_element_type=jnp.float32)
    rows = query.shape[0]
    for slot, ref in enumerate(part_refs):
        ref[0] = key_terms[slot * rows : (slot + 1) * rows].astype(jnp.bfloat16)
        ref[1] = value_terms[slot * rows : (slot + 1) * rows].astype(jnp.bfloat16)


def attend_forward(query_c, received, allowed, heads):
    rows, width = query_c.shape
    slots = len(received)
    mask = jnp.where(allowed, 1.0, 0.0).astype(jnp.float32).reshape(rows, slots * rows)
    flat_spec = pl.BlockSpec((rows, HEAD_DIM), lambda h: (0, h))
    pair_spec = pl.BlockSpec((2, rows, HEAD_DIM), lambda h: (0, 0, h))
    mask_spec = pl.BlockSpec((rows, slots * rows), lambda h: (0, 0))
    weights_spec = pl.BlockSpec((1, rows, slots * rows), lambda h: (h, 0, 0))
    return pl.pallas_call(
        forward_kernel,
        grid=(heads,),
        in_specs=[flat_spec, mask_spec] + [pair_spec] * slots,
        out_specs=[flat_spec, weights_spec],
        out_shape=[
            jax.ShapeDtypeStruct((rows, width), jnp.bfloat16),
            jax.ShapeDtypeStruct((heads, rows, slots * rows), jnp.float32),
        ],
    )(query_c, mask, *received)


def attend_backward(query_c, grad_c, output, weights32, received, heads):
    rows, width = query_c.shape
    slots = len(received)
    flat_spec = pl.BlockSpec((rows, HEAD_DIM), lambda h: (0, h))
    pair_spec = pl.BlockSpec((2, rows, HEAD_DIM), lambda h: (0, 0, h))
    weights_spec = pl.BlockSpec((1, rows, slots * rows), lambda h: (h, 0, 0))
    pair_shape = jax.ShapeDtypeStruct((2, rows, width), jnp.bfloat16)
    results = pl.pallas_call(
        backward_kernel,
        grid=(heads,),
        in_specs=[flat_spec, flat_spec, flat_spec, weights_spec] + [pair_spec] * slots,
        out_specs=[flat_spec] + [pair_spec] * slots,
        out_shape=[jax.ShapeDtypeStruct((rows, width), jnp.float32)] + [pair_shape] * slots,
    )(query_c, grad_c, output, weights32, *received)
    query_grad = results[0]
    own = (results[1][0], results[1][1])
    outgoing = list(results[2:])
    return query_grad, own, outgoing


def gather_back(own, outgoing, offsets):
    key_accum = own[0].astype(jnp.float32)
    value_accum = own[1].astype(jnp.float32)
    for parts, offset in zip(outgoing, offsets):
        returned = from_behind(parts, "ctx", -offset)
        key_accum = key_accum + returned[0].astype(jnp.float32)
        value_accum = value_accum + returned[1].astype(jnp.float32)
    return key_accum, value_accum


def on_device(queries, key_vectors, values, grad_out, file_lengths, reach_table):
    local_rows = queries.shape[0]
    width_all = queries.shape[1]
    per_shard = local_rows // BLOCK
    ctx_size = lax.axis_size("ctx")
    levels = (per_shard * ctx_size - 1).bit_length()
    offsets = [2**level_index for level_index in range(levels)]
    shard_index = lax.axis_index("ctx")
    global_rows = shard_index * local_rows + jnp.arange(local_rows, dtype=jnp.int32)
    positions = file_positions(file_lengths, global_rows)
    query_rot = rounded(rotary(queries, positions, HEADS, HEAD_DIM, False))
    key_rot = rounded(rotary(key_vectors, positions, HEADS, HEAD_DIM, False))
    valid_slots = reach_mask(reach_table, shard_index * per_shard, per_shard, levels)
    allowed = score_mask(valid_slots, BLOCK)
    chunk_heads = HEADS // CHUNKS
    chunk_width = chunk_heads * HEAD_DIM
    columns = [slice(chunk * chunk_width, (chunk + 1) * chunk_width) for chunk in range(CHUNKS)]
    pieces = []
    pending = []
    for chunk, cols in enumerate(columns):
        key_c, value_c = key_rot[:, cols], values[:, cols]
        if pending:
            key_c, value_c, _ = lax.optimization_barrier((key_c, value_c, pieces[-1][0]))
        received = send_chunk(key_c, value_c, offsets)
        output, weights32 = attend_forward(query_rot[:, cols], received, allowed, chunk_heads)
        query_grad, own, outgoing = attend_backward(
            query_rot[:, cols], grad_out[:, cols], output, weights32, received, chunk_heads
        )
        pending.append(outgoing)
        key_accum_c, value_accum_c = gather_back(own, outgoing, offsets)
        rows = query_rot.shape[0]
        pieces.append(
            (
                output.reshape(rows, chunk_width),
                query_grad.reshape(rows, chunk_width),
                key_accum_c.reshape(rows, chunk_width),
                value_accum_c.reshape(rows, chunk_width),
            )
        )
    attended, query_grad, key_accum, value_accum = [
        jnp.concatenate(parts, axis=1) for parts in zip(*pieces)
    ]
    grad_queries = rotary(query_grad, positions, HEADS, HEAD_DIM, True).astype(jnp.bfloat16)
    grad_keys = rotary(key_accum, positions, HEADS, HEAD_DIM, True).astype(jnp.bfloat16)
    grad_values = value_accum.astype(jnp.bfloat16)
    return (attended, grad_queries, grad_keys, grad_values)


def solution(mesh):
    placed = (
        P(("groups", "ctx"), None),
        P(("groups", "ctx"), None),
        P(("groups", "ctx"), None),
        P(("groups", "ctx"), None),
        P("groups"),
        P(("groups", "ctx")),
    )
    return jax.shard_map(
        on_device,
        mesh=mesh,
        in_specs=placed,
        out_specs=(
            P(("groups", "ctx"), None),
            P(("groups", "ctx"), None),
            P(("groups", "ctx"), None),
            P(("groups", "ctx"), None),
        ),
        check_vma=False,
    )
```

```python
import math

import jax
import jax.numpy as jnp
from jax import lax
from jax.sharding import PartitionSpec as P

HEADS = 16
HEAD_DIM = 128
BLOCK = 128
CHUNK_HEADS = (4, 6, 6)


def from_behind(value, axis, steps):
    count = lax.axis_size(axis)
    leading, last = (max(0, -steps), min(count, count - steps))
    return lax.ppermute(value, axis, [(source, source + steps) for source in range(leading, last)])


def rounded(matrix):
    return lax.optimization_barrier(matrix.astype(jnp.bfloat16))


def file_positions(file_lengths, global_rows):
    file_ends = jnp.cumsum(file_lengths)
    starts = file_ends - file_lengths
    owned_mask = starts[None, :] <= global_rows[:, None]
    latest = jnp.max(jnp.where(owned_mask, starts[None, :], 0), axis=1)
    return global_rows - latest


def rotary(matrix, positions, head_count, head_width, inverse):
    half_width = head_width // 2
    exponent = jnp.arange(half_width, dtype=jnp.float32) * (2.0 / head_width)
    frequency = jnp.exp(exponent * -math.log(10000.0))
    angles = positions.astype(jnp.float32)[:, None] * frequency[None, :]
    cosine = jnp.cos(angles)[:, None, :]
    sine_table = jnp.sin(angles)[:, None, :]
    shaped = matrix.astype(jnp.float32).reshape(matrix.shape[0], head_count, head_width)
    former = shaped[..., :half_width]
    latter = shaped[..., half_width:]
    if inverse:
        turned = jnp.concatenate(
            [former * cosine + latter * sine_table, latter * cosine - former * sine_table], axis=-1
        )
    else:
        turned = jnp.concatenate(
            [former * cosine - latter * sine_table, latter * cosine + former * sine_table], axis=-1
        )
    return turned.reshape(matrix.shape[0], head_count * head_width)


def reach_mask(reach_rows, first_block, per_shard, levels):
    block_ids = first_block + jnp.arange(per_shard, dtype=jnp.int32)
    level_ids = jnp.arange(levels, dtype=jnp.int32)
    distances = jnp.array([2**level_index for level_index in range(levels)], dtype=jnp.int32)
    reached = (level_ids[None, :] < reach_rows[:, None]) & (
        block_ids[:, None] - distances[None, :] >= 0
    )
    return jnp.concatenate([jnp.ones((per_shard, 1), dtype=bool), reached], axis=1)


def score_mask(valid_slots, block_rows):
    row_ids = jnp.arange(block_rows)
    causal = row_ids[None, :] <= row_ids[:, None]
    first_slot = jnp.arange(valid_slots.shape[1]) == 0
    inside = jnp.where(first_slot[:, None, None], causal[None], True)
    allowed = inside[None] & valid_slots[:, :, None, None]
    return jnp.transpose(allowed, (0, 2, 1, 3))[:, None]


def send_chunk(key_c, value_c, offsets):
    pair = jnp.stack([key_c, value_c])
    received = {0: pair}
    for offset in offsets:
        if (offset.bit_length() - 1) % 2 == 1:
            half = offset // 2
            received[offset] = from_behind(received[half], "ctx", half)
        else:
            received[offset] = from_behind(pair, "ctx", offset)
    return [received[0]] + [received[offset] for offset in offsets]


def attend_chunk(query_c, received, grad_c, allowed, offsets, heads):
    scale_factor = 1.0 / math.sqrt(HEAD_DIM)
    rows = query_c.shape[0]
    head_shape = (rows, heads, HEAD_DIM)
    key_stack = jnp.stack([moved[0].reshape(head_shape) for moved in received])[None]
    value_stack = jnp.stack([moved[1].reshape(head_shape) for moved in received])[None]
    query_stack = query_c.reshape((1,) + head_shape)
    grad_stack = grad_c.reshape((1,) + head_shape)
    raw_scores = (
        jnp.einsum("bthd,bnuhd->bhtnu", query_stack, key_stack, preferred_element_type=jnp.float32)
        * scale_factor
    )
    scores = jnp.where(allowed, raw_scores, -1e30)
    row_peak = jnp.max(scores, axis=(3, 4), keepdims=True)
    summed = jnp.sum(jnp.exp(scores - row_peak), axis=(3, 4), keepdims=True)
    log_total = row_peak + jnp.log(summed)
    weights32 = jnp.exp(scores - log_total)
    weights = rounded(weights32)
    output = rounded(
        jnp.einsum("bhtnu,bnuhd->bthd", weights, value_stack, preferred_element_type=jnp.float32)
    )
    grad_probs = jnp.einsum(
        "bthd,bnuhd->bhtnu", grad_stack, value_stack, preferred_element_type=jnp.float32
    )
    delta_rows = jnp.sum(grad_stack.astype(jnp.float32) * output.astype(jnp.float32), axis=-1)
    delta_rows = jnp.transpose(delta_rows, (0, 2, 1))[:, :, :, None, None]
    grad_scores = rounded(weights32 * (grad_probs - delta_rows) * scale_factor)
    query_grad = jnp.einsum(
        "bhtnu,bnuhd->bthd", grad_scores, key_stack, preferred_element_type=jnp.float32
    )
    key_terms = jnp.einsum(
        "bhtnu,bthd->bnuhd", grad_scores, query_stack, preferred_element_type=jnp.float32
    )
    value_terms = jnp.einsum(
        "bhtnu,bthd->bnuhd", weights, grad_stack, preferred_element_type=jnp.float32
    )
    own = (rounded(key_terms[0, 0]), rounded(value_terms[0, 0]))
    outgoing = [
        jnp.stack([key_terms[0, slot_index], value_terms[0, slot_index]]).astype(jnp.bfloat16)
        for slot_index in range(1, len(offsets) + 1)
    ]
    return output, query_grad, own, outgoing


def gather_back(own, outgoing, offsets):
    key_accum = own[0].astype(jnp.float32)
    value_accum = own[1].astype(jnp.float32)
    for parts, offset in zip(outgoing, offsets):
        returned = from_behind(parts, "ctx", -offset)
        key_accum = key_accum + returned[0].astype(jnp.float32)
        value_accum = value_accum + returned[1].astype(jnp.float32)
    return key_accum, value_accum


def on_device(queries, key_vectors, values, grad_out, file_lengths, reach_table):
    local_rows = queries.shape[0]
    width_all = queries.shape[1]
    per_shard = local_rows // BLOCK
    ctx_size = lax.axis_size("ctx")
    levels = (per_shard * ctx_size - 1).bit_length()
    offsets = [2**level_index for level_index in range(levels)]
    shard_index = lax.axis_index("ctx")
    global_rows = shard_index * local_rows + jnp.arange(local_rows, dtype=jnp.int32)
    positions = file_positions(file_lengths, global_rows)
    query_rot = rounded(rotary(queries, positions, HEADS, HEAD_DIM, False))
    key_rot = rounded(rotary(key_vectors, positions, HEADS, HEAD_DIM, False))
    valid_slots = reach_mask(reach_table, shard_index * per_shard, per_shard, levels)
    allowed = score_mask(valid_slots, BLOCK)
    bounds = [sum(CHUNK_HEADS[:chunk]) * HEAD_DIM for chunk in range(len(CHUNK_HEADS) + 1)]
    pieces = []
    pending = []
    for chunk, chunk_heads in enumerate(CHUNK_HEADS):
        chunk_width = chunk_heads * HEAD_DIM
        cols = slice(bounds[chunk], bounds[chunk + 1])
        key_c, value_c = key_rot[:, cols], values[:, cols]
        if pending:
            key_c, value_c, _ = lax.optimization_barrier((key_c, value_c, pieces[-1][0]))
        received = send_chunk(key_c, value_c, offsets)
        output, query_grad, own, outgoing = attend_chunk(
            query_rot[:, cols], received, grad_out[:, cols], allowed, offsets, chunk_heads
        )
        pending.append(outgoing)
        key_accum_c, value_accum_c = gather_back(own, outgoing, offsets)
        rows = query_rot.shape[0]
        pieces.append(
            (
                output.reshape(rows, chunk_width),
                query_grad.reshape(rows, chunk_width),
                key_accum_c.reshape(rows, chunk_width),
                value_accum_c.reshape(rows, chunk_width),
            )
        )
    attended, query_grad, key_accum, value_accum = [
        jnp.concatenate(parts, axis=1) for parts in zip(*pieces)
    ]
    grad_queries = rotary(query_grad, positions, HEADS, HEAD_DIM, True).astype(jnp.bfloat16)
    grad_keys = rotary(key_accum, positions, HEADS, HEAD_DIM, True).astype(jnp.bfloat16)
    grad_values = value_accum.astype(jnp.bfloat16)
    return (attended, grad_queries, grad_keys, grad_values)


def solution(mesh):
    placed = (
        P(("groups", "ctx"), None),
        P(("groups", "ctx"), None),
        P(("groups", "ctx"), None),
        P(("groups", "ctx"), None),
        P("groups"),
        P(("groups", "ctx")),
    )
    return jax.shard_map(
        on_device,
        mesh=mesh,
        in_specs=placed,
        out_specs=(
            P(("groups", "ctx"), None),
            P(("groups", "ctx"), None),
            P(("groups", "ctx"), None),
            P(("groups", "ctx"), None),
        ),
        check_vma=False,
    )
```

```python
import math

import jax
import jax.numpy as jnp
from jax import lax
from jax.sharding import PartitionSpec as P

HEADS = 16
HEAD_DIM = 128
BLOCK = 128
CHUNKS = 2


def from_behind(value, axis, steps):
    count = lax.axis_size(axis)
    leading, last = (max(0, -steps), min(count, count - steps))
    return lax.ppermute(value, axis, [(source, source + steps) for source in range(leading, last)])


def rounded(matrix):
    return lax.optimization_barrier(matrix.astype(jnp.bfloat16))


def file_positions(file_lengths, global_rows):
    file_ends = jnp.cumsum(file_lengths)
    starts = file_ends - file_lengths
    owned_mask = starts[None, :] <= global_rows[:, None]
    latest = jnp.max(jnp.where(owned_mask, starts[None, :], 0), axis=1)
    return global_rows - latest


def rotary(matrix, positions, head_count, head_width, inverse):
    half_width = head_width // 2
    exponent = jnp.arange(half_width, dtype=jnp.float32) * (2.0 / head_width)
    frequency = jnp.exp(exponent * -math.log(10000.0))
    angles = positions.astype(jnp.float32)[:, None] * frequency[None, :]
    cosine = jnp.cos(angles)[:, None, :]
    sine_table = jnp.sin(angles)[:, None, :]
    shaped = matrix.astype(jnp.float32).reshape(matrix.shape[0], head_count, head_width)
    former = shaped[..., :half_width]
    latter = shaped[..., half_width:]
    if inverse:
        turned = jnp.concatenate(
            [former * cosine + latter * sine_table, latter * cosine - former * sine_table], axis=-1
        )
    else:
        turned = jnp.concatenate(
            [former * cosine - latter * sine_table, latter * cosine + former * sine_table], axis=-1
        )
    return turned.reshape(matrix.shape[0], head_count * head_width)


def reach_mask(reach_rows, first_block, per_shard, levels):
    block_ids = first_block + jnp.arange(per_shard, dtype=jnp.int32)
    level_ids = jnp.arange(levels, dtype=jnp.int32)
    distances = jnp.array([2**level_index for level_index in range(levels)], dtype=jnp.int32)
    reached = (level_ids[None, :] < reach_rows[:, None]) & (
        block_ids[:, None] - distances[None, :] >= 0
    )
    return jnp.concatenate([jnp.ones((per_shard, 1), dtype=bool), reached], axis=1)


def score_mask(valid_slots, block_rows):
    row_ids = jnp.arange(block_rows)
    causal = row_ids[None, :] <= row_ids[:, None]
    first_slot = jnp.arange(valid_slots.shape[1]) == 0
    inside = jnp.where(first_slot[:, None, None], causal[None], True)
    allowed = inside[None] & valid_slots[:, :, None, None]
    return jnp.transpose(allowed, (0, 2, 1, 3))[:, None]


def send_chunk(key_c, value_c, offsets):
    pair = jnp.stack([key_c, value_c])
    received = {0: pair}
    for offset in offsets:
        if (offset.bit_length() - 1) % 2 == 1:
            half = offset // 2
            received[offset] = from_behind(received[half], "ctx", half)
        else:
            received[offset] = from_behind(pair, "ctx", offset)
    return [received[0]] + [received[offset] for offset in offsets]


def attend_chunk(query_c, received, grad_c, allowed, offsets, heads):
    scale_factor = 1.0 / math.sqrt(HEAD_DIM)
    rows = query_c.shape[0]
    head_shape = (rows, heads, HEAD_DIM)
    key_stack = jnp.stack([moved[0].reshape(head_shape) for moved in received])[None]
    value_stack = jnp.stack([moved[1].reshape(head_shape) for moved in received])[None]
    query_stack = query_c.reshape((1,) + head_shape)
    grad_stack = grad_c.reshape((1,) + head_shape)
    raw_scores = (
        jnp.einsum("bthd,bnuhd->bhtnu", query_stack, key_stack, preferred_element_type=jnp.float32)
        * scale_factor
    )
    scores = jnp.where(allowed, raw_scores, -1e30)
    row_peak = jnp.max(scores, axis=(3, 4), keepdims=True)
    summed = jnp.sum(jnp.exp(scores - row_peak), axis=(3, 4), keepdims=True)
    log_total = row_peak + jnp.log(summed)
    weights32 = jnp.exp(scores - log_total)
    weights = rounded(weights32)
    output = rounded(
        jnp.einsum("bhtnu,bnuhd->bthd", weights, value_stack, preferred_element_type=jnp.float32)
    )
    grad_probs = jnp.einsum(
        "bthd,bnuhd->bhtnu", grad_stack, value_stack, preferred_element_type=jnp.float32
    )
    delta_rows = jnp.sum(grad_stack.astype(jnp.float32) * output.astype(jnp.float32), axis=-1)
    delta_rows = jnp.transpose(delta_rows, (0, 2, 1))[:, :, :, None, None]
    grad_scores = rounded(weights32 * (grad_probs - delta_rows) * scale_factor)
    query_grad = jnp.einsum(
        "bhtnu,bnuhd->bthd", grad_scores, key_stack, preferred_element_type=jnp.float32
    )
    key_terms = jnp.einsum(
        "bhtnu,bthd->bnuhd", grad_scores, query_stack, preferred_element_type=jnp.float32
    )
    value_terms = jnp.einsum(
        "bhtnu,bthd->bnuhd", weights, grad_stack, preferred_element_type=jnp.float32
    )
    own = (rounded(key_terms[0, 0]), rounded(value_terms[0, 0]))
    outgoing = [
        jnp.stack([key_terms[0, slot_index], value_terms[0, slot_index]]).astype(jnp.bfloat16)
        for slot_index in range(1, len(offsets) + 1)
    ]
    return output, query_grad, own, outgoing, log_total


def gather_back(own, outgoing, offsets):
    key_accum = own[0].astype(jnp.float32)
    value_accum = own[1].astype(jnp.float32)
    for parts, offset in zip(outgoing, offsets):
        returned = from_behind(parts, "ctx", -offset)
        key_accum = key_accum + returned[0].astype(jnp.float32)
        value_accum = value_accum + returned[1].astype(jnp.float32)
    return key_accum, value_accum


def on_device(queries, key_vectors, values, grad_out, file_lengths, reach_table):
    local_rows = queries.shape[0]
    width_all = queries.shape[1]
    per_shard = local_rows // BLOCK
    ctx_size = lax.axis_size("ctx")
    levels = (per_shard * ctx_size - 1).bit_length()
    offsets = [2**level_index for level_index in range(levels)]
    shard_index = lax.axis_index("ctx")
    global_rows = shard_index * local_rows + jnp.arange(local_rows, dtype=jnp.int32)
    positions = file_positions(file_lengths, global_rows)
    query_rot = rounded(rotary(queries, positions, HEADS, HEAD_DIM, False))
    key_rot = rounded(rotary(key_vectors, positions, HEADS, HEAD_DIM, False))
    valid_slots = reach_mask(reach_table, shard_index * per_shard, per_shard, levels)
    allowed = score_mask(valid_slots, BLOCK)
    chunk_heads = HEADS // CHUNKS
    chunk_width = chunk_heads * HEAD_DIM
    columns = [slice(chunk * chunk_width, (chunk + 1) * chunk_width) for chunk in range(CHUNKS)]
    pieces = []
    pending = []
    for chunk, cols in enumerate(columns):
        key_c, value_c = key_rot[:, cols], values[:, cols]
        if pending:
            key_c, value_c, _ = lax.optimization_barrier((key_c, value_c, statistics))
        received = send_chunk(key_c, value_c, offsets)
        output, query_grad, own, outgoing, log_total = attend_chunk(
            query_rot[:, cols], received, grad_out[:, cols], allowed, offsets, chunk_heads
        )
        pending.append(outgoing)
        statistics = log_total
        key_accum_c, value_accum_c = gather_back(own, outgoing, offsets)
        rows = query_rot.shape[0]
        pieces.append(
            (
                output.reshape(rows, chunk_width),
                query_grad.reshape(rows, chunk_width),
                key_accum_c.reshape(rows, chunk_width),
                value_accum_c.reshape(rows, chunk_width),
            )
        )
    attended, query_grad, key_accum, value_accum = [
        jnp.concatenate(parts, axis=1) for parts in zip(*pieces)
    ]
    grad_queries = rotary(query_grad, positions, HEADS, HEAD_DIM, True).astype(jnp.bfloat16)
    grad_keys = rotary(key_accum, positions, HEADS, HEAD_DIM, True).astype(jnp.bfloat16)
    grad_values = value_accum.astype(jnp.bfloat16)
    return (attended, grad_queries, grad_keys, grad_values)


def solution(mesh):
    placed = (
        P(("groups", "ctx"), None),
        P(("groups", "ctx"), None),
        P(("groups", "ctx"), None),
        P(("groups", "ctx"), None),
        P("groups"),
        P(("groups", "ctx")),
    )
    return jax.shard_map(
        on_device,
        mesh=mesh,
        in_specs=placed,
        out_specs=(
            P(("groups", "ctx"), None),
            P(("groups", "ctx"), None),
            P(("groups", "ctx"), None),
            P(("groups", "ctx"), None),
        ),
        check_vma=False,
    )
```

```python
import math

import jax
import jax.numpy as jnp
from jax import lax
from jax.experimental import pallas as pl
from jax.sharding import PartitionSpec as P

HEADS = 16
HEAD_DIM = 128
BLOCK = 128
CHUNKS = 2


def from_behind(value, axis, steps):
    count = lax.axis_size(axis)
    leading, last = (max(0, -steps), min(count, count - steps))
    return lax.ppermute(value, axis, [(source, source + steps) for source in range(leading, last)])


def rounded(matrix):
    return lax.optimization_barrier(matrix.astype(jnp.bfloat16))


def file_positions(file_lengths, global_rows):
    file_ends = jnp.cumsum(file_lengths)
    starts = file_ends - file_lengths
    owned_mask = starts[None, :] <= global_rows[:, None]
    latest = jnp.max(jnp.where(owned_mask, starts[None, :], 0), axis=1)
    return global_rows - latest


def rotary(matrix, positions, head_count, head_width, inverse):
    half_width = head_width // 2
    exponent = jnp.arange(half_width, dtype=jnp.float32) * (2.0 / head_width)
    frequency = jnp.exp(exponent * -math.log(10000.0))
    angles = positions.astype(jnp.float32)[:, None] * frequency[None, :]
    cosine = jnp.cos(angles)[:, None, :]
    sine_table = jnp.sin(angles)[:, None, :]
    shaped = matrix.astype(jnp.float32).reshape(matrix.shape[0], head_count, head_width)
    former = shaped[..., :half_width]
    latter = shaped[..., half_width:]
    if inverse:
        turned = jnp.concatenate(
            [former * cosine + latter * sine_table, latter * cosine - former * sine_table], axis=-1
        )
    else:
        turned = jnp.concatenate(
            [former * cosine - latter * sine_table, latter * cosine + former * sine_table], axis=-1
        )
    return turned.reshape(matrix.shape[0], head_count * head_width)


def reach_mask(reach_rows, first_block, per_shard, levels):
    block_ids = first_block + jnp.arange(per_shard, dtype=jnp.int32)
    level_ids = jnp.arange(levels, dtype=jnp.int32)
    distances = jnp.array([2**level_index for level_index in range(levels)], dtype=jnp.int32)
    reached = (level_ids[None, :] < reach_rows[:, None]) & (
        block_ids[:, None] - distances[None, :] >= 0
    )
    return jnp.concatenate([jnp.ones((per_shard, 1), dtype=bool), reached], axis=1)


def score_mask(valid_slots, block_rows):
    row_ids = jnp.arange(block_rows)
    causal = row_ids[None, :] <= row_ids[:, None]
    first_slot = jnp.arange(valid_slots.shape[1]) == 0
    inside = jnp.where(first_slot[:, None, None], causal[None], True)
    allowed = inside[None] & valid_slots[:, :, None, None]
    return jnp.transpose(allowed, (0, 2, 1, 3))[:, None]


def send_chunk(key_c, value_c, offsets):
    pair = jnp.stack([key_c, value_c])
    received = {0: pair}
    for offset in offsets:
        if (offset.bit_length() - 1) % 2 == 1:
            half = offset // 2
            received[offset] = from_behind(received[half], "ctx", half)
        else:
            received[offset] = from_behind(pair, "ctx", offset)
    return [received[0]] + [received[offset] for offset in offsets]


def attention_kernel(*refs):
    slots = (len(refs) - 5) // 2
    query_ref, grad_ref, mask_ref = refs[0], refs[1], refs[2]
    pair_refs = refs[3 : 3 + slots]
    out_ref, qgrad_ref = refs[3 + slots], refs[4 + slots]
    part_refs = refs[5 + slots :]
    scale_factor = 1.0 / math.sqrt(HEAD_DIM)
    query = query_ref[...]
    grad = grad_ref[...]
    keys = jnp.concatenate([ref[0] for ref in pair_refs], axis=0)
    vals = jnp.concatenate([ref[1] for ref in pair_refs], axis=0)
    last = (((1,), (1,)), ((), ()))
    first = (((0,), (0,)), ((), ()))
    raw = lax.dot_general(query, keys, last, preferred_element_type=jnp.float32)
    scores = jnp.where(mask_ref[...] > 0, raw * scale_factor, -1e30)
    row_peak = jnp.max(scores, axis=1, keepdims=True)
    summed = jnp.sum(jnp.exp(scores - row_peak), axis=1, keepdims=True)
    log_total = row_peak + jnp.log(summed)
    weights32 = jnp.exp(scores - log_total)
    weights = weights32.astype(jnp.bfloat16)
    output = jnp.dot(weights, vals, preferred_element_type=jnp.float32).astype(jnp.bfloat16)
    out_ref[...] = output
    grad_probs = lax.dot_general(grad, vals, last, preferred_element_type=jnp.float32)
    delta = jnp.sum(grad.astype(jnp.float32) * output.astype(jnp.float32), axis=1, keepdims=True)
    grad_scores = (weights32 * (grad_probs - delta) * scale_factor).astype(jnp.bfloat16)
    qgrad_ref[...] = jnp.dot(grad_scores, keys, preferred_element_type=jnp.float32)
    key_terms = lax.dot_general(grad_scores, query, first, preferred_element_type=jnp.float32)
    value_terms = lax.dot_general(weights, grad, first, preferred_element_type=jnp.float32)
    rows = query.shape[0]
    for slot, ref in enumerate(part_refs):
        ref[0] = key_terms[slot * rows : (slot + 1) * rows].astype(jnp.bfloat16)
        ref[1] = value_terms[slot * rows : (slot + 1) * rows].astype(jnp.bfloat16)


def attend_chunk_kernel(query_c, received, grad_c, allowed, offsets, heads):
    rows, width = query_c.shape
    slots = len(received)
    mask = jnp.where(allowed, 1.0, 0.0).astype(jnp.float32).reshape(rows, slots * rows)
    flat_spec = pl.BlockSpec((rows, HEAD_DIM), lambda h: (0, h))
    pair_spec = pl.BlockSpec((2, rows, HEAD_DIM), lambda h: (0, 0, h))
    mask_spec = pl.BlockSpec((rows, slots * rows), lambda h: (0, 0))
    pair_shape = jax.ShapeDtypeStruct((2, rows, width), jnp.bfloat16)
    results = pl.pallas_call(
        attention_kernel,
        grid=(heads,),
        in_specs=[flat_spec, flat_spec, mask_spec] + [pair_spec] * slots,
        out_specs=[flat_spec, flat_spec] + [pair_spec] * slots,
        out_shape=[
            jax.ShapeDtypeStruct((rows, width), jnp.bfloat16),
            jax.ShapeDtypeStruct((rows, width), jnp.float32),
        ]
        + [pair_shape] * slots,
    )(query_c, grad_c, mask, *received)
    output, query_grad = results[0], results[1]
    own = (results[2][0], results[2][1])
    outgoing = list(results[3:])
    return output, query_grad, own, outgoing


def attend_chunk(query_c, received, grad_c, allowed, offsets, heads):
    scale_factor = 1.0 / math.sqrt(HEAD_DIM)
    rows = query_c.shape[0]
    head_shape = (rows, heads, HEAD_DIM)
    key_stack = jnp.stack([moved[0].reshape(head_shape) for moved in received])[None]
    value_stack = jnp.stack([moved[1].reshape(head_shape) for moved in received])[None]
    query_stack = query_c.reshape((1,) + head_shape)
    grad_stack = grad_c.reshape((1,) + head_shape)
    raw_scores = (
        jnp.einsum("bthd,bnuhd->bhtnu", query_stack, key_stack, preferred_element_type=jnp.float32)
        * scale_factor
    )
    scores = jnp.where(allowed, raw_scores, -1e30)
    row_peak = jnp.max(scores, axis=(3, 4), keepdims=True)
    summed = jnp.sum(jnp.exp(scores - row_peak), axis=(3, 4), keepdims=True)
    log_total = row_peak + jnp.log(summed)
    weights32 = jnp.exp(scores - log_total)
    weights = rounded(weights32)
    output = rounded(
        jnp.einsum("bhtnu,bnuhd->bthd", weights, value_stack, preferred_element_type=jnp.float32)
    )
    grad_probs = jnp.einsum(
        "bthd,bnuhd->bhtnu", grad_stack, value_stack, preferred_element_type=jnp.float32
    )
    delta_rows = jnp.sum(grad_stack.astype(jnp.float32) * output.astype(jnp.float32), axis=-1)
    delta_rows = jnp.transpose(delta_rows, (0, 2, 1))[:, :, :, None, None]
    grad_scores = rounded(weights32 * (grad_probs - delta_rows) * scale_factor)
    query_grad = jnp.einsum(
        "bhtnu,bnuhd->bthd", grad_scores, key_stack, preferred_element_type=jnp.float32
    )
    key_terms = jnp.einsum(
        "bhtnu,bthd->bnuhd", grad_scores, query_stack, preferred_element_type=jnp.float32
    )
    value_terms = jnp.einsum(
        "bhtnu,bthd->bnuhd", weights, grad_stack, preferred_element_type=jnp.float32
    )
    own = (rounded(key_terms[0, 0]), rounded(value_terms[0, 0]))
    outgoing = [
        jnp.stack([key_terms[0, slot_index], value_terms[0, slot_index]]).astype(jnp.bfloat16)
        for slot_index in range(1, len(offsets) + 1)
    ]
    return output, query_grad, own, outgoing


def gather_back(own, outgoing, offsets):
    key_accum = own[0].astype(jnp.float32)
    value_accum = own[1].astype(jnp.float32)
    for parts, offset in zip(outgoing, offsets):
        returned = from_behind(parts, "ctx", -offset)
        key_accum = key_accum + returned[0].astype(jnp.float32)
        value_accum = value_accum + returned[1].astype(jnp.float32)
    return key_accum, value_accum


def on_device(queries, key_vectors, values, grad_out, file_lengths, reach_table):
    local_rows = queries.shape[0]
    width_all = queries.shape[1]
    per_shard = local_rows // BLOCK
    ctx_size = lax.axis_size("ctx")
    levels = (per_shard * ctx_size - 1).bit_length()
    offsets = [2**level_index for level_index in range(levels)]
    shard_index = lax.axis_index("ctx")
    global_rows = shard_index * local_rows + jnp.arange(local_rows, dtype=jnp.int32)
    positions = file_positions(file_lengths, global_rows)
    query_rot = rounded(rotary(queries, positions, HEADS, HEAD_DIM, False))
    key_rot = rounded(rotary(key_vectors, positions, HEADS, HEAD_DIM, False))
    valid_slots = reach_mask(reach_table, shard_index * per_shard, per_shard, levels)
    allowed = score_mask(valid_slots, BLOCK)
    chunk_heads = HEADS // CHUNKS
    chunk_width = chunk_heads * HEAD_DIM
    columns = [slice(chunk * chunk_width, (chunk + 1) * chunk_width) for chunk in range(CHUNKS)]
    pieces = []
    pending = []
    for chunk, cols in enumerate(columns):
        key_c, value_c = key_rot[:, cols], values[:, cols]
        if pending:
            key_c, value_c, _ = lax.optimization_barrier((key_c, value_c, pieces[-1][0]))
        received = send_chunk(key_c, value_c, offsets)
        attend = attend_chunk_kernel if chunk == CHUNKS - 1 else attend_chunk
        output, query_grad, own, outgoing = attend(
            query_rot[:, cols], received, grad_out[:, cols], allowed, offsets, chunk_heads
        )
        pending.append(outgoing)
        key_accum_c, value_accum_c = gather_back(own, outgoing, offsets)
        rows = query_rot.shape[0]
        pieces.append(
            (
                output.reshape(rows, chunk_width),
                query_grad.reshape(rows, chunk_width),
                key_accum_c.reshape(rows, chunk_width),
                value_accum_c.reshape(rows, chunk_width),
            )
        )
    attended, query_grad, key_accum, value_accum = [
        jnp.concatenate(parts, axis=1) for parts in zip(*pieces)
    ]
    grad_queries = rotary(query_grad, positions, HEADS, HEAD_DIM, True).astype(jnp.bfloat16)
    grad_keys = rotary(key_accum, positions, HEADS, HEAD_DIM, True).astype(jnp.bfloat16)
    grad_values = value_accum.astype(jnp.bfloat16)
    return (attended, grad_queries, grad_keys, grad_values)


def solution(mesh):
    placed = (
        P(("groups", "ctx"), None),
        P(("groups", "ctx"), None),
        P(("groups", "ctx"), None),
        P(("groups", "ctx"), None),
        P("groups"),
        P(("groups", "ctx")),
    )
    return jax.shard_map(
        on_device,
        mesh=mesh,
        in_specs=placed,
        out_specs=(
            P(("groups", "ctx"), None),
            P(("groups", "ctx"), None),
            P(("groups", "ctx"), None),
            P(("groups", "ctx"), None),
        ),
        check_vma=False,
    )
```

```python
import math

import jax
import jax.numpy as jnp
from jax import lax
from jax.sharding import PartitionSpec as P

HEADS = 16
HEAD_DIM = 128
BLOCK = 128
CHUNKS = 2


def from_behind(value, axis, steps):
    count = lax.axis_size(axis)
    leading, last = (max(0, -steps), min(count, count - steps))
    return lax.ppermute(value, axis, [(source, source + steps) for source in range(leading, last)])


def rounded(matrix):
    return lax.optimization_barrier(matrix.astype(jnp.bfloat16))


def file_positions(file_lengths, global_rows):
    file_ends = jnp.cumsum(file_lengths)
    starts = file_ends - file_lengths
    owned_mask = starts[None, :] <= global_rows[:, None]
    latest = jnp.max(jnp.where(owned_mask, starts[None, :], 0), axis=1)
    return global_rows - latest


def rotary(matrix, positions, head_count, head_width, inverse):
    half_width = head_width // 2
    exponent = jnp.arange(half_width, dtype=jnp.float32) * (2.0 / head_width)
    frequency = jnp.exp(exponent * -math.log(10000.0))
    angles = positions.astype(jnp.float32)[:, None] * frequency[None, :]
    cosine = jnp.cos(angles)[:, None, :]
    sine_table = jnp.sin(angles)[:, None, :]
    shaped = matrix.astype(jnp.float32).reshape(matrix.shape[0], head_count, head_width)
    former = shaped[..., :half_width]
    latter = shaped[..., half_width:]
    if inverse:
        turned = jnp.concatenate(
            [former * cosine + latter * sine_table, latter * cosine - former * sine_table], axis=-1
        )
    else:
        turned = jnp.concatenate(
            [former * cosine - latter * sine_table, latter * cosine + former * sine_table], axis=-1
        )
    return turned.reshape(matrix.shape[0], head_count * head_width)


def reach_mask(reach_rows, first_block, per_shard, levels):
    block_ids = first_block + jnp.arange(per_shard, dtype=jnp.int32)
    level_ids = jnp.arange(levels, dtype=jnp.int32)
    distances = jnp.array([2**level_index for level_index in range(levels)], dtype=jnp.int32)
    reached = (level_ids[None, :] < reach_rows[:, None]) & (
        block_ids[:, None] - distances[None, :] >= 0
    )
    return jnp.concatenate([jnp.ones((per_shard, 1), dtype=bool), reached], axis=1)


def score_mask(valid_slots, block_rows):
    row_ids = jnp.arange(block_rows)
    causal = row_ids[None, :] <= row_ids[:, None]
    first_slot = jnp.arange(valid_slots.shape[1]) == 0
    inside = jnp.where(first_slot[:, None, None], causal[None], True)
    allowed = inside[None] & valid_slots[:, :, None, None]
    return jnp.transpose(allowed, (0, 2, 1, 3))[:, None]


def send_chunk(key_c, value_c, offsets, relay):
    pair = jnp.stack([key_c, value_c])
    received = {0: pair}
    for offset in offsets:
        if relay and (offset.bit_length() - 1) % 2 == 1:
            half = offset // 2
            received[offset] = from_behind(received[half], "ctx", half)
        else:
            received[offset] = from_behind(pair, "ctx", offset)
    return [received[0]] + [received[offset] for offset in offsets]


def attend_chunk(query_c, received, grad_c, allowed, offsets, heads):
    scale_factor = 1.0 / math.sqrt(HEAD_DIM)
    rows = query_c.shape[0]
    head_shape = (rows, heads, HEAD_DIM)
    key_stack = jnp.stack([moved[0].reshape(head_shape) for moved in received])[None]
    value_stack = jnp.stack([moved[1].reshape(head_shape) for moved in received])[None]
    query_stack = query_c.reshape((1,) + head_shape)
    grad_stack = grad_c.reshape((1,) + head_shape)
    raw_scores = (
        jnp.einsum("bthd,bnuhd->bhtnu", query_stack, key_stack, preferred_element_type=jnp.float32)
        * scale_factor
    )
    scores = jnp.where(allowed, raw_scores, -1e30)
    row_peak = jnp.max(scores, axis=(3, 4), keepdims=True)
    summed = jnp.sum(jnp.exp(scores - row_peak), axis=(3, 4), keepdims=True)
    log_total = row_peak + jnp.log(summed)
    weights32 = jnp.exp(scores - log_total)
    weights = rounded(weights32)
    output = rounded(
        jnp.einsum("bhtnu,bnuhd->bthd", weights, value_stack, preferred_element_type=jnp.float32)
    )
    grad_probs = jnp.einsum(
        "bthd,bnuhd->bhtnu", grad_stack, value_stack, preferred_element_type=jnp.float32
    )
    delta_rows = jnp.sum(grad_stack.astype(jnp.float32) * output.astype(jnp.float32), axis=-1)
    delta_rows = jnp.transpose(delta_rows, (0, 2, 1))[:, :, :, None, None]
    grad_scores = rounded(weights32 * (grad_probs - delta_rows) * scale_factor)
    query_grad = jnp.einsum(
        "bhtnu,bnuhd->bthd", grad_scores, key_stack, preferred_element_type=jnp.float32
    )
    key_terms = jnp.einsum(
        "bhtnu,bthd->bnuhd", grad_scores, query_stack, preferred_element_type=jnp.float32
    )
    value_terms = jnp.einsum(
        "bhtnu,bthd->bnuhd", weights, grad_stack, preferred_element_type=jnp.float32
    )
    own = (rounded(key_terms[0, 0]), rounded(value_terms[0, 0]))
    outgoing = [
        jnp.stack([key_terms[0, slot_index], value_terms[0, slot_index]]).astype(jnp.bfloat16)
        for slot_index in range(1, len(offsets) + 1)
    ]
    return output, query_grad, own, outgoing


def gather_back(own, outgoing, offsets):
    key_accum = own[0].astype(jnp.float32)
    value_accum = own[1].astype(jnp.float32)
    for parts, offset in zip(outgoing, offsets):
        returned = from_behind(parts, "ctx", -offset)
        key_accum = key_accum + returned[0].astype(jnp.float32)
        value_accum = value_accum + returned[1].astype(jnp.float32)
    return key_accum, value_accum


def on_device(queries, key_vectors, values, grad_out, file_lengths, reach_table):
    local_rows = queries.shape[0]
    width_all = queries.shape[1]
    per_shard = local_rows // BLOCK
    ctx_size = lax.axis_size("ctx")
    levels = (per_shard * ctx_size - 1).bit_length()
    offsets = [2**level_index for level_index in range(levels)]
    shard_index = lax.axis_index("ctx")
    global_rows = shard_index * local_rows + jnp.arange(local_rows, dtype=jnp.int32)
    positions = file_positions(file_lengths, global_rows)
    query_rot = rounded(rotary(queries, positions, HEADS, HEAD_DIM, False))
    key_rot = rounded(rotary(key_vectors, positions, HEADS, HEAD_DIM, False))
    valid_slots = reach_mask(reach_table, shard_index * per_shard, per_shard, levels)
    allowed = score_mask(valid_slots, BLOCK)
    chunk_heads = HEADS // CHUNKS
    chunk_width = chunk_heads * HEAD_DIM
    columns = [slice(chunk * chunk_width, (chunk + 1) * chunk_width) for chunk in range(CHUNKS)]
    pieces = []
    pending = []
    for chunk, cols in enumerate(columns):
        key_c, value_c = key_rot[:, cols], values[:, cols]
        if pending:
            key_c, value_c, _ = lax.optimization_barrier((key_c, value_c, pieces[-1][0]))
        received = send_chunk(key_c, value_c, offsets, relay=not pending)
        output, query_grad, own, outgoing = attend_chunk(
            query_rot[:, cols], received, grad_out[:, cols], allowed, offsets, chunk_heads
        )
        pending.append(outgoing)
        key_accum_c, value_accum_c = gather_back(own, outgoing, offsets)
        rows = query_rot.shape[0]
        pieces.append(
            (
                output.reshape(rows, chunk_width),
                query_grad.reshape(rows, chunk_width),
                key_accum_c.reshape(rows, chunk_width),
                value_accum_c.reshape(rows, chunk_width),
            )
        )
    attended, query_grad, key_accum, value_accum = [
        jnp.concatenate(parts, axis=1) for parts in zip(*pieces)
    ]
    grad_queries = rotary(query_grad, positions, HEADS, HEAD_DIM, True).astype(jnp.bfloat16)
    grad_keys = rotary(key_accum, positions, HEADS, HEAD_DIM, True).astype(jnp.bfloat16)
    grad_values = value_accum.astype(jnp.bfloat16)
    return (attended, grad_queries, grad_keys, grad_values)


def solution(mesh):
    placed = (
        P(("groups", "ctx"), None),
        P(("groups", "ctx"), None),
        P(("groups", "ctx"), None),
        P(("groups", "ctx"), None),
        P("groups"),
        P(("groups", "ctx")),
    )
    return jax.shard_map(
        on_device,
        mesh=mesh,
        in_specs=placed,
        out_specs=(
            P(("groups", "ctx"), None),
            P(("groups", "ctx"), None),
            P(("groups", "ctx"), None),
            P(("groups", "ctx"), None),
        ),
        check_vma=False,
    )
```

```python
import math

import jax
import jax.numpy as jnp
from jax import lax
from jax.sharding import PartitionSpec as P

HEADS = 16
HEAD_DIM = 128
BLOCK = 128
CHUNKS = 2


def from_behind(value, axis, steps):
    count = lax.axis_size(axis)
    leading, last = (max(0, -steps), min(count, count - steps))
    return lax.ppermute(value, axis, [(source, source + steps) for source in range(leading, last)])


def rounded(matrix):
    return lax.optimization_barrier(matrix.astype(jnp.bfloat16))


def file_positions(file_lengths, global_rows):
    file_ends = jnp.cumsum(file_lengths)
    starts = file_ends - file_lengths
    owned_mask = starts[None, :] <= global_rows[:, None]
    latest = jnp.max(jnp.where(owned_mask, starts[None, :], 0), axis=1)
    return global_rows - latest


def rotary(matrix, positions, head_count, head_width, inverse):
    half_width = head_width // 2
    exponent = jnp.arange(half_width, dtype=jnp.float32) * (2.0 / head_width)
    frequency = jnp.exp(exponent * -math.log(10000.0))
    angles = positions.astype(jnp.float32)[:, None] * frequency[None, :]
    cosine = jnp.cos(angles)[:, None, :]
    sine_table = jnp.sin(angles)[:, None, :]
    shaped = matrix.astype(jnp.float32).reshape(matrix.shape[0], head_count, head_width)
    former = shaped[..., :half_width]
    latter = shaped[..., half_width:]
    if inverse:
        turned = jnp.concatenate(
            [former * cosine + latter * sine_table, latter * cosine - former * sine_table], axis=-1
        )
    else:
        turned = jnp.concatenate(
            [former * cosine - latter * sine_table, latter * cosine + former * sine_table], axis=-1
        )
    return turned.reshape(matrix.shape[0], head_count * head_width)


def reach_mask(reach_rows, first_block, per_shard, levels):
    block_ids = first_block + jnp.arange(per_shard, dtype=jnp.int32)
    level_ids = jnp.arange(levels, dtype=jnp.int32)
    distances = jnp.array([2**level_index for level_index in range(levels)], dtype=jnp.int32)
    reached = (level_ids[None, :] < reach_rows[:, None]) & (
        block_ids[:, None] - distances[None, :] >= 0
    )
    return jnp.concatenate([jnp.ones((per_shard, 1), dtype=bool), reached], axis=1)


def score_mask(valid_slots, block_rows):
    row_ids = jnp.arange(block_rows)
    causal = row_ids[None, :] <= row_ids[:, None]
    first_slot = jnp.arange(valid_slots.shape[1]) == 0
    inside = jnp.where(first_slot[:, None, None], causal[None], True)
    allowed = inside[None] & valid_slots[:, :, None, None]
    return jnp.transpose(allowed, (0, 2, 1, 3))[:, None]


def send_chunk(key_c, value_c, offsets, relay):
    pair = jnp.stack([key_c, value_c])
    received = {0: pair}
    for offset in offsets:
        if relay and offset >= 8 and (offset.bit_length() - 1) % 2 == 1:
            half = offset // 2
            received[offset] = from_behind(received[half], "ctx", half)
        else:
            received[offset] = from_behind(pair, "ctx", offset)
    return [received[0]] + [received[offset] for offset in offsets]


def attend_chunk(query_c, received, grad_c, allowed, offsets, heads):
    scale_factor = 1.0 / math.sqrt(HEAD_DIM)
    rows = query_c.shape[0]
    head_shape = (rows, heads, HEAD_DIM)
    key_stack = jnp.stack([moved[0].reshape(head_shape) for moved in received])[None]
    value_stack = jnp.stack([moved[1].reshape(head_shape) for moved in received])[None]
    query_stack = query_c.reshape((1,) + head_shape)
    grad_stack = grad_c.reshape((1,) + head_shape)
    raw_scores = (
        jnp.einsum("bthd,bnuhd->bhtnu", query_stack, key_stack, preferred_element_type=jnp.float32)
        * scale_factor
    )
    scores = jnp.where(allowed, raw_scores, -1e30)
    row_peak = jnp.max(scores, axis=(3, 4), keepdims=True)
    summed = jnp.sum(jnp.exp(scores - row_peak), axis=(3, 4), keepdims=True)
    log_total = row_peak + jnp.log(summed)
    weights32 = jnp.exp(scores - log_total)
    weights = rounded(weights32)
    output = rounded(
        jnp.einsum("bhtnu,bnuhd->bthd", weights, value_stack, preferred_element_type=jnp.float32)
    )
    grad_probs = jnp.einsum(
        "bthd,bnuhd->bhtnu", grad_stack, value_stack, preferred_element_type=jnp.float32
    )
    delta_rows = jnp.sum(grad_stack.astype(jnp.float32) * output.astype(jnp.float32), axis=-1)
    delta_rows = jnp.transpose(delta_rows, (0, 2, 1))[:, :, :, None, None]
    grad_scores = rounded(weights32 * (grad_probs - delta_rows) * scale_factor)
    query_grad = jnp.einsum(
        "bhtnu,bnuhd->bthd", grad_scores, key_stack, preferred_element_type=jnp.float32
    )
    key_terms = jnp.einsum(
        "bhtnu,bthd->bnuhd", grad_scores, query_stack, preferred_element_type=jnp.float32
    )
    value_terms = jnp.einsum(
        "bhtnu,bthd->bnuhd", weights, grad_stack, preferred_element_type=jnp.float32
    )
    own = (rounded(key_terms[0, 0]), rounded(value_terms[0, 0]))
    outgoing = [
        jnp.stack([key_terms[0, slot_index], value_terms[0, slot_index]]).astype(jnp.bfloat16)
        for slot_index in range(1, len(offsets) + 1)
    ]
    return output, query_grad, own, outgoing


def gather_back(own, outgoing, offsets):
    key_accum = own[0].astype(jnp.float32)
    value_accum = own[1].astype(jnp.float32)
    for parts, offset in zip(outgoing, offsets):
        returned = from_behind(parts, "ctx", -offset)
        key_accum = key_accum + returned[0].astype(jnp.float32)
        value_accum = value_accum + returned[1].astype(jnp.float32)
    return key_accum, value_accum


def on_device(queries, key_vectors, values, grad_out, file_lengths, reach_table):
    local_rows = queries.shape[0]
    width_all = queries.shape[1]
    per_shard = local_rows // BLOCK
    ctx_size = lax.axis_size("ctx")
    levels = (per_shard * ctx_size - 1).bit_length()
    offsets = [2**level_index for level_index in range(levels)]
    shard_index = lax.axis_index("ctx")
    global_rows = shard_index * local_rows + jnp.arange(local_rows, dtype=jnp.int32)
    positions = file_positions(file_lengths, global_rows)
    query_rot = rounded(rotary(queries, positions, HEADS, HEAD_DIM, False))
    key_rot = rounded(rotary(key_vectors, positions, HEADS, HEAD_DIM, False))
    valid_slots = reach_mask(reach_table, shard_index * per_shard, per_shard, levels)
    allowed = score_mask(valid_slots, BLOCK)
    chunk_heads = HEADS // CHUNKS
    chunk_width = chunk_heads * HEAD_DIM
    columns = [slice(chunk * chunk_width, (chunk + 1) * chunk_width) for chunk in range(CHUNKS)]
    pieces = []
    pending = []
    for chunk, cols in enumerate(columns):
        key_c, value_c = key_rot[:, cols], values[:, cols]
        if pending:
            key_c, value_c, _ = lax.optimization_barrier((key_c, value_c, pieces[-1][0]))
        received = send_chunk(key_c, value_c, offsets, relay=not pending)
        output, query_grad, own, outgoing = attend_chunk(
            query_rot[:, cols], received, grad_out[:, cols], allowed, offsets, chunk_heads
        )
        pending.append(outgoing)
        key_accum_c, value_accum_c = gather_back(own, outgoing, offsets)
        rows = query_rot.shape[0]
        pieces.append(
            (
                output.reshape(rows, chunk_width),
                query_grad.reshape(rows, chunk_width),
                key_accum_c.reshape(rows, chunk_width),
                value_accum_c.reshape(rows, chunk_width),
            )
        )
    attended, query_grad, key_accum, value_accum = [
        jnp.concatenate(parts, axis=1) for parts in zip(*pieces)
    ]
    grad_queries = rotary(query_grad, positions, HEADS, HEAD_DIM, True).astype(jnp.bfloat16)
    grad_keys = rotary(key_accum, positions, HEADS, HEAD_DIM, True).astype(jnp.bfloat16)
    grad_values = value_accum.astype(jnp.bfloat16)
    return (attended, grad_queries, grad_keys, grad_values)


def solution(mesh):
    placed = (
        P(("groups", "ctx"), None),
        P(("groups", "ctx"), None),
        P(("groups", "ctx"), None),
        P(("groups", "ctx"), None),
        P("groups"),
        P(("groups", "ctx")),
    )
    return jax.shard_map(
        on_device,
        mesh=mesh,
        in_specs=placed,
        out_specs=(
            P(("groups", "ctx"), None),
            P(("groups", "ctx"), None),
            P(("groups", "ctx"), None),
            P(("groups", "ctx"), None),
        ),
        check_vma=False,
    )
```

```python
import math

import jax
import jax.numpy as jnp
from jax import lax
from jax.sharding import PartitionSpec as P

HEADS = 16
HEAD_DIM = 128
BLOCK = 128
CHUNK_HEADS = (6, 10)


def from_behind(value, axis, steps):
    count = lax.axis_size(axis)
    leading, last = (max(0, -steps), min(count, count - steps))
    return lax.ppermute(value, axis, [(source, source + steps) for source in range(leading, last)])


def rounded(matrix):
    return lax.optimization_barrier(matrix.astype(jnp.bfloat16))


def file_positions(file_lengths, global_rows):
    file_ends = jnp.cumsum(file_lengths)
    starts = file_ends - file_lengths
    owned_mask = starts[None, :] <= global_rows[:, None]
    latest = jnp.max(jnp.where(owned_mask, starts[None, :], 0), axis=1)
    return global_rows - latest


def rotary(matrix, positions, head_count, head_width, inverse):
    half_width = head_width // 2
    exponent = jnp.arange(half_width, dtype=jnp.float32) * (2.0 / head_width)
    frequency = jnp.exp(exponent * -math.log(10000.0))
    angles = positions.astype(jnp.float32)[:, None] * frequency[None, :]
    cosine = jnp.cos(angles)[:, None, :]
    sine_table = jnp.sin(angles)[:, None, :]
    shaped = matrix.astype(jnp.float32).reshape(matrix.shape[0], head_count, head_width)
    former = shaped[..., :half_width]
    latter = shaped[..., half_width:]
    if inverse:
        turned = jnp.concatenate(
            [former * cosine + latter * sine_table, latter * cosine - former * sine_table], axis=-1
        )
    else:
        turned = jnp.concatenate(
            [former * cosine - latter * sine_table, latter * cosine + former * sine_table], axis=-1
        )
    return turned.reshape(matrix.shape[0], head_count * head_width)


def reach_mask(reach_rows, first_block, per_shard, levels):
    block_ids = first_block + jnp.arange(per_shard, dtype=jnp.int32)
    level_ids = jnp.arange(levels, dtype=jnp.int32)
    distances = jnp.array([2**level_index for level_index in range(levels)], dtype=jnp.int32)
    reached = (level_ids[None, :] < reach_rows[:, None]) & (
        block_ids[:, None] - distances[None, :] >= 0
    )
    return jnp.concatenate([jnp.ones((per_shard, 1), dtype=bool), reached], axis=1)


def score_mask(valid_slots, block_rows):
    row_ids = jnp.arange(block_rows)
    causal = row_ids[None, :] <= row_ids[:, None]
    first_slot = jnp.arange(valid_slots.shape[1]) == 0
    inside = jnp.where(first_slot[:, None, None], causal[None], True)
    allowed = inside[None] & valid_slots[:, :, None, None]
    return jnp.transpose(allowed, (0, 2, 1, 3))[:, None]


def send_chunk(key_c, value_c, offsets, relay):
    pair = jnp.stack([key_c, value_c])
    received = {0: pair}
    for offset in offsets:
        if relay and (offset.bit_length() - 1) % 2 == 1:
            half = offset // 2
            received[offset] = from_behind(received[half], "ctx", half)
        else:
            received[offset] = from_behind(pair, "ctx", offset)
    return [received[0]] + [received[offset] for offset in offsets]


def attend_chunk(query_c, received, grad_c, allowed, offsets, heads):
    scale_factor = 1.0 / math.sqrt(HEAD_DIM)
    rows = query_c.shape[0]
    head_shape = (rows, heads, HEAD_DIM)
    key_stack = jnp.stack([moved[0].reshape(head_shape) for moved in received])[None]
    value_stack = jnp.stack([moved[1].reshape(head_shape) for moved in received])[None]
    query_stack = query_c.reshape((1,) + head_shape)
    grad_stack = grad_c.reshape((1,) + head_shape)
    raw_scores = (
        jnp.einsum("bthd,bnuhd->bhtnu", query_stack, key_stack, preferred_element_type=jnp.float32)
        * scale_factor
    )
    scores = jnp.where(allowed, raw_scores, -1e30)
    row_peak = jnp.max(scores, axis=(3, 4), keepdims=True)
    summed = jnp.sum(jnp.exp(scores - row_peak), axis=(3, 4), keepdims=True)
    log_total = row_peak + jnp.log(summed)
    weights32 = jnp.exp(scores - log_total)
    weights = rounded(weights32)
    output = rounded(
        jnp.einsum("bhtnu,bnuhd->bthd", weights, value_stack, preferred_element_type=jnp.float32)
    )
    grad_probs = jnp.einsum(
        "bthd,bnuhd->bhtnu", grad_stack, value_stack, preferred_element_type=jnp.float32
    )
    delta_rows = jnp.sum(grad_stack.astype(jnp.float32) * output.astype(jnp.float32), axis=-1)
    delta_rows = jnp.transpose(delta_rows, (0, 2, 1))[:, :, :, None, None]
    grad_scores = rounded(weights32 * (grad_probs - delta_rows) * scale_factor)
    query_grad = jnp.einsum(
        "bhtnu,bnuhd->bthd", grad_scores, key_stack, preferred_element_type=jnp.float32
    )
    key_terms = jnp.einsum(
        "bhtnu,bthd->bnuhd", grad_scores, query_stack, preferred_element_type=jnp.float32
    )
    value_terms = jnp.einsum(
        "bhtnu,bthd->bnuhd", weights, grad_stack, preferred_element_type=jnp.float32
    )
    own = (rounded(key_terms[0, 0]), rounded(value_terms[0, 0]))
    outgoing = [
        jnp.stack([key_terms[0, slot_index], value_terms[0, slot_index]]).astype(jnp.bfloat16)
        for slot_index in range(1, len(offsets) + 1)
    ]
    return output, query_grad, own, outgoing


def gather_back(own, outgoing, offsets):
    key_accum = own[0].astype(jnp.float32)
    value_accum = own[1].astype(jnp.float32)
    for parts, offset in zip(outgoing, offsets):
        returned = from_behind(parts, "ctx", -offset)
        key_accum = key_accum + returned[0].astype(jnp.float32)
        value_accum = value_accum + returned[1].astype(jnp.float32)
    return key_accum, value_accum


def on_device(queries, key_vectors, values, grad_out, file_lengths, reach_table):
    local_rows = queries.shape[0]
    width_all = queries.shape[1]
    per_shard = local_rows // BLOCK
    ctx_size = lax.axis_size("ctx")
    levels = (per_shard * ctx_size - 1).bit_length()
    offsets = [2**level_index for level_index in range(levels)]
    shard_index = lax.axis_index("ctx")
    global_rows = shard_index * local_rows + jnp.arange(local_rows, dtype=jnp.int32)
    positions = file_positions(file_lengths, global_rows)
    query_rot = rounded(rotary(queries, positions, HEADS, HEAD_DIM, False))
    key_rot = rounded(rotary(key_vectors, positions, HEADS, HEAD_DIM, False))
    valid_slots = reach_mask(reach_table, shard_index * per_shard, per_shard, levels)
    allowed = score_mask(valid_slots, BLOCK)
    bounds = [sum(CHUNK_HEADS[:chunk]) * HEAD_DIM for chunk in range(len(CHUNK_HEADS) + 1)]
    pieces = []
    pending = []
    for chunk, chunk_heads in enumerate(CHUNK_HEADS):
        chunk_width = chunk_heads * HEAD_DIM
        cols = slice(bounds[chunk], bounds[chunk + 1])
        key_c, value_c = key_rot[:, cols], values[:, cols]
        if pending:
            key_c, value_c, _ = lax.optimization_barrier((key_c, value_c, pieces[-1][0]))
        received = send_chunk(key_c, value_c, offsets, relay=not pending)
        output, query_grad, own, outgoing = attend_chunk(
            query_rot[:, cols], received, grad_out[:, cols], allowed, offsets, chunk_heads
        )
        pending.append(outgoing)
        key_accum_c, value_accum_c = gather_back(own, outgoing, offsets)
        rows = query_rot.shape[0]
        pieces.append(
            (
                output.reshape(rows, chunk_width),
                query_grad.reshape(rows, chunk_width),
                key_accum_c.reshape(rows, chunk_width),
                value_accum_c.reshape(rows, chunk_width),
            )
        )
    attended, query_grad, key_accum, value_accum = [
        jnp.concatenate(parts, axis=1) for parts in zip(*pieces)
    ]
    grad_queries = rotary(query_grad, positions, HEADS, HEAD_DIM, True).astype(jnp.bfloat16)
    grad_keys = rotary(key_accum, positions, HEADS, HEAD_DIM, True).astype(jnp.bfloat16)
    grad_values = value_accum.astype(jnp.bfloat16)
    return (attended, grad_queries, grad_keys, grad_values)


def solution(mesh):
    placed = (
        P(("groups", "ctx"), None),
        P(("groups", "ctx"), None),
        P(("groups", "ctx"), None),
        P(("groups", "ctx"), None),
        P("groups"),
        P(("groups", "ctx")),
    )
    return jax.shard_map(
        on_device,
        mesh=mesh,
        in_specs=placed,
        out_specs=(
            P(("groups", "ctx"), None),
            P(("groups", "ctx"), None),
            P(("groups", "ctx"), None),
            P(("groups", "ctx"), None),
        ),
        check_vma=False,
    )
```

```python
import math

import jax
import jax.numpy as jnp
from jax import lax
from jax.sharding import PartitionSpec as P

HEADS = 16
HEAD_DIM = 128
BLOCK = 128
CHUNK_HEADS = (8, 4, 4)


def from_behind(value, axis, steps):
    count = lax.axis_size(axis)
    leading, last = (max(0, -steps), min(count, count - steps))
    return lax.ppermute(value, axis, [(source, source + steps) for source in range(leading, last)])


def rounded(matrix):
    return lax.optimization_barrier(matrix.astype(jnp.bfloat16))


def file_positions(file_lengths, global_rows):
    file_ends = jnp.cumsum(file_lengths)
    starts = file_ends - file_lengths
    owned_mask = starts[None, :] <= global_rows[:, None]
    latest = jnp.max(jnp.where(owned_mask, starts[None, :], 0), axis=1)
    return global_rows - latest


def rotary(matrix, positions, head_count, head_width, inverse):
    half_width = head_width // 2
    exponent = jnp.arange(half_width, dtype=jnp.float32) * (2.0 / head_width)
    frequency = jnp.exp(exponent * -math.log(10000.0))
    angles = positions.astype(jnp.float32)[:, None] * frequency[None, :]
    cosine = jnp.cos(angles)[:, None, :]
    sine_table = jnp.sin(angles)[:, None, :]
    shaped = matrix.astype(jnp.float32).reshape(matrix.shape[0], head_count, head_width)
    former = shaped[..., :half_width]
    latter = shaped[..., half_width:]
    if inverse:
        turned = jnp.concatenate(
            [former * cosine + latter * sine_table, latter * cosine - former * sine_table], axis=-1
        )
    else:
        turned = jnp.concatenate(
            [former * cosine - latter * sine_table, latter * cosine + former * sine_table], axis=-1
        )
    return turned.reshape(matrix.shape[0], head_count * head_width)


def reach_mask(reach_rows, first_block, per_shard, levels):
    block_ids = first_block + jnp.arange(per_shard, dtype=jnp.int32)
    level_ids = jnp.arange(levels, dtype=jnp.int32)
    distances = jnp.array([2**level_index for level_index in range(levels)], dtype=jnp.int32)
    reached = (level_ids[None, :] < reach_rows[:, None]) & (
        block_ids[:, None] - distances[None, :] >= 0
    )
    return jnp.concatenate([jnp.ones((per_shard, 1), dtype=bool), reached], axis=1)


def score_mask(valid_slots, block_rows):
    row_ids = jnp.arange(block_rows)
    causal = row_ids[None, :] <= row_ids[:, None]
    first_slot = jnp.arange(valid_slots.shape[1]) == 0
    inside = jnp.where(first_slot[:, None, None], causal[None], True)
    allowed = inside[None] & valid_slots[:, :, None, None]
    return jnp.transpose(allowed, (0, 2, 1, 3))[:, None]


def send_chunk(key_c, value_c, offsets, relay):
    pair = jnp.stack([key_c, value_c])
    received = {0: pair}
    for offset in offsets:
        if relay and (offset.bit_length() - 1) % 2 == 1:
            half = offset // 2
            received[offset] = from_behind(received[half], "ctx", half)
        else:
            received[offset] = from_behind(pair, "ctx", offset)
    return [received[0]] + [received[offset] for offset in offsets]


def attend_chunk(query_c, received, grad_c, allowed, offsets, heads):
    scale_factor = 1.0 / math.sqrt(HEAD_DIM)
    rows = query_c.shape[0]
    head_shape = (rows, heads, HEAD_DIM)
    key_stack = jnp.stack([moved[0].reshape(head_shape) for moved in received])[None]
    value_stack = jnp.stack([moved[1].reshape(head_shape) for moved in received])[None]
    query_stack = query_c.reshape((1,) + head_shape)
    grad_stack = grad_c.reshape((1,) + head_shape)
    raw_scores = (
        jnp.einsum("bthd,bnuhd->bhtnu", query_stack, key_stack, preferred_element_type=jnp.float32)
        * scale_factor
    )
    scores = jnp.where(allowed, raw_scores, -1e30)
    row_peak = jnp.max(scores, axis=(3, 4), keepdims=True)
    summed = jnp.sum(jnp.exp(scores - row_peak), axis=(3, 4), keepdims=True)
    log_total = row_peak + jnp.log(summed)
    weights32 = jnp.exp(scores - log_total)
    weights = rounded(weights32)
    output = rounded(
        jnp.einsum("bhtnu,bnuhd->bthd", weights, value_stack, preferred_element_type=jnp.float32)
    )
    grad_probs = jnp.einsum(
        "bthd,bnuhd->bhtnu", grad_stack, value_stack, preferred_element_type=jnp.float32
    )
    delta_rows = jnp.sum(grad_stack.astype(jnp.float32) * output.astype(jnp.float32), axis=-1)
    delta_rows = jnp.transpose(delta_rows, (0, 2, 1))[:, :, :, None, None]
    grad_scores = rounded(weights32 * (grad_probs - delta_rows) * scale_factor)
    query_grad = jnp.einsum(
        "bhtnu,bnuhd->bthd", grad_scores, key_stack, preferred_element_type=jnp.float32
    )
    key_terms = jnp.einsum(
        "bhtnu,bthd->bnuhd", grad_scores, query_stack, preferred_element_type=jnp.float32
    )
    value_terms = jnp.einsum(
        "bhtnu,bthd->bnuhd", weights, grad_stack, preferred_element_type=jnp.float32
    )
    own = (rounded(key_terms[0, 0]), rounded(value_terms[0, 0]))
    outgoing = [
        jnp.stack([key_terms[0, slot_index], value_terms[0, slot_index]]).astype(jnp.bfloat16)
        for slot_index in range(1, len(offsets) + 1)
    ]
    return output, query_grad, own, outgoing


def gather_back(own, outgoing, offsets):
    key_accum = own[0].astype(jnp.float32)
    value_accum = own[1].astype(jnp.float32)
    for parts, offset in zip(outgoing, offsets):
        returned = from_behind(parts, "ctx", -offset)
        key_accum = key_accum + returned[0].astype(jnp.float32)
        value_accum = value_accum + returned[1].astype(jnp.float32)
    return key_accum, value_accum


def on_device(queries, key_vectors, values, grad_out, file_lengths, reach_table):
    local_rows = queries.shape[0]
    width_all = queries.shape[1]
    per_shard = local_rows // BLOCK
    ctx_size = lax.axis_size("ctx")
    levels = (per_shard * ctx_size - 1).bit_length()
    offsets = [2**level_index for level_index in range(levels)]
    shard_index = lax.axis_index("ctx")
    global_rows = shard_index * local_rows + jnp.arange(local_rows, dtype=jnp.int32)
    positions = file_positions(file_lengths, global_rows)
    query_rot = rounded(rotary(queries, positions, HEADS, HEAD_DIM, False))
    key_rot = rounded(rotary(key_vectors, positions, HEADS, HEAD_DIM, False))
    valid_slots = reach_mask(reach_table, shard_index * per_shard, per_shard, levels)
    allowed = score_mask(valid_slots, BLOCK)
    bounds = [sum(CHUNK_HEADS[:chunk]) * HEAD_DIM for chunk in range(len(CHUNK_HEADS) + 1)]
    pieces = []
    pending = []
    for chunk, chunk_heads in enumerate(CHUNK_HEADS):
        chunk_width = chunk_heads * HEAD_DIM
        cols = slice(bounds[chunk], bounds[chunk + 1])
        key_c, value_c = key_rot[:, cols], values[:, cols]
        if pending:
            key_c, value_c, _ = lax.optimization_barrier((key_c, value_c, pieces[-1][0]))
        received = send_chunk(key_c, value_c, offsets, relay=not pending)
        output, query_grad, own, outgoing = attend_chunk(
            query_rot[:, cols], received, grad_out[:, cols], allowed, offsets, chunk_heads
        )
        pending.append(outgoing)
        key_accum_c, value_accum_c = gather_back(own, outgoing, offsets)
        rows = query_rot.shape[0]
        pieces.append(
            (
                output.reshape(rows, chunk_width),
                query_grad.reshape(rows, chunk_width),
                key_accum_c.reshape(rows, chunk_width),
                value_accum_c.reshape(rows, chunk_width),
            )
        )
    attended, query_grad, key_accum, value_accum = [
        jnp.concatenate(parts, axis=1) for parts in zip(*pieces)
    ]
    grad_queries = rotary(query_grad, positions, HEADS, HEAD_DIM, True).astype(jnp.bfloat16)
    grad_keys = rotary(key_accum, positions, HEADS, HEAD_DIM, True).astype(jnp.bfloat16)
    grad_values = value_accum.astype(jnp.bfloat16)
    return (attended, grad_queries, grad_keys, grad_values)


def solution(mesh):
    placed = (
        P(("groups", "ctx"), None),
        P(("groups", "ctx"), None),
        P(("groups", "ctx"), None),
        P(("groups", "ctx"), None),
        P("groups"),
        P(("groups", "ctx")),
    )
    return jax.shard_map(
        on_device,
        mesh=mesh,
        in_specs=placed,
        out_specs=(
            P(("groups", "ctx"), None),
            P(("groups", "ctx"), None),
            P(("groups", "ctx"), None),
            P(("groups", "ctx"), None),
        ),
        check_vma=False,
    )
```

```python
import math

import jax
import jax.numpy as jnp
from jax import lax
from jax.sharding import PartitionSpec as P

HEADS = 16
HEAD_DIM = 128
BLOCK = 128
CHUNKS = 2


def from_behind(value, axis, steps):
    count = lax.axis_size(axis)
    leading, last = (max(0, -steps), min(count, count - steps))
    return lax.ppermute(value, axis, [(source, source + steps) for source in range(leading, last)])


def rounded(matrix):
    return lax.optimization_barrier(matrix.astype(jnp.bfloat16))


def file_positions(file_lengths, global_rows):
    file_ends = jnp.cumsum(file_lengths)
    starts = file_ends - file_lengths
    owned_mask = starts[None, :] <= global_rows[:, None]
    latest = jnp.max(jnp.where(owned_mask, starts[None, :], 0), axis=1)
    return global_rows - latest


def rotary(matrix, positions, head_count, head_width, inverse):
    half_width = head_width // 2
    exponent = jnp.arange(half_width, dtype=jnp.float32) * (2.0 / head_width)
    frequency = jnp.exp(exponent * -math.log(10000.0))
    angles = positions.astype(jnp.float32)[:, None] * frequency[None, :]
    cosine = jnp.cos(angles)[:, None, :]
    sine_table = jnp.sin(angles)[:, None, :]
    shaped = matrix.astype(jnp.float32).reshape(matrix.shape[0], head_count, head_width)
    former = shaped[..., :half_width]
    latter = shaped[..., half_width:]
    if inverse:
        turned = jnp.concatenate(
            [former * cosine + latter * sine_table, latter * cosine - former * sine_table], axis=-1
        )
    else:
        turned = jnp.concatenate(
            [former * cosine - latter * sine_table, latter * cosine + former * sine_table], axis=-1
        )
    return turned.reshape(matrix.shape[0], head_count * head_width)


def reach_mask(reach_rows, first_block, per_shard, levels):
    block_ids = first_block + jnp.arange(per_shard, dtype=jnp.int32)
    level_ids = jnp.arange(levels, dtype=jnp.int32)
    distances = jnp.array([2**level_index for level_index in range(levels)], dtype=jnp.int32)
    reached = (level_ids[None, :] < reach_rows[:, None]) & (
        block_ids[:, None] - distances[None, :] >= 0
    )
    return jnp.concatenate([jnp.ones((per_shard, 1), dtype=bool), reached], axis=1)


def score_mask(valid_slots, block_rows):
    row_ids = jnp.arange(block_rows)
    causal = row_ids[None, :] <= row_ids[:, None]
    first_slot = jnp.arange(valid_slots.shape[1]) == 0
    inside = jnp.where(first_slot[:, None, None], causal[None], True)
    allowed = inside[None] & valid_slots[:, :, None, None]
    return jnp.transpose(allowed, (0, 2, 1, 3))[:, None]


def send_chunk(key_c, value_c, offsets, relay):
    pair = jnp.stack([key_c, value_c])
    received = {0: pair}
    for offset in offsets:
        if relay and (offset.bit_length() - 1) % 2 == 1:
            half = offset // 2
            received[offset] = from_behind(received[half], "ctx", half)
        elif relay:
            received[offset] = from_behind(pair, "ctx", offset)
        else:
            moved_key = from_behind(key_c, "ctx", offset)
            moved_value = from_behind(value_c, "ctx", offset)
            received[offset] = jnp.stack([moved_key, moved_value])
    return [received[0]] + [received[offset] for offset in offsets]


def attend_chunk(query_c, received, grad_c, allowed, offsets, heads):
    scale_factor = 1.0 / math.sqrt(HEAD_DIM)
    rows = query_c.shape[0]
    head_shape = (rows, heads, HEAD_DIM)
    key_stack = jnp.stack([moved[0].reshape(head_shape) for moved in received])[None]
    value_stack = jnp.stack([moved[1].reshape(head_shape) for moved in received])[None]
    query_stack = query_c.reshape((1,) + head_shape)
    grad_stack = grad_c.reshape((1,) + head_shape)
    raw_scores = (
        jnp.einsum("bthd,bnuhd->bhtnu", query_stack, key_stack, preferred_element_type=jnp.float32)
        * scale_factor
    )
    scores = jnp.where(allowed, raw_scores, -1e30)
    row_peak = jnp.max(scores, axis=(3, 4), keepdims=True)
    summed = jnp.sum(jnp.exp(scores - row_peak), axis=(3, 4), keepdims=True)
    log_total = row_peak + jnp.log(summed)
    weights32 = jnp.exp(scores - log_total)
    weights = rounded(weights32)
    output = rounded(
        jnp.einsum("bhtnu,bnuhd->bthd", weights, value_stack, preferred_element_type=jnp.float32)
    )
    grad_probs = jnp.einsum(
        "bthd,bnuhd->bhtnu", grad_stack, value_stack, preferred_element_type=jnp.float32
    )
    delta_rows = jnp.sum(grad_stack.astype(jnp.float32) * output.astype(jnp.float32), axis=-1)
    delta_rows = jnp.transpose(delta_rows, (0, 2, 1))[:, :, :, None, None]
    grad_scores = rounded(weights32 * (grad_probs - delta_rows) * scale_factor)
    query_grad = jnp.einsum(
        "bhtnu,bnuhd->bthd", grad_scores, key_stack, preferred_element_type=jnp.float32
    )
    key_terms = jnp.einsum(
        "bhtnu,bthd->bnuhd", grad_scores, query_stack, preferred_element_type=jnp.float32
    )
    value_terms = jnp.einsum(
        "bhtnu,bthd->bnuhd", weights, grad_stack, preferred_element_type=jnp.float32
    )
    own = (rounded(key_terms[0, 0]), rounded(value_terms[0, 0]))
    outgoing = [
        jnp.stack([key_terms[0, slot_index], value_terms[0, slot_index]]).astype(jnp.bfloat16)
        for slot_index in range(1, len(offsets) + 1)
    ]
    return output, query_grad, own, outgoing


def gather_back(own, outgoing, offsets):
    key_accum = own[0].astype(jnp.float32)
    value_accum = own[1].astype(jnp.float32)
    for parts, offset in zip(outgoing, offsets):
        returned = from_behind(parts, "ctx", -offset)
        key_accum = key_accum + returned[0].astype(jnp.float32)
        value_accum = value_accum + returned[1].astype(jnp.float32)
    return key_accum, value_accum


def on_device(queries, key_vectors, values, grad_out, file_lengths, reach_table):
    local_rows = queries.shape[0]
    width_all = queries.shape[1]
    per_shard = local_rows // BLOCK
    ctx_size = lax.axis_size("ctx")
    levels = (per_shard * ctx_size - 1).bit_length()
    offsets = [2**level_index for level_index in range(levels)]
    shard_index = lax.axis_index("ctx")
    global_rows = shard_index * local_rows + jnp.arange(local_rows, dtype=jnp.int32)
    positions = file_positions(file_lengths, global_rows)
    query_rot = rounded(rotary(queries, positions, HEADS, HEAD_DIM, False))
    key_rot = rounded(rotary(key_vectors, positions, HEADS, HEAD_DIM, False))
    valid_slots = reach_mask(reach_table, shard_index * per_shard, per_shard, levels)
    allowed = score_mask(valid_slots, BLOCK)
    chunk_heads = HEADS // CHUNKS
    chunk_width = chunk_heads * HEAD_DIM
    columns = [slice(chunk * chunk_width, (chunk + 1) * chunk_width) for chunk in range(CHUNKS)]
    pieces = []
    pending = []
    for chunk, cols in enumerate(columns):
        key_c, value_c = key_rot[:, cols], values[:, cols]
        if pending:
            key_c, value_c, _ = lax.optimization_barrier((key_c, value_c, pieces[-1][0]))
        received = send_chunk(key_c, value_c, offsets, relay=not pending)
        output, query_grad, own, outgoing = attend_chunk(
            query_rot[:, cols], received, grad_out[:, cols], allowed, offsets, chunk_heads
        )
        pending.append(outgoing)
        key_accum_c, value_accum_c = gather_back(own, outgoing, offsets)
        rows = query_rot.shape[0]
        pieces.append(
            (
                output.reshape(rows, chunk_width),
                query_grad.reshape(rows, chunk_width),
                key_accum_c.reshape(rows, chunk_width),
                value_accum_c.reshape(rows, chunk_width),
            )
        )
    attended, query_grad, key_accum, value_accum = [
        jnp.concatenate(parts, axis=1) for parts in zip(*pieces)
    ]
    grad_queries = rotary(query_grad, positions, HEADS, HEAD_DIM, True).astype(jnp.bfloat16)
    grad_keys = rotary(key_accum, positions, HEADS, HEAD_DIM, True).astype(jnp.bfloat16)
    grad_values = value_accum.astype(jnp.bfloat16)
    return (attended, grad_queries, grad_keys, grad_values)


def solution(mesh):
    placed = (
        P(("groups", "ctx"), None),
        P(("groups", "ctx"), None),
        P(("groups", "ctx"), None),
        P(("groups", "ctx"), None),
        P("groups"),
        P(("groups", "ctx")),
    )
    return jax.shard_map(
        on_device,
        mesh=mesh,
        in_specs=placed,
        out_specs=(
            P(("groups", "ctx"), None),
            P(("groups", "ctx"), None),
            P(("groups", "ctx"), None),
            P(("groups", "ctx"), None),
        ),
        check_vma=False,
    )
```

```python
import math

import jax
import jax.numpy as jnp
from jax import lax
from jax.sharding import PartitionSpec as P

HEADS = 16
HEAD_DIM = 128
BLOCK = 128
CHUNKS = 2


def from_behind(value, axis, steps):
    count = lax.axis_size(axis)
    leading, last = (max(0, -steps), min(count, count - steps))
    return lax.ppermute(value, axis, [(source, source + steps) for source in range(leading, last)])


def rounded(matrix):
    return lax.optimization_barrier(matrix.astype(jnp.bfloat16))


def file_positions(file_lengths, global_rows):
    file_ends = jnp.cumsum(file_lengths)
    starts = file_ends - file_lengths
    owned_mask = starts[None, :] <= global_rows[:, None]
    latest = jnp.max(jnp.where(owned_mask, starts[None, :], 0), axis=1)
    return global_rows - latest


def rotary(matrix, positions, head_count, head_width, inverse):
    half_width = head_width // 2
    exponent = jnp.arange(half_width, dtype=jnp.float32) * (2.0 / head_width)
    frequency = jnp.exp(exponent * -math.log(10000.0))
    angles = positions.astype(jnp.float32)[:, None] * frequency[None, :]
    cosine = jnp.cos(angles)[:, None, :]
    sine_table = jnp.sin(angles)[:, None, :]
    shaped = matrix.astype(jnp.float32).reshape(matrix.shape[0], head_count, head_width)
    former = shaped[..., :half_width]
    latter = shaped[..., half_width:]
    if inverse:
        turned = jnp.concatenate(
            [former * cosine + latter * sine_table, latter * cosine - former * sine_table], axis=-1
        )
    else:
        turned = jnp.concatenate(
            [former * cosine - latter * sine_table, latter * cosine + former * sine_table], axis=-1
        )
    return turned.reshape(matrix.shape[0], head_count * head_width)


def reach_mask(reach_rows, first_block, per_shard, levels):
    block_ids = first_block + jnp.arange(per_shard, dtype=jnp.int32)
    level_ids = jnp.arange(levels, dtype=jnp.int32)
    distances = jnp.array([2**level_index for level_index in range(levels)], dtype=jnp.int32)
    reached = (level_ids[None, :] < reach_rows[:, None]) & (
        block_ids[:, None] - distances[None, :] >= 0
    )
    return jnp.concatenate([jnp.ones((per_shard, 1), dtype=bool), reached], axis=1)


def score_mask(valid_slots, block_rows):
    row_ids = jnp.arange(block_rows)
    causal = row_ids[None, :] <= row_ids[:, None]
    first_slot = jnp.arange(valid_slots.shape[1]) == 0
    inside = jnp.where(first_slot[:, None, None], causal[None], True)
    allowed = inside[None] & valid_slots[:, :, None, None]
    return jnp.transpose(allowed, (0, 2, 1, 3))[:, None]


def send_chunk(key_c, value_c, offsets, relay):
    pair = jnp.stack([key_c, value_c])
    received = {0: pair}
    for offset in offsets:
        if relay and (offset.bit_length() - 1) % 2 == 1:
            half = offset // 2
            received[offset] = from_behind(received[half], "ctx", half)
        else:
            received[offset] = from_behind(pair, "ctx", offset)
    return [received[0]] + [received[offset] for offset in offsets]


def attend_chunk(query_c, received, grad_c, allowed, offsets, heads):
    scale_factor = 1.0 / math.sqrt(HEAD_DIM)
    rows = query_c.shape[0]
    head_shape = (rows, heads, HEAD_DIM)
    key_stack = jnp.stack([moved[0].reshape(head_shape) for moved in received])[None]
    value_stack = jnp.stack([moved[1].reshape(head_shape) for moved in received])[None]
    query_stack = query_c.reshape((1,) + head_shape)
    grad_stack = grad_c.reshape((1,) + head_shape)
    raw_scores = (
        jnp.einsum("bthd,bnuhd->bhtnu", query_stack, key_stack, preferred_element_type=jnp.float32)
        * scale_factor
    )
    scores = jnp.where(allowed, raw_scores, -1e30)
    row_peak = jnp.max(scores, axis=(3, 4), keepdims=True)
    summed = jnp.sum(jnp.exp(scores - row_peak), axis=(3, 4), keepdims=True)
    log_total = row_peak + jnp.log(summed)
    weights32 = jnp.exp(scores - log_total)
    weights = rounded(weights32)
    output = rounded(
        jnp.einsum("bhtnu,bnuhd->bthd", weights, value_stack, preferred_element_type=jnp.float32)
    )
    grad_probs = jnp.einsum(
        "bthd,bnuhd->bhtnu", grad_stack, value_stack, preferred_element_type=jnp.float32
    )
    delta_rows = jnp.sum(grad_stack.astype(jnp.float32) * output.astype(jnp.float32), axis=-1)
    delta_rows = jnp.transpose(delta_rows, (0, 2, 1))[:, :, :, None, None]
    grad_scores = rounded(weights32 * (grad_probs - delta_rows) * scale_factor)
    query_grad = jnp.einsum(
        "bhtnu,bnuhd->bthd", grad_scores, key_stack, preferred_element_type=jnp.float32
    )
    key_terms = jnp.einsum(
        "bhtnu,bthd->bnuhd", grad_scores, query_stack, preferred_element_type=jnp.float32
    )
    value_terms = jnp.einsum(
        "bhtnu,bthd->bnuhd", weights, grad_stack, preferred_element_type=jnp.float32
    )
    own = (rounded(key_terms[0, 0]), rounded(value_terms[0, 0]))
    outgoing = [
        jnp.stack([key_terms[0, slot_index], value_terms[0, slot_index]]).astype(jnp.bfloat16)
        for slot_index in range(1, len(offsets) + 1)
    ]
    return output, query_grad, own, outgoing


def gather_back(own, outgoing, offsets):
    key_accum = own[0].astype(jnp.float32)
    value_accum = own[1].astype(jnp.float32)
    for parts, offset in zip(outgoing, offsets):
        returned = from_behind(parts, "ctx", -offset)
        key_accum = key_accum + returned[0].astype(jnp.float32)
        value_accum = value_accum + returned[1].astype(jnp.float32)
    return key_accum, value_accum


def on_device(queries, key_vectors, values, grad_out, file_lengths, reach_table):
    local_rows = queries.shape[0]
    width_all = queries.shape[1]
    per_shard = local_rows // BLOCK
    ctx_size = lax.axis_size("ctx")
    levels = (per_shard * ctx_size - 1).bit_length()
    offsets = [2**level_index for level_index in range(levels)]
    shard_index = lax.axis_index("ctx")
    global_rows = shard_index * local_rows + jnp.arange(local_rows, dtype=jnp.int32)
    positions = file_positions(file_lengths, global_rows)
    query_rot = rounded(rotary(queries, positions, HEADS, HEAD_DIM, False))
    key_rot = rounded(rotary(key_vectors, positions, HEADS, HEAD_DIM, False))
    valid_slots = reach_mask(reach_table, shard_index * per_shard, per_shard, levels)
    allowed = score_mask(valid_slots, BLOCK)
    chunk_heads = HEADS // CHUNKS
    chunk_width = chunk_heads * HEAD_DIM
    columns = [slice(chunk * chunk_width, (chunk + 1) * chunk_width) for chunk in range(CHUNKS)]
    pieces = []
    pending = []
    for chunk, cols in enumerate(columns):
        key_c, value_c = key_rot[:, cols], values[:, cols]
        if pending:
            key_c, value_c, _ = lax.optimization_barrier((key_c, value_c, pieces[-1][0]))
        received = send_chunk(key_c, value_c, offsets, relay=False)
        output, query_grad, own, outgoing = attend_chunk(
            query_rot[:, cols], received, grad_out[:, cols], allowed, offsets, chunk_heads
        )
        pending.append(outgoing)
        key_accum_c, value_accum_c = gather_back(own, outgoing, offsets)
        rows = query_rot.shape[0]
        pieces.append(
            (
                output.reshape(rows, chunk_width),
                query_grad.reshape(rows, chunk_width),
                key_accum_c.reshape(rows, chunk_width),
                value_accum_c.reshape(rows, chunk_width),
            )
        )
    attended, query_grad, key_accum, value_accum = [
        jnp.concatenate(parts, axis=1) for parts in zip(*pieces)
    ]
    grad_queries = rotary(query_grad, positions, HEADS, HEAD_DIM, True).astype(jnp.bfloat16)
    grad_keys = rotary(key_accum, positions, HEADS, HEAD_DIM, True).astype(jnp.bfloat16)
    grad_values = value_accum.astype(jnp.bfloat16)
    return (attended, grad_queries, grad_keys, grad_values)


def solution(mesh):
    placed = (
        P(("groups", "ctx"), None),
        P(("groups", "ctx"), None),
        P(("groups", "ctx"), None),
        P(("groups", "ctx"), None),
        P("groups"),
        P(("groups", "ctx")),
    )
    return jax.shard_map(
        on_device,
        mesh=mesh,
        in_specs=placed,
        out_specs=(
            P(("groups", "ctx"), None),
            P(("groups", "ctx"), None),
            P(("groups", "ctx"), None),
            P(("groups", "ctx"), None),
        ),
        check_vma=False,
    )
```

```python
import math

import jax
import jax.numpy as jnp
from jax import lax
from jax.sharding import PartitionSpec as P

HEADS = 16
HEAD_DIM = 128
BLOCK = 128
CHUNKS = 2


def from_behind(value, axis, steps):
    count = lax.axis_size(axis)
    leading, last = (max(0, -steps), min(count, count - steps))
    return lax.ppermute(value, axis, [(source, source + steps) for source in range(leading, last)])


def rounded(matrix):
    return lax.optimization_barrier(matrix.astype(jnp.bfloat16))


def file_positions(file_lengths, global_rows):
    file_ends = jnp.cumsum(file_lengths)
    starts = file_ends - file_lengths
    owned_mask = starts[None, :] <= global_rows[:, None]
    latest = jnp.max(jnp.where(owned_mask, starts[None, :], 0), axis=1)
    return global_rows - latest


def rotary(matrix, positions, head_count, head_width, inverse):
    half_width = head_width // 2
    exponent = jnp.arange(half_width, dtype=jnp.float32) * (2.0 / head_width)
    frequency = jnp.exp(exponent * -math.log(10000.0))
    angles = positions.astype(jnp.float32)[:, None] * frequency[None, :]
    cosine = jnp.cos(angles)[:, None, :]
    sine_table = jnp.sin(angles)[:, None, :]
    shaped = matrix.astype(jnp.float32).reshape(matrix.shape[0], head_count, head_width)
    former = shaped[..., :half_width]
    latter = shaped[..., half_width:]
    if inverse:
        turned = jnp.concatenate(
            [former * cosine + latter * sine_table, latter * cosine - former * sine_table], axis=-1
        )
    else:
        turned = jnp.concatenate(
            [former * cosine - latter * sine_table, latter * cosine + former * sine_table], axis=-1
        )
    return turned.reshape(matrix.shape[0], head_count * head_width)


def reach_mask(reach_rows, first_block, per_shard, levels):
    block_ids = first_block + jnp.arange(per_shard, dtype=jnp.int32)
    level_ids = jnp.arange(levels, dtype=jnp.int32)
    distances = jnp.array([2**level_index for level_index in range(levels)], dtype=jnp.int32)
    reached = (level_ids[None, :] < reach_rows[:, None]) & (
        block_ids[:, None] - distances[None, :] >= 0
    )
    return jnp.concatenate([jnp.ones((per_shard, 1), dtype=bool), reached], axis=1)


def score_mask(valid_slots, block_rows):
    row_ids = jnp.arange(block_rows)
    causal = row_ids[None, :] <= row_ids[:, None]
    first_slot = jnp.arange(valid_slots.shape[1]) == 0
    inside = jnp.where(first_slot[:, None, None], causal[None], True)
    allowed = inside[None] & valid_slots[:, :, None, None]
    return jnp.transpose(allowed, (0, 2, 1, 3))[:, None]


def send_chunk(key_c, value_c, offsets, relay):
    pair = jnp.stack([key_c, value_c])
    received = {0: pair}
    for offset in offsets:
        if relay and (offset.bit_length() - 1) % 2 == 1:
            half = offset // 2
            received[offset] = from_behind(received[half], "ctx", half)
        else:
            received[offset] = from_behind(pair, "ctx", offset)
    return [received[0]] + [received[offset] for offset in offsets]


def attend_chunk(query_c, received, grad_c, allowed, offsets, heads):
    scale_factor = 1.0 / math.sqrt(HEAD_DIM)
    rows = query_c.shape[0]
    head_shape = (rows, heads, HEAD_DIM)
    key_stack = jnp.stack([moved[0].reshape(head_shape) for moved in received])[None]
    value_stack = jnp.stack([moved[1].reshape(head_shape) for moved in received])[None]
    query_stack = query_c.reshape((1,) + head_shape)
    grad_stack = grad_c.reshape((1,) + head_shape)
    raw_scores = (
        jnp.einsum("bthd,bnuhd->bhtnu", query_stack, key_stack, preferred_element_type=jnp.float32)
        * scale_factor
    )
    scores = jnp.where(allowed, raw_scores, -1e30)
    row_peak = jnp.max(scores, axis=(3, 4), keepdims=True)
    summed = jnp.sum(jnp.exp(scores - row_peak), axis=(3, 4), keepdims=True)
    log_total = row_peak + jnp.log(summed)
    weights32 = jnp.exp(scores - log_total)
    weights = rounded(weights32)
    output = rounded(
        jnp.einsum("bhtnu,bnuhd->bthd", weights, value_stack, preferred_element_type=jnp.float32)
    )
    grad_probs = jnp.einsum(
        "bthd,bnuhd->bhtnu", grad_stack, value_stack, preferred_element_type=jnp.float32
    )
    delta_rows = jnp.sum(grad_stack.astype(jnp.float32) * output.astype(jnp.float32), axis=-1)
    delta_rows = jnp.transpose(delta_rows, (0, 2, 1))[:, :, :, None, None]
    grad_scores = rounded(weights32 * (grad_probs - delta_rows) * scale_factor)
    query_grad = jnp.einsum(
        "bhtnu,bnuhd->bthd", grad_scores, key_stack, preferred_element_type=jnp.float32
    )
    key_terms = jnp.einsum(
        "bhtnu,bthd->bnuhd", grad_scores, query_stack, preferred_element_type=jnp.float32
    )
    value_terms = jnp.einsum(
        "bhtnu,bthd->bnuhd", weights, grad_stack, preferred_element_type=jnp.float32
    )
    own = (rounded(key_terms[0, 0]), rounded(value_terms[0, 0]))
    outgoing = [
        jnp.stack([key_terms[0, slot_index], value_terms[0, slot_index]]).astype(jnp.bfloat16)
        for slot_index in range(1, len(offsets) + 1)
    ]
    return output, query_grad, own, outgoing


def gather_back(own, outgoing, offsets):
    key_accum = own[0].astype(jnp.float32)
    value_accum = own[1].astype(jnp.float32)
    for parts, offset in zip(outgoing, offsets):
        returned = from_behind(parts, "ctx", -offset)
        key_accum = key_accum + returned[0].astype(jnp.float32)
        value_accum = value_accum + returned[1].astype(jnp.float32)
    return key_accum, value_accum


def on_device(queries, key_vectors, values, grad_out, file_lengths, reach_table):
    local_rows = queries.shape[0]
    width_all = queries.shape[1]
    per_shard = local_rows // BLOCK
    ctx_size = lax.axis_size("ctx")
    levels = (per_shard * ctx_size - 1).bit_length()
    offsets = [2**level_index for level_index in range(levels)]
    shard_index = lax.axis_index("ctx")
    global_rows = shard_index * local_rows + jnp.arange(local_rows, dtype=jnp.int32)
    positions = file_positions(file_lengths, global_rows)
    query_rot = rounded(rotary(queries, positions, HEADS, HEAD_DIM, False))
    key_rot = rounded(rotary(key_vectors, positions, HEADS, HEAD_DIM, False))
    valid_slots = reach_mask(reach_table, shard_index * per_shard, per_shard, levels)
    allowed = score_mask(valid_slots, BLOCK)
    chunk_heads = HEADS // CHUNKS
    chunk_width = chunk_heads * HEAD_DIM
    columns = [slice(chunk * chunk_width, (chunk + 1) * chunk_width) for chunk in range(CHUNKS)]
    pieces = []
    pending = []
    for chunk, cols in enumerate(columns):
        key_c, value_c = key_rot[:, cols], values[:, cols]
        if pending:
            key_c, value_c, _ = lax.optimization_barrier((key_c, value_c, pieces[-1][0]))
        received = send_chunk(key_c, value_c, offsets, relay=not pending)
        output, query_grad, own, outgoing = attend_chunk(
            query_rot[:, cols], received, grad_out[:, cols], allowed, offsets, chunk_heads
        )
        pending.append(outgoing)
        key_accum_c, value_accum_c = gather_back(own, outgoing, offsets)
        rows = query_rot.shape[0]
        pieces.append(
            (
                output.reshape(rows, chunk_width),
                rotary(
                    query_grad.reshape(rows, chunk_width), positions, chunk_heads, HEAD_DIM, True
                ).astype(jnp.bfloat16),
                rotary(
                    key_accum_c.reshape(rows, chunk_width), positions, chunk_heads, HEAD_DIM, True
                ).astype(jnp.bfloat16),
                value_accum_c.reshape(rows, chunk_width).astype(jnp.bfloat16),
            )
        )
    attended, grad_queries, grad_keys, grad_values = [
        jnp.concatenate(parts, axis=1) for parts in zip(*pieces)
    ]
    return (attended, grad_queries, grad_keys, grad_values)


def solution(mesh):
    placed = (
        P(("groups", "ctx"), None),
        P(("groups", "ctx"), None),
        P(("groups", "ctx"), None),
        P(("groups", "ctx"), None),
        P("groups"),
        P(("groups", "ctx")),
    )
    return jax.shard_map(
        on_device,
        mesh=mesh,
        in_specs=placed,
        out_specs=(
            P(("groups", "ctx"), None),
            P(("groups", "ctx"), None),
            P(("groups", "ctx"), None),
            P(("groups", "ctx"), None),
        ),
        check_vma=False,
    )
```

```python
import math

import jax
import jax.numpy as jnp
from jax import lax
from jax.sharding import PartitionSpec as P

HEADS = 16
HEAD_DIM = 128
BLOCK = 128
CHUNKS = 2


def from_behind(value, axis, steps):
    count = lax.axis_size(axis)
    leading, last = (max(0, -steps), min(count, count - steps))
    return lax.ppermute(value, axis, [(source, source + steps) for source in range(leading, last)])


def rounded(matrix):
    return lax.optimization_barrier(matrix.astype(jnp.bfloat16))


def file_positions(file_lengths, global_rows):
    file_ends = jnp.cumsum(file_lengths)
    starts = file_ends - file_lengths
    owned_mask = starts[None, :] <= global_rows[:, None]
    latest = jnp.max(jnp.where(owned_mask, starts[None, :], 0), axis=1)
    return global_rows - latest


def rotary(matrix, positions, head_count, head_width, inverse):
    half_width = head_width // 2
    exponent = jnp.arange(half_width, dtype=jnp.float32) * (2.0 / head_width)
    frequency = jnp.exp(exponent * -math.log(10000.0))
    angles = positions.astype(jnp.float32)[:, None] * frequency[None, :]
    cosine = jnp.cos(angles)[:, None, :]
    sine_table = jnp.sin(angles)[:, None, :]
    shaped = matrix.astype(jnp.float32).reshape(matrix.shape[0], head_count, head_width)
    former = shaped[..., :half_width]
    latter = shaped[..., half_width:]
    if inverse:
        turned = jnp.concatenate(
            [former * cosine + latter * sine_table, latter * cosine - former * sine_table], axis=-1
        )
    else:
        turned = jnp.concatenate(
            [former * cosine - latter * sine_table, latter * cosine + former * sine_table], axis=-1
        )
    return turned.reshape(matrix.shape[0], head_count * head_width)


def reach_mask(reach_rows, first_block, per_shard, levels):
    block_ids = first_block + jnp.arange(per_shard, dtype=jnp.int32)
    level_ids = jnp.arange(levels, dtype=jnp.int32)
    distances = jnp.array([2**level_index for level_index in range(levels)], dtype=jnp.int32)
    reached = (level_ids[None, :] < reach_rows[:, None]) & (
        block_ids[:, None] - distances[None, :] >= 0
    )
    return jnp.concatenate([jnp.ones((per_shard, 1), dtype=bool), reached], axis=1)


def score_mask(valid_slots, block_rows):
    row_ids = jnp.arange(block_rows)
    causal = row_ids[None, :] <= row_ids[:, None]
    first_slot = jnp.arange(valid_slots.shape[1]) == 0
    inside = jnp.where(first_slot[:, None, None], causal[None], True)
    allowed = inside[None] & valid_slots[:, :, None, None]
    return jnp.transpose(allowed, (0, 2, 1, 3))[:, None]


def send_chunk(key_c, value_c, offsets, relay):
    pair = jnp.stack([key_c, value_c])
    received = {0: pair}
    for offset in offsets:
        if relay and (offset.bit_length() - 1) % 2 == 1:
            half = offset // 2
            received[offset] = from_behind(received[half], "ctx", half)
        else:
            received[offset] = from_behind(pair, "ctx", offset)
    return [received[0]] + [received[offset] for offset in offsets]


def attend_chunk(query_c, received, grad_c, allowed, offsets, heads):
    scale_factor = 1.0 / math.sqrt(HEAD_DIM)
    rows = query_c.shape[0]
    head_shape = (rows, heads, HEAD_DIM)
    key_stack = jnp.stack([moved[0].reshape(head_shape) for moved in received])[None]
    value_stack = jnp.stack([moved[1].reshape(head_shape) for moved in received])[None]
    query_stack = query_c.reshape((1,) + head_shape)
    grad_stack = grad_c.reshape((1,) + head_shape)
    raw_scores = (
        jnp.einsum("bthd,bnuhd->bhtnu", query_stack, key_stack, preferred_element_type=jnp.float32)
        * scale_factor
    )
    scores = jnp.where(allowed, raw_scores, -1e30)
    row_peak = jnp.max(scores, axis=(3, 4), keepdims=True)
    summed = jnp.sum(jnp.exp(scores - row_peak), axis=(3, 4), keepdims=True)
    log_total = row_peak + jnp.log(summed)
    weights32 = jnp.exp(scores - log_total)
    weights = rounded(weights32)
    output = rounded(
        jnp.einsum("bhtnu,bnuhd->bthd", weights, value_stack, preferred_element_type=jnp.float32)
    )
    grad_probs = jnp.einsum(
        "bthd,bnuhd->bhtnu", grad_stack, value_stack, preferred_element_type=jnp.float32
    )
    delta_rows = jnp.sum(grad_stack.astype(jnp.float32) * output.astype(jnp.float32), axis=-1)
    delta_rows = jnp.transpose(delta_rows, (0, 2, 1))[:, :, :, None, None]
    grad_scores = rounded(weights32 * (grad_probs - delta_rows) * scale_factor)
    query_grad = jnp.einsum(
        "bhtnu,bnuhd->bthd", grad_scores, key_stack, preferred_element_type=jnp.float32
    )
    key_terms = jnp.einsum(
        "bhtnu,bthd->bnuhd", grad_scores, query_stack, preferred_element_type=jnp.float32
    )
    value_terms = jnp.einsum(
        "bhtnu,bthd->bnuhd", weights, grad_stack, preferred_element_type=jnp.float32
    )
    own = (rounded(key_terms[0, 0]), rounded(value_terms[0, 0]))
    outgoing = [
        jnp.stack([key_terms[0, slot_index], value_terms[0, slot_index]]).astype(jnp.bfloat16)
        for slot_index in range(1, len(offsets) + 1)
    ]
    return output, query_grad, own, outgoing


def gather_back(own, outgoing, offsets):
    key_accum = own[0].astype(jnp.float32)
    value_accum = own[1].astype(jnp.float32)
    for parts, offset in zip(outgoing, offsets):
        returned = from_behind(parts, "ctx", -offset)
        key_accum = key_accum + returned[0].astype(jnp.float32)
        value_accum = value_accum + returned[1].astype(jnp.float32)
    return key_accum, value_accum


def on_device(queries, key_vectors, values, grad_out, file_lengths, reach_table):
    local_rows = queries.shape[0]
    width_all = queries.shape[1]
    per_shard = local_rows // BLOCK
    ctx_size = lax.axis_size("ctx")
    levels = (per_shard * ctx_size - 1).bit_length()
    offsets = [2**level_index for level_index in range(levels)]
    shard_index = lax.axis_index("ctx")
    global_rows = shard_index * local_rows + jnp.arange(local_rows, dtype=jnp.int32)
    positions = file_positions(file_lengths, global_rows)
    query_rot = rounded(rotary(queries, positions, HEADS, HEAD_DIM, False))
    key_rot = rounded(rotary(key_vectors, positions, HEADS, HEAD_DIM, False))
    valid_slots = reach_mask(reach_table, shard_index * per_shard, per_shard, levels)
    allowed = score_mask(valid_slots, BLOCK)
    chunk_heads = HEADS // CHUNKS
    chunk_width = chunk_heads * HEAD_DIM
    columns = [slice(chunk * chunk_width, (chunk + 1) * chunk_width) for chunk in range(CHUNKS)]
    pieces = []
    pending = []
    for chunk, cols in enumerate(columns):
        key_c, value_c = key_rot[:, cols], values[:, cols]
        if pending:
            key_c, value_c, _ = lax.optimization_barrier((key_c, value_c, pending[-1]))
        received = send_chunk(key_c, value_c, offsets, relay=not pending)
        output, query_grad, own, outgoing = attend_chunk(
            query_rot[:, cols], received, grad_out[:, cols], allowed, offsets, chunk_heads
        )
        pending.append(outgoing)
        key_accum_c, value_accum_c = gather_back(own, outgoing, offsets)
        rows = query_rot.shape[0]
        pieces.append(
            (
                output.reshape(rows, chunk_width),
                query_grad.reshape(rows, chunk_width),
                key_accum_c.reshape(rows, chunk_width),
                value_accum_c.reshape(rows, chunk_width),
            )
        )
    attended, query_grad, key_accum, value_accum = [
        jnp.concatenate(parts, axis=1) for parts in zip(*pieces)
    ]
    grad_queries = rotary(query_grad, positions, HEADS, HEAD_DIM, True).astype(jnp.bfloat16)
    grad_keys = rotary(key_accum, positions, HEADS, HEAD_DIM, True).astype(jnp.bfloat16)
    grad_values = value_accum.astype(jnp.bfloat16)
    return (attended, grad_queries, grad_keys, grad_values)


def solution(mesh):
    placed = (
        P(("groups", "ctx"), None),
        P(("groups", "ctx"), None),
        P(("groups", "ctx"), None),
        P(("groups", "ctx"), None),
        P("groups"),
        P(("groups", "ctx")),
    )
    return jax.shard_map(
        on_device,
        mesh=mesh,
        in_specs=placed,
        out_specs=(
            P(("groups", "ctx"), None),
            P(("groups", "ctx"), None),
            P(("groups", "ctx"), None),
            P(("groups", "ctx"), None),
        ),
        check_vma=False,
    )
```

```python
import math

import jax
import jax.numpy as jnp
from jax import lax
from jax.sharding import PartitionSpec as P

HEADS = 16
HEAD_DIM = 128
BLOCK = 128
CHUNKS = 2


def from_behind(value, axis, steps):
    count = lax.axis_size(axis)
    leading, last = (max(0, -steps), min(count, count - steps))
    return lax.ppermute(value, axis, [(source, source + steps) for source in range(leading, last)])


def rounded(matrix):
    return lax.optimization_barrier(matrix.astype(jnp.bfloat16))


def file_positions(file_lengths, global_rows):
    file_ends = jnp.cumsum(file_lengths)
    starts = file_ends - file_lengths
    owned_mask = starts[None, :] <= global_rows[:, None]
    latest = jnp.max(jnp.where(owned_mask, starts[None, :], 0), axis=1)
    return global_rows - latest


def rotary(matrix, positions, head_count, head_width, inverse):
    half_width = head_width // 2
    exponent = jnp.arange(half_width, dtype=jnp.float32) * (2.0 / head_width)
    frequency = jnp.exp(exponent * -math.log(10000.0))
    angles = positions.astype(jnp.float32)[:, None] * frequency[None, :]
    cosine = jnp.cos(angles)[:, None, :]
    sine_table = jnp.sin(angles)[:, None, :]
    shaped = matrix.astype(jnp.float32).reshape(matrix.shape[0], head_count, head_width)
    former = shaped[..., :half_width]
    latter = shaped[..., half_width:]
    if inverse:
        turned = jnp.concatenate(
            [former * cosine + latter * sine_table, latter * cosine - former * sine_table], axis=-1
        )
    else:
        turned = jnp.concatenate(
            [former * cosine - latter * sine_table, latter * cosine + former * sine_table], axis=-1
        )
    return turned.reshape(matrix.shape[0], head_count * head_width)


def reach_mask(reach_rows, first_block, per_shard, levels):
    block_ids = first_block + jnp.arange(per_shard, dtype=jnp.int32)
    level_ids = jnp.arange(levels, dtype=jnp.int32)
    distances = jnp.array([2**level_index for level_index in range(levels)], dtype=jnp.int32)
    reached = (level_ids[None, :] < reach_rows[:, None]) & (
        block_ids[:, None] - distances[None, :] >= 0
    )
    return jnp.concatenate([jnp.ones((per_shard, 1), dtype=bool), reached], axis=1)


def score_mask(valid_slots, block_rows):
    row_ids = jnp.arange(block_rows)
    causal = row_ids[None, :] <= row_ids[:, None]
    first_slot = jnp.arange(valid_slots.shape[1]) == 0
    inside = jnp.where(first_slot[:, None, None], causal[None], True)
    allowed = inside[None] & valid_slots[:, :, None, None]
    return jnp.transpose(allowed, (0, 2, 1, 3))[:, None]


def send_chunk(key_c, value_c, offsets, relay):
    pair = jnp.stack([key_c, value_c])
    received = {0: pair}
    for offset in offsets:
        if (relay or offset >= 8) and (offset.bit_length() - 1) % 2 == 1:
            half = offset // 2
            received[offset] = from_behind(received[half], "ctx", half)
        else:
            received[offset] = from_behind(pair, "ctx", offset)
    return [received[0]] + [received[offset] for offset in offsets]


def attend_chunk(query_c, received, grad_c, allowed, offsets, heads):
    scale_factor = 1.0 / math.sqrt(HEAD_DIM)
    rows = query_c.shape[0]
    head_shape = (rows, heads, HEAD_DIM)
    key_stack = jnp.stack([moved[0].reshape(head_shape) for moved in received])[None]
    value_stack = jnp.stack([moved[1].reshape(head_shape) for moved in received])[None]
    query_stack = query_c.reshape((1,) + head_shape)
    grad_stack = grad_c.reshape((1,) + head_shape)
    raw_scores = (
        jnp.einsum("bthd,bnuhd->bhtnu", query_stack, key_stack, preferred_element_type=jnp.float32)
        * scale_factor
    )
    scores = jnp.where(allowed, raw_scores, -1e30)
    row_peak = jnp.max(scores, axis=(3, 4), keepdims=True)
    summed = jnp.sum(jnp.exp(scores - row_peak), axis=(3, 4), keepdims=True)
    log_total = row_peak + jnp.log(summed)
    weights32 = jnp.exp(scores - log_total)
    weights = rounded(weights32)
    output = rounded(
        jnp.einsum("bhtnu,bnuhd->bthd", weights, value_stack, preferred_element_type=jnp.float32)
    )
    grad_probs = jnp.einsum(
        "bthd,bnuhd->bhtnu", grad_stack, value_stack, preferred_element_type=jnp.float32
    )
    delta_rows = jnp.sum(grad_stack.astype(jnp.float32) * output.astype(jnp.float32), axis=-1)
    delta_rows = jnp.transpose(delta_rows, (0, 2, 1))[:, :, :, None, None]
    grad_scores = rounded(weights32 * (grad_probs - delta_rows) * scale_factor)
    query_grad = jnp.einsum(
        "bhtnu,bnuhd->bthd", grad_scores, key_stack, preferred_element_type=jnp.float32
    )
    key_terms = jnp.einsum(
        "bhtnu,bthd->bnuhd", grad_scores, query_stack, preferred_element_type=jnp.float32
    )
    value_terms = jnp.einsum(
        "bhtnu,bthd->bnuhd", weights, grad_stack, preferred_element_type=jnp.float32
    )
    own = (rounded(key_terms[0, 0]), rounded(value_terms[0, 0]))
    outgoing = [
        jnp.stack([key_terms[0, slot_index], value_terms[0, slot_index]]).astype(jnp.bfloat16)
        for slot_index in range(1, len(offsets) + 1)
    ]
    return output, query_grad, own, outgoing


def gather_back(own, outgoing, offsets):
    key_accum = own[0].astype(jnp.float32)
    value_accum = own[1].astype(jnp.float32)
    for parts, offset in zip(outgoing, offsets):
        returned = from_behind(parts, "ctx", -offset)
        key_accum = key_accum + returned[0].astype(jnp.float32)
        value_accum = value_accum + returned[1].astype(jnp.float32)
    return key_accum, value_accum


def on_device(queries, key_vectors, values, grad_out, file_lengths, reach_table):
    local_rows = queries.shape[0]
    width_all = queries.shape[1]
    per_shard = local_rows // BLOCK
    ctx_size = lax.axis_size("ctx")
    levels = (per_shard * ctx_size - 1).bit_length()
    offsets = [2**level_index for level_index in range(levels)]
    shard_index = lax.axis_index("ctx")
    global_rows = shard_index * local_rows + jnp.arange(local_rows, dtype=jnp.int32)
    positions = file_positions(file_lengths, global_rows)
    query_rot = rounded(rotary(queries, positions, HEADS, HEAD_DIM, False))
    key_rot = rounded(rotary(key_vectors, positions, HEADS, HEAD_DIM, False))
    valid_slots = reach_mask(reach_table, shard_index * per_shard, per_shard, levels)
    allowed = score_mask(valid_slots, BLOCK)
    chunk_heads = HEADS // CHUNKS
    chunk_width = chunk_heads * HEAD_DIM
    columns = [slice(chunk * chunk_width, (chunk + 1) * chunk_width) for chunk in range(CHUNKS)]
    pieces = []
    pending = []
    for chunk, cols in enumerate(columns):
        key_c, value_c = key_rot[:, cols], values[:, cols]
        if pending:
            key_c, value_c, _ = lax.optimization_barrier((key_c, value_c, pieces[-1][0]))
        received = send_chunk(key_c, value_c, offsets, relay=not pending)
        output, query_grad, own, outgoing = attend_chunk(
            query_rot[:, cols], received, grad_out[:, cols], allowed, offsets, chunk_heads
        )
        pending.append(outgoing)
        key_accum_c, value_accum_c = gather_back(own, outgoing, offsets)
        rows = query_rot.shape[0]
        pieces.append(
            (
                output.reshape(rows, chunk_width),
                query_grad.reshape(rows, chunk_width),
                key_accum_c.reshape(rows, chunk_width),
                value_accum_c.reshape(rows, chunk_width),
            )
        )
    attended, query_grad, key_accum, value_accum = [
        jnp.concatenate(parts, axis=1) for parts in zip(*pieces)
    ]
    grad_queries = rotary(query_grad, positions, HEADS, HEAD_DIM, True).astype(jnp.bfloat16)
    grad_keys = rotary(key_accum, positions, HEADS, HEAD_DIM, True).astype(jnp.bfloat16)
    grad_values = value_accum.astype(jnp.bfloat16)
    return (attended, grad_queries, grad_keys, grad_values)


def solution(mesh):
    placed = (
        P(("groups", "ctx"), None),
        P(("groups", "ctx"), None),
        P(("groups", "ctx"), None),
        P(("groups", "ctx"), None),
        P("groups"),
        P(("groups", "ctx")),
    )
    return jax.shard_map(
        on_device,
        mesh=mesh,
        in_specs=placed,
        out_specs=(
            P(("groups", "ctx"), None),
            P(("groups", "ctx"), None),
            P(("groups", "ctx"), None),
            P(("groups", "ctx"), None),
        ),
        check_vma=False,
    )
```

```python
import math

import jax
import jax.numpy as jnp
from jax import lax
from jax.sharding import PartitionSpec as P

HEADS = 16
HEAD_DIM = 128
BLOCK = 128
CHUNKS = 2


def from_behind(value, axis, steps):
    count = lax.axis_size(axis)
    leading, last = (max(0, -steps), min(count, count - steps))
    return lax.ppermute(value, axis, [(source, source + steps) for source in range(leading, last)])


def rounded(matrix):
    return lax.optimization_barrier(matrix.astype(jnp.bfloat16))


def file_positions(file_lengths, global_rows):
    file_ends = jnp.cumsum(file_lengths)
    starts = file_ends - file_lengths
    owned_mask = starts[None, :] <= global_rows[:, None]
    latest = jnp.max(jnp.where(owned_mask, starts[None, :], 0), axis=1)
    return global_rows - latest


def rotary(matrix, positions, head_count, head_width, inverse):
    half_width = head_width // 2
    exponent = jnp.arange(half_width, dtype=jnp.float32) * (2.0 / head_width)
    frequency = jnp.exp(exponent * -math.log(10000.0))
    angles = positions.astype(jnp.float32)[:, None] * frequency[None, :]
    cosine = jnp.cos(angles)[:, None, :]
    sine_table = jnp.sin(angles)[:, None, :]
    shaped = matrix.astype(jnp.float32).reshape(matrix.shape[0], head_count, head_width)
    former = shaped[..., :half_width]
    latter = shaped[..., half_width:]
    if inverse:
        turned = jnp.concatenate(
            [former * cosine + latter * sine_table, latter * cosine - former * sine_table], axis=-1
        )
    else:
        turned = jnp.concatenate(
            [former * cosine - latter * sine_table, latter * cosine + former * sine_table], axis=-1
        )
    return turned.reshape(matrix.shape[0], head_count * head_width)


def reach_mask(reach_rows, first_block, per_shard, levels):
    block_ids = first_block + jnp.arange(per_shard, dtype=jnp.int32)
    level_ids = jnp.arange(levels, dtype=jnp.int32)
    distances = jnp.array([2**level_index for level_index in range(levels)], dtype=jnp.int32)
    reached = (level_ids[None, :] < reach_rows[:, None]) & (
        block_ids[:, None] - distances[None, :] >= 0
    )
    return jnp.concatenate([jnp.ones((per_shard, 1), dtype=bool), reached], axis=1)


def score_mask(valid_slots, block_rows):
    row_ids = jnp.arange(block_rows)
    causal = row_ids[None, :] <= row_ids[:, None]
    first_slot = jnp.arange(valid_slots.shape[1]) == 0
    inside = jnp.where(first_slot[:, None, None], causal[None], True)
    allowed = inside[None] & valid_slots[:, :, None, None]
    return jnp.transpose(allowed, (0, 2, 1, 3))[:, None]


def send_chunk(key_c, value_c, offsets, relay):
    pair = jnp.stack([key_c, value_c])
    received = {0: pair}
    for offset in offsets:
        if relay and (offset.bit_length() - 1) % 2 == 1:
            half = offset // 2
            received[offset] = from_behind(received[half], "ctx", half)
        else:
            received[offset] = from_behind(pair, "ctx", offset)
    return [received[0]] + [received[offset] for offset in offsets]


def attend_chunk(query_c, received, grad_c, allowed, offsets, heads):
    scale_factor = 1.0 / math.sqrt(HEAD_DIM)
    rows = query_c.shape[0]
    head_shape = (rows, heads, HEAD_DIM)
    key_stack = jnp.stack([moved[0].reshape(head_shape) for moved in received])[None]
    value_stack = jnp.stack([moved[1].reshape(head_shape) for moved in received])[None]
    query_stack = query_c.reshape((1,) + head_shape)
    grad_stack = grad_c.reshape((1,) + head_shape)
    raw_scores = (
        jnp.einsum("bthd,bnuhd->bhtnu", query_stack, key_stack, preferred_element_type=jnp.float32)
        * scale_factor
    )
    scores = jnp.where(allowed, raw_scores, -1e30)
    row_peak = jnp.max(scores, axis=(3, 4), keepdims=True)
    summed = jnp.sum(jnp.exp(scores - row_peak), axis=(3, 4), keepdims=True)
    log_total = row_peak + jnp.log(summed)
    weights32 = jnp.exp(scores - log_total)
    weights = rounded(weights32)
    output = rounded(
        jnp.einsum("bhtnu,bnuhd->bthd", weights, value_stack, preferred_element_type=jnp.float32)
    )
    grad_probs = jnp.einsum(
        "bthd,bnuhd->bhtnu", grad_stack, value_stack, preferred_element_type=jnp.float32
    )
    delta_rows = jnp.sum(grad_stack.astype(jnp.float32) * output.astype(jnp.float32), axis=-1)
    delta_rows = jnp.transpose(delta_rows, (0, 2, 1))[:, :, :, None, None]
    grad_scores = rounded(weights32 * (grad_probs - delta_rows) * scale_factor)
    query_grad = jnp.einsum(
        "bhtnu,bnuhd->bthd", grad_scores, key_stack, preferred_element_type=jnp.float32
    )
    key_terms = jnp.einsum(
        "bhtnu,bthd->bnuhd", grad_scores, query_stack, preferred_element_type=jnp.float32
    )
    value_terms = jnp.einsum(
        "bhtnu,bthd->bnuhd", weights, grad_stack, preferred_element_type=jnp.float32
    )
    own = (rounded(key_terms[0, 0]), rounded(value_terms[0, 0]))
    outgoing = [
        jnp.stack([key_terms[0, slot_index], value_terms[0, slot_index]]).astype(jnp.bfloat16)
        for slot_index in range(1, len(offsets) + 1)
    ]
    return output, query_grad, own, outgoing


def gather_back(own, outgoing, offsets):
    key_accum = own[0].astype(jnp.float32)
    value_accum = own[1].astype(jnp.float32)
    for parts, offset in list(zip(outgoing, offsets))[::-1]:
        returned = from_behind(parts, "ctx", -offset)
        key_accum = key_accum + returned[0].astype(jnp.float32)
        value_accum = value_accum + returned[1].astype(jnp.float32)
    return key_accum, value_accum


def on_device(queries, key_vectors, values, grad_out, file_lengths, reach_table):
    local_rows = queries.shape[0]
    width_all = queries.shape[1]
    per_shard = local_rows // BLOCK
    ctx_size = lax.axis_size("ctx")
    levels = (per_shard * ctx_size - 1).bit_length()
    offsets = [2**level_index for level_index in range(levels)]
    shard_index = lax.axis_index("ctx")
    global_rows = shard_index * local_rows + jnp.arange(local_rows, dtype=jnp.int32)
    positions = file_positions(file_lengths, global_rows)
    query_rot = rounded(rotary(queries, positions, HEADS, HEAD_DIM, False))
    key_rot = rounded(rotary(key_vectors, positions, HEADS, HEAD_DIM, False))
    valid_slots = reach_mask(reach_table, shard_index * per_shard, per_shard, levels)
    allowed = score_mask(valid_slots, BLOCK)
    chunk_heads = HEADS // CHUNKS
    chunk_width = chunk_heads * HEAD_DIM
    columns = [slice(chunk * chunk_width, (chunk + 1) * chunk_width) for chunk in range(CHUNKS)]
    pieces = []
    pending = []
    for chunk, cols in enumerate(columns):
        key_c, value_c = key_rot[:, cols], values[:, cols]
        if pending:
            key_c, value_c, _ = lax.optimization_barrier((key_c, value_c, pieces[-1][0]))
        received = send_chunk(key_c, value_c, offsets, relay=not pending)
        output, query_grad, own, outgoing = attend_chunk(
            query_rot[:, cols], received, grad_out[:, cols], allowed, offsets, chunk_heads
        )
        pending.append(outgoing)
        key_accum_c, value_accum_c = gather_back(own, outgoing, offsets)
        rows = query_rot.shape[0]
        pieces.append(
            (
                output.reshape(rows, chunk_width),
                query_grad.reshape(rows, chunk_width),
                key_accum_c.reshape(rows, chunk_width),
                value_accum_c.reshape(rows, chunk_width),
            )
        )
    attended, query_grad, key_accum, value_accum = [
        jnp.concatenate(parts, axis=1) for parts in zip(*pieces)
    ]
    grad_queries = rotary(query_grad, positions, HEADS, HEAD_DIM, True).astype(jnp.bfloat16)
    grad_keys = rotary(key_accum, positions, HEADS, HEAD_DIM, True).astype(jnp.bfloat16)
    grad_values = value_accum.astype(jnp.bfloat16)
    return (attended, grad_queries, grad_keys, grad_values)


def solution(mesh):
    placed = (
        P(("groups", "ctx"), None),
        P(("groups", "ctx"), None),
        P(("groups", "ctx"), None),
        P(("groups", "ctx"), None),
        P("groups"),
        P(("groups", "ctx")),
    )
    return jax.shard_map(
        on_device,
        mesh=mesh,
        in_specs=placed,
        out_specs=(
            P(("groups", "ctx"), None),
            P(("groups", "ctx"), None),
            P(("groups", "ctx"), None),
            P(("groups", "ctx"), None),
        ),
        check_vma=False,
    )
```

```python
import math

import jax
import jax.numpy as jnp
from jax import lax
from jax.sharding import PartitionSpec as P

HEADS = 16
HEAD_DIM = 128
BLOCK = 128
CHUNKS = 2


def from_behind(value, axis, steps):
    count = lax.axis_size(axis)
    leading, last = (max(0, -steps), min(count, count - steps))
    return lax.ppermute(value, axis, [(source, source + steps) for source in range(leading, last)])


def rounded(matrix):
    return lax.optimization_barrier(matrix.astype(jnp.bfloat16))


def file_positions(file_lengths, global_rows):
    file_ends = jnp.cumsum(file_lengths)
    starts = file_ends - file_lengths
    owned_mask = starts[None, :] <= global_rows[:, None]
    latest = jnp.max(jnp.where(owned_mask, starts[None, :], 0), axis=1)
    return global_rows - latest


def rotary(matrix, positions, head_count, head_width, inverse):
    half_width = head_width // 2
    exponent = jnp.arange(half_width, dtype=jnp.float32) * (2.0 / head_width)
    frequency = jnp.exp(exponent * -math.log(10000.0))
    angles = positions.astype(jnp.float32)[:, None] * frequency[None, :]
    cosine = jnp.cos(angles)[:, None, :]
    sine_table = jnp.sin(angles)[:, None, :]
    shaped = matrix.astype(jnp.float32).reshape(matrix.shape[0], head_count, head_width)
    former = shaped[..., :half_width]
    latter = shaped[..., half_width:]
    if inverse:
        turned = jnp.concatenate(
            [former * cosine + latter * sine_table, latter * cosine - former * sine_table], axis=-1
        )
    else:
        turned = jnp.concatenate(
            [former * cosine - latter * sine_table, latter * cosine + former * sine_table], axis=-1
        )
    return turned.reshape(matrix.shape[0], head_count * head_width)


def reach_mask(reach_rows, first_block, per_shard, levels):
    block_ids = first_block + jnp.arange(per_shard, dtype=jnp.int32)
    level_ids = jnp.arange(levels, dtype=jnp.int32)
    distances = jnp.array([2**level_index for level_index in range(levels)], dtype=jnp.int32)
    reached = (level_ids[None, :] < reach_rows[:, None]) & (
        block_ids[:, None] - distances[None, :] >= 0
    )
    return jnp.concatenate([jnp.ones((per_shard, 1), dtype=bool), reached], axis=1)


def score_mask(valid_slots, block_rows):
    row_ids = jnp.arange(block_rows)
    causal = row_ids[None, :] <= row_ids[:, None]
    first_slot = jnp.arange(valid_slots.shape[1]) == 0
    inside = jnp.where(first_slot[:, None, None], causal[None], True)
    allowed = inside[None] & valid_slots[:, :, None, None]
    return jnp.transpose(allowed, (0, 2, 1, 3))[:, None]


def send_chunk(key_c, value_c, offsets, relay):
    pair = jnp.stack([key_c, value_c])
    received = {0: pair}
    for offset in offsets:
        if relay and offset >= 2:
            half = offset // 2
            received[offset] = from_behind(received[half], "ctx", half)
        else:
            received[offset] = from_behind(pair, "ctx", offset)
    return [received[0]] + [received[offset] for offset in offsets]


def attend_chunk(query_c, received, grad_c, allowed, offsets, heads):
    scale_factor = 1.0 / math.sqrt(HEAD_DIM)
    rows = query_c.shape[0]
    head_shape = (rows, heads, HEAD_DIM)
    key_stack = jnp.stack([moved[0].reshape(head_shape) for moved in received])[None]
    value_stack = jnp.stack([moved[1].reshape(head_shape) for moved in received])[None]
    query_stack = query_c.reshape((1,) + head_shape)
    grad_stack = grad_c.reshape((1,) + head_shape)
    raw_scores = (
        jnp.einsum("bthd,bnuhd->bhtnu", query_stack, key_stack, preferred_element_type=jnp.float32)
        * scale_factor
    )
    scores = jnp.where(allowed, raw_scores, -1e30)
    row_peak = jnp.max(scores, axis=(3, 4), keepdims=True)
    summed = jnp.sum(jnp.exp(scores - row_peak), axis=(3, 4), keepdims=True)
    log_total = row_peak + jnp.log(summed)
    weights32 = jnp.exp(scores - log_total)
    weights = rounded(weights32)
    output = rounded(
        jnp.einsum("bhtnu,bnuhd->bthd", weights, value_stack, preferred_element_type=jnp.float32)
    )
    grad_probs = jnp.einsum(
        "bthd,bnuhd->bhtnu", grad_stack, value_stack, preferred_element_type=jnp.float32
    )
    delta_rows = jnp.sum(grad_stack.astype(jnp.float32) * output.astype(jnp.float32), axis=-1)
    delta_rows = jnp.transpose(delta_rows, (0, 2, 1))[:, :, :, None, None]
    grad_scores = rounded(weights32 * (grad_probs - delta_rows) * scale_factor)
    query_grad = jnp.einsum(
        "bhtnu,bnuhd->bthd", grad_scores, key_stack, preferred_element_type=jnp.float32
    )
    key_terms = jnp.einsum(
        "bhtnu,bthd->bnuhd", grad_scores, query_stack, preferred_element_type=jnp.float32
    )
    value_terms = jnp.einsum(
        "bhtnu,bthd->bnuhd", weights, grad_stack, preferred_element_type=jnp.float32
    )
    own = (rounded(key_terms[0, 0]), rounded(value_terms[0, 0]))
    outgoing = [
        jnp.stack([key_terms[0, slot_index], value_terms[0, slot_index]]).astype(jnp.bfloat16)
        for slot_index in range(1, len(offsets) + 1)
    ]
    return output, query_grad, own, outgoing


def gather_back(own, outgoing, offsets):
    key_accum = own[0].astype(jnp.float32)
    value_accum = own[1].astype(jnp.float32)
    for parts, offset in zip(outgoing, offsets):
        returned = from_behind(parts, "ctx", -offset)
        key_accum = key_accum + returned[0].astype(jnp.float32)
        value_accum = value_accum + returned[1].astype(jnp.float32)
    return key_accum, value_accum


def on_device(queries, key_vectors, values, grad_out, file_lengths, reach_table):
    local_rows = queries.shape[0]
    width_all = queries.shape[1]
    per_shard = local_rows // BLOCK
    ctx_size = lax.axis_size("ctx")
    levels = (per_shard * ctx_size - 1).bit_length()
    offsets = [2**level_index for level_index in range(levels)]
    shard_index = lax.axis_index("ctx")
    global_rows = shard_index * local_rows + jnp.arange(local_rows, dtype=jnp.int32)
    positions = file_positions(file_lengths, global_rows)
    query_rot = rounded(rotary(queries, positions, HEADS, HEAD_DIM, False))
    key_rot = rounded(rotary(key_vectors, positions, HEADS, HEAD_DIM, False))
    valid_slots = reach_mask(reach_table, shard_index * per_shard, per_shard, levels)
    allowed = score_mask(valid_slots, BLOCK)
    chunk_heads = HEADS // CHUNKS
    chunk_width = chunk_heads * HEAD_DIM
    columns = [slice(chunk * chunk_width, (chunk + 1) * chunk_width) for chunk in range(CHUNKS)]
    pieces = []
    pending = []
    for chunk, cols in enumerate(columns):
        key_c, value_c = key_rot[:, cols], values[:, cols]
        if pending:
            key_c, value_c, _ = lax.optimization_barrier((key_c, value_c, pieces[-1][0]))
        received = send_chunk(key_c, value_c, offsets, relay=not pending)
        output, query_grad, own, outgoing = attend_chunk(
            query_rot[:, cols], received, grad_out[:, cols], allowed, offsets, chunk_heads
        )
        pending.append(outgoing)
        key_accum_c, value_accum_c = gather_back(own, outgoing, offsets)
        rows = query_rot.shape[0]
        pieces.append(
            (
                output.reshape(rows, chunk_width),
                query_grad.reshape(rows, chunk_width),
                key_accum_c.reshape(rows, chunk_width),
                value_accum_c.reshape(rows, chunk_width),
            )
        )
    attended, query_grad, key_accum, value_accum = [
        jnp.concatenate(parts, axis=1) for parts in zip(*pieces)
    ]
    grad_queries = rotary(query_grad, positions, HEADS, HEAD_DIM, True).astype(jnp.bfloat16)
    grad_keys = rotary(key_accum, positions, HEADS, HEAD_DIM, True).astype(jnp.bfloat16)
    grad_values = value_accum.astype(jnp.bfloat16)
    return (attended, grad_queries, grad_keys, grad_values)


def solution(mesh):
    placed = (
        P(("groups", "ctx"), None),
        P(("groups", "ctx"), None),
        P(("groups", "ctx"), None),
        P(("groups", "ctx"), None),
        P("groups"),
        P(("groups", "ctx")),
    )
    return jax.shard_map(
        on_device,
        mesh=mesh,
        in_specs=placed,
        out_specs=(
            P(("groups", "ctx"), None),
            P(("groups", "ctx"), None),
            P(("groups", "ctx"), None),
            P(("groups", "ctx"), None),
        ),
        check_vma=False,
    )
```

```python
import math

import jax
import jax.numpy as jnp
from jax import lax
from jax.sharding import PartitionSpec as P

HEADS = 16
HEAD_DIM = 128
BLOCK = 128
CHUNKS = 2


def from_behind(value, axis, steps):
    count = lax.axis_size(axis)
    leading, last = (max(0, -steps), min(count, count - steps))
    return lax.ppermute(value, axis, [(source, source + steps) for source in range(leading, last)])


def rounded(matrix):
    return lax.optimization_barrier(matrix.astype(jnp.bfloat16))


def file_positions(file_lengths, global_rows):
    file_ends = jnp.cumsum(file_lengths)
    starts = file_ends - file_lengths
    owned_mask = starts[None, :] <= global_rows[:, None]
    latest = jnp.max(jnp.where(owned_mask, starts[None, :], 0), axis=1)
    return global_rows - latest


def rotary(matrix, positions, head_count, head_width, inverse):
    half_width = head_width // 2
    exponent = jnp.arange(half_width, dtype=jnp.float32) * (2.0 / head_width)
    frequency = jnp.exp(exponent * -math.log(10000.0))
    angles = positions.astype(jnp.float32)[:, None] * frequency[None, :]
    cosine = jnp.cos(angles)[:, None, :]
    sine_table = jnp.sin(angles)[:, None, :]
    shaped = matrix.astype(jnp.float32).reshape(matrix.shape[0], head_count, head_width)
    former = shaped[..., :half_width]
    latter = shaped[..., half_width:]
    if inverse:
        turned = jnp.concatenate(
            [former * cosine + latter * sine_table, latter * cosine - former * sine_table], axis=-1
        )
    else:
        turned = jnp.concatenate(
            [former * cosine - latter * sine_table, latter * cosine + former * sine_table], axis=-1
        )
    return turned.reshape(matrix.shape[0], head_count * head_width)


def reach_mask(reach_rows, first_block, per_shard, levels):
    block_ids = first_block + jnp.arange(per_shard, dtype=jnp.int32)
    level_ids = jnp.arange(levels, dtype=jnp.int32)
    distances = jnp.array([2**level_index for level_index in range(levels)], dtype=jnp.int32)
    reached = (level_ids[None, :] < reach_rows[:, None]) & (
        block_ids[:, None] - distances[None, :] >= 0
    )
    return jnp.concatenate([jnp.ones((per_shard, 1), dtype=bool), reached], axis=1)


def score_mask(valid_slots, block_rows):
    row_ids = jnp.arange(block_rows)
    causal = row_ids[None, :] <= row_ids[:, None]
    first_slot = jnp.arange(valid_slots.shape[1]) == 0
    inside = jnp.where(first_slot[:, None, None], causal[None], True)
    allowed = inside[None] & valid_slots[:, :, None, None]
    return jnp.transpose(allowed, (0, 2, 1, 3))[:, None]


def send_chunk(pair, offsets, relay):
    received = {0: pair}
    for offset in offsets:
        if relay and (offset.bit_length() - 1) % 2 == 1:
            half = offset // 2
            received[offset] = from_behind(received[half], "ctx", half)
        else:
            received[offset] = from_behind(pair, "ctx", offset)
    return [received[0]] + [received[offset] for offset in offsets]


def attend_chunk(query_c, received, grad_c, allowed, offsets, heads):
    scale_factor = 1.0 / math.sqrt(HEAD_DIM)
    rows = query_c.shape[0]
    head_shape = (rows, heads, HEAD_DIM)
    key_stack = jnp.stack([moved[0].reshape(head_shape) for moved in received])[None]
    value_stack = jnp.stack([moved[1].reshape(head_shape) for moved in received])[None]
    query_stack = query_c.reshape((1,) + head_shape)
    grad_stack = grad_c.reshape((1,) + head_shape)
    raw_scores = (
        jnp.einsum("bthd,bnuhd->bhtnu", query_stack, key_stack, preferred_element_type=jnp.float32)
        * scale_factor
    )
    scores = jnp.where(allowed, raw_scores, -1e30)
    row_peak = jnp.max(scores, axis=(3, 4), keepdims=True)
    summed = jnp.sum(jnp.exp(scores - row_peak), axis=(3, 4), keepdims=True)
    log_total = row_peak + jnp.log(summed)
    weights32 = jnp.exp(scores - log_total)
    weights = rounded(weights32)
    output = rounded(
        jnp.einsum("bhtnu,bnuhd->bthd", weights, value_stack, preferred_element_type=jnp.float32)
    )
    grad_probs = jnp.einsum(
        "bthd,bnuhd->bhtnu", grad_stack, value_stack, preferred_element_type=jnp.float32
    )
    delta_rows = jnp.sum(grad_stack.astype(jnp.float32) * output.astype(jnp.float32), axis=-1)
    delta_rows = jnp.transpose(delta_rows, (0, 2, 1))[:, :, :, None, None]
    grad_scores = rounded(weights32 * (grad_probs - delta_rows) * scale_factor)
    query_grad = jnp.einsum(
        "bhtnu,bnuhd->bthd", grad_scores, key_stack, preferred_element_type=jnp.float32
    )
    key_terms = jnp.einsum(
        "bhtnu,bthd->bnuhd", grad_scores, query_stack, preferred_element_type=jnp.float32
    )
    value_terms = jnp.einsum(
        "bhtnu,bthd->bnuhd", weights, grad_stack, preferred_element_type=jnp.float32
    )
    own = (rounded(key_terms[0, 0]), rounded(value_terms[0, 0]))
    outgoing = [
        jnp.stack([key_terms[0, slot_index], value_terms[0, slot_index]]).astype(jnp.bfloat16)
        for slot_index in range(1, len(offsets) + 1)
    ]
    return output, query_grad, own, outgoing


def gather_back(own, outgoing, offsets):
    key_accum = own[0].astype(jnp.float32)
    value_accum = own[1].astype(jnp.float32)
    for parts, offset in zip(outgoing, offsets):
        returned = from_behind(parts, "ctx", -offset)
        key_accum = key_accum + returned[0].astype(jnp.float32)
        value_accum = value_accum + returned[1].astype(jnp.float32)
    return key_accum, value_accum


def on_device(queries, key_vectors, values, grad_out, file_lengths, reach_table):
    local_rows = queries.shape[0]
    width_all = queries.shape[1]
    per_shard = local_rows // BLOCK
    ctx_size = lax.axis_size("ctx")
    levels = (per_shard * ctx_size - 1).bit_length()
    offsets = [2**level_index for level_index in range(levels)]
    shard_index = lax.axis_index("ctx")
    global_rows = shard_index * local_rows + jnp.arange(local_rows, dtype=jnp.int32)
    positions = file_positions(file_lengths, global_rows)
    query_rot = rounded(rotary(queries, positions, HEADS, HEAD_DIM, False))
    key_rot = rounded(rotary(key_vectors, positions, HEADS, HEAD_DIM, False))
    valid_slots = reach_mask(reach_table, shard_index * per_shard, per_shard, levels)
    allowed = score_mask(valid_slots, BLOCK)
    chunk_heads = HEADS // CHUNKS
    chunk_width = chunk_heads * HEAD_DIM
    columns = [slice(chunk * chunk_width, (chunk + 1) * chunk_width) for chunk in range(CHUNKS)]
    pieces = []
    pending = []
    for chunk, cols in enumerate(columns):
        pair = jnp.stack([key_rot[:, cols], values[:, cols]])
        if pending:
            pair, _ = lax.optimization_barrier((pair, pieces[-1][0]))
        received = send_chunk(pair, offsets, relay=not pending)
        output, query_grad, own, outgoing = attend_chunk(
            query_rot[:, cols], received, grad_out[:, cols], allowed, offsets, chunk_heads
        )
        pending.append(outgoing)
        key_accum_c, value_accum_c = gather_back(own, outgoing, offsets)
        rows = query_rot.shape[0]
        pieces.append(
            (
                output.reshape(rows, chunk_width),
                query_grad.reshape(rows, chunk_width),
                key_accum_c.reshape(rows, chunk_width),
                value_accum_c.reshape(rows, chunk_width),
            )
        )
    attended, query_grad, key_accum, value_accum = [
        jnp.concatenate(parts, axis=1) for parts in zip(*pieces)
    ]
    grad_queries = rotary(query_grad, positions, HEADS, HEAD_DIM, True).astype(jnp.bfloat16)
    grad_keys = rotary(key_accum, positions, HEADS, HEAD_DIM, True).astype(jnp.bfloat16)
    grad_values = value_accum.astype(jnp.bfloat16)
    return (attended, grad_queries, grad_keys, grad_values)


def solution(mesh):
    placed = (
        P(("groups", "ctx"), None),
        P(("groups", "ctx"), None),
        P(("groups", "ctx"), None),
        P(("groups", "ctx"), None),
        P("groups"),
        P(("groups", "ctx")),
    )
    return jax.shard_map(
        on_device,
        mesh=mesh,
        in_specs=placed,
        out_specs=(
            P(("groups", "ctx"), None),
            P(("groups", "ctx"), None),
            P(("groups", "ctx"), None),
            P(("groups", "ctx"), None),
        ),
        check_vma=False,
    )
```
